256 devices in a mesh: zslab: 8 (over y, x_lo), blk: 32 (over z, x_hi, core).
Axes of the slice: x: 4 (x_hi: 2, x_lo: 2; x = x_hi * 2 + x_lo), y: 4, z: 8, core: 2. Of those that a mesh axis runs over, the one named last changes fastest.
Arguments:
- field: bfloat16 [256, 16, 32, 128], P('blk', None, 'zslab'), may hold values from -6 to 6
- fracture_mask: int32 [256, 16, 32], P('blk', None, 'zslab'), may hold values 0 or 1
- dilation: int32 [2, 3], replicated, may hold values from 1 to 2, as said below
- conv_weight: bfloat16 [2, 3456, 128], replicated, may hold values from -0.109375 to 0.109375
- embed_weight: bfloat16 [8, 2048, 1024], P('zslab', 'blk'), may hold values from -0.046875 to 0.046875
- qkv_weight: bfloat16 [3, 1024, 1024], P(None, 'blk', 'zslab'), may hold values from -3 to 3
- out_grad: bfloat16 [1024, 1024], P('blk', 'zslab'), may hold values from -6 to 6
Outputs:
- field_grad: bfloat16 [256, 16, 32, 128], P('blk', None, 'zslab')
The draws below stay inside these ranges and needn't reach their ends.
Inputs may be any that keep to these rules, and one draw needn't show every extreme that they name: The dilation of each of the 2 layers along x, y and z; some entry is 1 and some entry is 2.
All inputs are finite; a program needn't handle non-finite values. No bound on the sum of `fracture_mask` on one device may be relied on, other than what follows from the above.
Results may differ from the reference program's by a relative error of at most 0.04.
Values may be sent and summed in bfloat16 or wider, within the bound.
No kernel may reach another device: no remote copies, remote signals or barrier semaphores. Data moves between devices by JAX's collectives and lax.ppermute only.
A program may use at most 64 MiB of HBM per device.

```python
import jax
import jax.numpy as jnp
from jax import lax

C = 128
HEADS = 8
HD = 128
D = 1024
PX = 8
PY = 8
PZ = 2
FEAT = 16384
NY = 16
LAYERS = 2
DMAX = 2
NX = 256
NZ = 32
TOKENS = 1024


def draw_dilation(key, part):
    entries = jax.random.randint(jax.random.fold_in(key, 11), (LAYERS * 3,), 1, 3).astype(jnp.int32)
    order = jax.random.permutation(jax.random.fold_in(key, 13), LAYERS * 3)
    positions = jnp.arange(LAYERS * 3)
    entries = jnp.where(positions == order[0], 2, entries)
    entries = jnp.where(positions == order[1], 1, entries)
    return entries.reshape(LAYERS, 3).astype(jnp.int32)


def draw_qkv_weight(key, part):
    entries = jax.random.normal(key, (3, D, D), jnp.float32) * D ** (-0.5)
    return jnp.clip(entries, -3.0, 3.0).astype(jnp.bfloat16)


def place_ends(values, key, least, largest):
    longest = values.shape.index(max(values.shape))
    spots = []
    for shift in (0, 1):
        where = [jax.random.randint(jax.random.fold_in(key, axis), (), 0, length) for axis, length in enumerate(values.shape)]
        where[longest] = (where[longest] + shift) % values.shape[longest]
        spots.append(tuple(where))
    return values.at[spots[0]].set(least).at[spots[1]].set(largest)


def steps_of(stream_key, extent, shards, smallest, top_value):
    def one(position, shards_of):
        steps = jax.random.uniform(jax.random.fold_in(jax.random.fold_in(stream_key, 6), position), (shards_of,), jnp.float32, smallest / len(shards), top_value / len(shards))
        return jnp.repeat(jnp.exp(steps), extent[position] // shards_of).reshape((-1,) + (1,) * (len(extent) - position - 1))

    level = one(*shards[0])
    for cut in shards[1:]:
        level = level * one(*cut)
    return level


def centred(rng, shape, scale, bound, cuts=(), kind=jnp.bfloat16):
    values = scale * jax.random.normal(rng, shape, jnp.float32)
    if cuts:
        values = values * steps_of(rng, shape, cuts, -0.22, 0.18)
    return jnp.clip(values, -bound, bound).astype(kind)


def setup_inputs(seed: int = 0) -> dict:
    key_of = jax.random.split(jax.random.key(seed), 8)
    field = centred(key_of[0], (NX, NY, NZ, C), 1.0, 6.0, ((0, 32), (2, 8)))
    fracture_mask = place_ends((jax.random.randint(key_of[1], (NX, NY, NZ), 0, 3) < 1).astype(jnp.int32), jax.random.fold_in(key_of[1], 1), 0, 1)
    dilation = draw_dilation(jax.random.fold_in(key_of[7], 71), 0)
    conv_weight = centred(key_of[3], (LAYERS, 27 * C, C), (27 * C) ** -0.5, 0.109375)
    embed_weight = centred(key_of[4], (PX, PY * PZ * C, D), FEAT ** -0.5, 0.046875, ((0, 8), (1, 32)))
    qkv_weight = draw_qkv_weight(jax.random.fold_in(key_of[7], 71), 0)
    out_grad = centred(key_of[6], (TOKENS, D), 1.0, 6.0, ((0, 32), (1, 8)))
    return dict(field=field, fracture_mask=fracture_mask, dilation=dilation, conv_weight=conv_weight, embed_weight=embed_weight, qkv_weight=qkv_weight, out_grad=out_grad)


def apply_offsets(padded, weight, dilate, direction, dims_out):
    x_cells, y_cells, z_cells, channels = dims_out
    summed = jnp.zeros((x_cells * y_cells * z_cells, weight.shape[-1]), jnp.float32)
    for offset_x in (-1, 0, 1):
        for offset_y in (-1, 0, 1):
            for offset_z in (-1, 0, 1):
                tap_index = 9 * (offset_x + 1) + 3 * (offset_y + 1) + offset_z + 1
                anchor = (
                    (DMAX + direction * offset_x * dilate[0]).astype(jnp.int32),
                    (DMAX + direction * offset_y * dilate[1]).astype(jnp.int32),
                    (DMAX + direction * offset_z * dilate[2]).astype(jnp.int32),
                    jnp.int32(0),
                )
                window = lax.dynamic_slice(padded, anchor, (x_cells, y_cells, z_cells, channels))
                summed = summed + jnp.dot(
                    window.reshape(-1, channels),
                    weight[tap_index * channels:(tap_index + 1) * channels],
                    preferred_element_type=jnp.float32,
                )
    return summed.reshape(x_cells, y_cells, z_cells, -1)


def head_grads(items):
    query_h, key_h, value_h, grad_h = items
    inv_root = HD ** -0.5
    scores = jnp.dot(query_h, key_h.T, preferred_element_type=jnp.float32) * inv_root
    top_score = jnp.max(scores, axis=1, keepdims=True)
    expo = jnp.exp(scores - top_score)
    probs = expo / jnp.sum(expo, axis=1, keepdims=True)
    probs_b = probs.astype(jnp.bfloat16)
    attended = jnp.dot(probs_b, value_h, preferred_element_type=jnp.float32)
    row_delta = jnp.sum(grad_h.astype(jnp.float32) * attended, axis=1, keepdims=True)
    score_grad = jnp.dot(grad_h, value_h.T, preferred_element_type=jnp.float32)
    dscore = (probs * (score_grad - row_delta) * inv_root).astype(jnp.bfloat16)
    grad_query = jnp.dot(dscore, key_h, preferred_element_type=jnp.float32).astype(jnp.bfloat16)
    grad_key = jnp.dot(dscore.T, query_h, preferred_element_type=jnp.float32).astype(jnp.bfloat16)
    grad_value = jnp.dot(probs_b.T, grad_h, preferred_element_type=jnp.float32).astype(jnp.bfloat16)
    return grad_query, grad_key, grad_value


def by_heads(matrix):
    return matrix.reshape(TOKENS, HEADS, HD).transpose(1, 0, 2)


def from_heads(stacked):
    return stacked.transpose(1, 0, 2).reshape(TOKENS, D)


def reference(field, fracture_mask, dilation, conv_weight, embed_weight, qkv_weight, out_grad):
    margins = ((DMAX, DMAX), (DMAX, DMAX), (DMAX, DMAX), (0, 0))
    gate_mask = fracture_mask.astype(jnp.float32)[..., None]
    hidden = field
    conv_outs = []
    for layer_num in range(LAYERS):
        conv_out = apply_offsets(jnp.pad(hidden, margins), conv_weight[layer_num], dilation[layer_num], 1, hidden.shape)
        conv_outs.append(conv_out)
        hidden = (hidden.astype(jnp.float32) + gate_mask * (conv_out * jax.nn.sigmoid(conv_out))).astype(jnp.bfloat16)
    patches = hidden.reshape(NX // PX, PX, NY // PY, PY, NZ // PZ, PZ, C).transpose(0, 2, 4, 1, 3, 5, 6).reshape(TOKENS, FEAT)
    embed_flat = embed_weight.reshape(FEAT, D)
    tokens = jnp.dot(patches, embed_flat, preferred_element_type=jnp.float32).astype(jnp.bfloat16)
    query = jnp.dot(tokens, qkv_weight[0], preferred_element_type=jnp.float32).astype(jnp.bfloat16)
    key = jnp.dot(tokens, qkv_weight[1], preferred_element_type=jnp.float32).astype(jnp.bfloat16)
    value = jnp.dot(tokens, qkv_weight[2], preferred_element_type=jnp.float32).astype(jnp.bfloat16)
    grad_query, grad_key, grad_value = lax.map(head_grads, (by_heads(query), by_heads(key), by_heads(value), by_heads(out_grad)))
    grad_tokens = (
        jnp.dot(from_heads(grad_query), qkv_weight[0].T, preferred_element_type=jnp.float32)
        + jnp.dot(from_heads(grad_key), qkv_weight[1].T, preferred_element_type=jnp.float32)
        + jnp.dot(from_heads(grad_value), qkv_weight[2].T, preferred_element_type=jnp.float32)
    ).astype(jnp.bfloat16)
    patch_grad = jnp.dot(grad_tokens, embed_flat.T, preferred_element_type=jnp.float32).astype(jnp.bfloat16)
    grid_grad = patch_grad.reshape(NX // PX, NY // PY, NZ // PZ, PX, PY, PZ, C).transpose(0, 3, 1, 4, 2, 5, 6).reshape(NX, NY, NZ, C)
    for layer_num in reversed(range(LAYERS)):
        conv_out = conv_outs[layer_num]
        sigma = jax.nn.sigmoid(conv_out)
        slope_grad = (gate_mask * sigma * (1.0 + conv_out * (1.0 - sigma)) * grid_grad.astype(jnp.float32)).astype(jnp.bfloat16)
        flipped = conv_weight[layer_num].reshape(27, C, C).transpose(0, 2, 1).reshape(27 * C, C)
        backward = apply_offsets(jnp.pad(slope_grad, margins), flipped, dilation[layer_num], -1, slope_grad.shape)
        grid_grad = (grid_grad.astype(jnp.float32) + backward).astype(jnp.bfloat16)
    return grid_grad
```

```python
import jax
import jax.numpy as jnp
from jax import lax
from jax.sharding import PartitionSpec as P

HD = 128
PY = 8
PZ = 2
LAYERS = 2
DMAX = 2


def padded_2(cells, sides, width):
    for axis, dim in sides:
        count = lax.axis_size(axis)
        ends = count - 1
        head = lax.slice_in_dim(cells, 0, width, axis=dim)
        tail = lax.slice_in_dim(cells, cells.shape[dim] - width, cells.shape[dim], axis=dim)
        cells = jnp.concatenate(
            [
                lax.ppermute(tail, axis, [(i, (i + 1) % count) for i in range(ends)]),
                cells,
                lax.ppermute(head, axis, [((i + 1) % count, i) for i in range(ends)]),
            ],
            axis=dim,
        )
    return cells


def copy_for_each(shard, axis):
    peers = lax.axis_size(axis)
    return lax.all_to_all(
        jnp.broadcast_to(shard[None], (peers, *shard.shape)), axis, 0, 0, tiled=True
    )


def taken_together(shard, axis):
    return copy_for_each(shard, axis).astype(jnp.float32).sum(axis=0)


def joined_along(pieces, dim):
    shape = list(pieces.shape[1:])
    shape[dim] *= pieces.shape[0]
    return jnp.moveaxis(pieces, 0, dim).reshape(shape)


def gather_together(arrays, axis, dims):
    line = jnp.concatenate([a.reshape(-1) for a in arrays])
    lines, at, finished = (lax.all_gather(line, axis), 0, [])
    for a, dim in zip(arrays, dims):
        pieces = lines[:, at : at + a.size].reshape(-1, *a.shape)
        finished.append(joined_along(pieces, dim))
        at += a.size
    return tuple(finished)


def side_by_side(arrays, axis, dim, along):
    ends, at = ([], 0)
    for a in arrays[:-1]:
        at += a.shape[along]
        ends.append(at)
    both = jnp.concatenate(arrays, axis=along)
    return tuple(jnp.split(lax.all_gather(both, axis, axis=dim, tiled=True), ends, axis=along))


def cut_along(shard, dim, peers):
    before, after = (shard.shape[:dim], shard.shape[dim + 1 :])
    return jnp.moveaxis(shard.reshape(*before, peers, -1, *after), dim, 0)


def sum_at_owner(shard, axis, dim):
    peers = lax.axis_size(axis)
    pieces = lax.all_to_all(cut_along(shard, dim, peers), axis, 0, 0, tiled=True)
    return jnp.sum(pieces.astype(jnp.float32), axis=0)


def with_rim(volume):
    padded = padded_2(volume, (("zslab", 2), ("blk", 0)), DMAX)
    return jnp.pad(padded, ((0, 0), (DMAX, DMAX), (0, 0), (0, 0)))


def apply_offsets(padded, weight, dilate, direction, dims_out):
    x_cells, y_cells, z_cells, channels = dims_out
    summed = jnp.zeros((x_cells * y_cells * z_cells, weight.shape[-1]), jnp.float32)
    for offset_x in (-1, 0, 1):
        pieces = []
        for offset_y in (-1, 0, 1):
            for offset_z in (-1, 0, 1):
                anchor = (
                    DMAX + direction * offset_x * dilate[0],
                    DMAX + direction * offset_y * dilate[1],
                    DMAX + direction * offset_z * dilate[2],
                    jnp.int32(0),
                )
                pieces.append(
                    lax.dynamic_slice(padded, anchor, (x_cells, y_cells, z_cells, channels))
                )
        stacked = jnp.concatenate(pieces, axis=3).reshape(x_cells * y_cells * z_cells, 9 * channels)
        group_rows = weight[(offset_x + 1) * 9 * channels : (offset_x + 2) * 9 * channels]
        summed = summed + jnp.dot(stacked, group_rows, preferred_element_type=jnp.float32)
    return summed.reshape(x_cells, y_cells, z_cells, -1)


def slab_total(term):
    return taken_together(term.astype(jnp.bfloat16), "zslab").astype(jnp.float32)


def slab_sum(term):
    total = lax.psum(term, "zslab")
    return lax.reduce_precision(total, exponent_bits=8, mantissa_bits=7).astype(jnp.bfloat16)


def local(field, fracture_mask, dilation, conv_weight, embed_weight, qkv_weight, out_grad):
    x_cells, y_cells, z_cells, channels = field.shape
    gate_mask = fracture_mask.astype(jnp.float32)[..., None]
    hidden = field
    conv_outs = []
    for layer_num in range(LAYERS):
        conv_out = apply_offsets(
            with_rim(hidden), conv_weight[layer_num], dilation[layer_num], 1, field.shape
        )
        conv_outs.append(conv_out)
        hidden = (
            hidden.astype(jnp.float32) + gate_mask * (conv_out * jax.nn.sigmoid(conv_out))
        ).astype(jnp.bfloat16)
    slab_view = lax.all_to_all(hidden, "zslab", split_axis=0, concat_axis=2, tiled=True)
    x_local, z_total = (slab_view.shape[0], slab_view.shape[2])
    y_blocks, z_blocks = (y_cells // PY, z_total // PZ)
    patches = slab_view.reshape(x_local, y_blocks, PY, z_blocks, PZ, channels).transpose(
        1, 3, 0, 2, 4, 5
    )
    patches = patches.reshape(y_blocks * z_blocks, x_local, PY * PZ * channels)
    embed_rows = lax.all_gather(embed_weight, "blk", axis=1, tiled=True)
    qkv_rows = lax.all_gather(qkv_weight, "blk", axis=1, tiled=True)
    partial_value = jnp.einsum(
        "tpf,pfd->td", patches, embed_rows, preferred_element_type=jnp.float32
    )
    tokens = slab_sum(partial_value)
    projected = jnp.einsum(
        "td,sde->ste", tokens, qkv_rows, preferred_element_type=jnp.float32
    ).astype(jnp.bfloat16)
    key_rows, value_rows = gather_together((projected[1], projected[2]), "blk", (0, 0))
    tok_rows = tokens.shape[0]
    head_cols = projected.shape[2]
    heads_here = head_cols // HD
    inv_root = HD ** (-0.5)
    queries = projected[0].reshape(tok_rows, heads_here, HD)
    key_all = key_rows.reshape(-1, heads_here, HD)
    value_all = value_rows.reshape(-1, heads_here, HD)
    grad_out = out_grad.reshape(tok_rows, heads_here, HD)
    scores = (
        jnp.einsum("qhd,khd->hqk", queries, key_all, preferred_element_type=jnp.float32) * inv_root
    )
    top_score = jnp.max(scores, axis=2, keepdims=True)
    expo = jnp.exp(scores - top_score)
    total = jnp.sum(expo, axis=2, keepdims=True)
    probs = expo / total
    probs_b = probs.astype(jnp.bfloat16)
    attended = jnp.einsum("hqk,khd->qhd", probs_b, value_all, preferred_element_type=jnp.float32)
    row_delta = jnp.sum(grad_out.astype(jnp.float32) * attended, axis=2).T[:, :, None]
    score_grad = jnp.einsum("qhd,khd->hqk", grad_out, value_all, preferred_element_type=jnp.float32)
    dscore = (probs * (score_grad - row_delta) * inv_root).astype(jnp.bfloat16)
    grad_query = jnp.einsum("hqk,khd->qhd", dscore, key_all, preferred_element_type=jnp.float32)
    grad_query = grad_query.astype(jnp.bfloat16).reshape(tok_rows, head_cols)
    key_term = jnp.einsum("hqk,qhd->khd", dscore, queries, preferred_element_type=jnp.float32)
    value_term = jnp.einsum("hqk,qhd->khd", probs_b, grad_out, preferred_element_type=jnp.float32)
    key_value_grad = lax.psum_scatter(
        jnp.concatenate(
            [
                key_term.reshape(tok_rows * lax.axis_size("blk"), head_cols),
                value_term.reshape(tok_rows * lax.axis_size("blk"), head_cols),
            ],
            axis=1,
        ),
        "blk",
        scatter_dimension=0,
        tiled=True,
    ).astype(jnp.bfloat16)
    grad_key = key_value_grad[:, :head_cols]
    grad_value = key_value_grad[:, head_cols:]
    stacked_grads = jnp.stack([grad_query, grad_key, grad_value])
    partial_grad = jnp.einsum(
        "ste,sde->td", stacked_grads, qkv_rows, preferred_element_type=jnp.float32
    )
    grad_tokens = slab_sum(partial_grad)
    patch_grad = jnp.einsum(
        "td,pfd->tpf", grad_tokens, embed_rows, preferred_element_type=jnp.float32
    ).astype(jnp.bfloat16)
    grid_grad = patch_grad.reshape(y_blocks, z_blocks, x_local, PY, PZ, channels).transpose(
        2, 0, 3, 1, 4, 5
    )
    grid_grad = grid_grad.reshape(x_local, y_cells, z_total, channels)
    grid_grad = lax.all_to_all(grid_grad, "zslab", split_axis=2, concat_axis=0, tiled=True)
    for layer_num in reversed(range(LAYERS)):
        conv_out = conv_outs[layer_num]
        sigma = jax.nn.sigmoid(conv_out)
        slope_grad = (
            gate_mask * sigma * (1.0 + conv_out * (1.0 - sigma)) * grid_grad.astype(jnp.float32)
        ).astype(jnp.bfloat16)
        flipped = (
            conv_weight[layer_num]
            .reshape(27, channels, channels)
            .transpose(0, 2, 1)
            .reshape(27 * channels, channels)
        )
        backward = apply_offsets(
            with_rim(slope_grad), flipped, dilation[layer_num], -1, field.shape
        )
        grid_grad = (grid_grad.astype(jnp.float32) + backward).astype(jnp.bfloat16)
    return grid_grad


def solution(mesh):
    return jax.shard_map(
        local,
        mesh=mesh,
        in_specs=(
            P("blk", None, "zslab", None),
            P("blk", None, "zslab"),
            P(),
            P(),
            P("zslab", "blk", None),
            P(None, "blk", "zslab"),
            P("blk", "zslab"),
        ),
        out_specs=P("blk", None, "zslab", None),
        check_vma=False,
    )
```

```python
import jax
import jax.numpy as jnp
from jax import lax
from jax.sharding import PartitionSpec as P

HD = 128
PY = 8
PZ = 2
LAYERS = 2
DMAX = 2


def padded_2(cells, sides, width):
    for axis, dim in sides:
        count = lax.axis_size(axis)
        ends = count - 1
        head = lax.slice_in_dim(cells, 0, width, axis=dim)
        tail = lax.slice_in_dim(cells, cells.shape[dim] - width, cells.shape[dim], axis=dim)
        cells = jnp.concatenate(
            [
                lax.ppermute(tail, axis, [(i, (i + 1) % count) for i in range(ends)]),
                cells,
                lax.ppermute(head, axis, [((i + 1) % count, i) for i in range(ends)]),
            ],
            axis=dim,
        )
    return cells


def copy_for_each(shard, axis):
    peers = lax.axis_size(axis)
    return lax.all_to_all(
        jnp.broadcast_to(shard[None], (peers, *shard.shape)), axis, 0, 0, tiled=True
    )


def taken_together(shard, axis):
    return copy_for_each(shard, axis).astype(jnp.float32).sum(axis=0)


def joined_along(pieces, dim):
    shape = list(pieces.shape[1:])
    shape[dim] *= pieces.shape[0]
    return jnp.moveaxis(pieces, 0, dim).reshape(shape)


def gather_together(arrays, axis, dims):
    line = jnp.concatenate([a.reshape(-1) for a in arrays])
    lines, at, finished = (lax.all_gather(line, axis), 0, [])
    for a, dim in zip(arrays, dims):
        pieces = lines[:, at : at + a.size].reshape(-1, *a.shape)
        finished.append(joined_along(pieces, dim))
        at += a.size
    return tuple(finished)


def side_by_side(arrays, axis, dim, along):
    ends, at = ([], 0)
    for a in arrays[:-1]:
        at += a.shape[along]
        ends.append(at)
    both = jnp.concatenate(arrays, axis=along)
    return tuple(jnp.split(lax.all_gather(both, axis, axis=dim, tiled=True), ends, axis=along))


def cut_along(shard, dim, peers):
    before, after = (shard.shape[:dim], shard.shape[dim + 1 :])
    return jnp.moveaxis(shard.reshape(*before, peers, -1, *after), dim, 0)


def sum_at_owner(shard, axis, dim):
    peers = lax.axis_size(axis)
    pieces = lax.all_to_all(cut_along(shard, dim, peers), axis, 0, 0, tiled=True)
    return jnp.sum(pieces.astype(jnp.float32), axis=0)


def gather_weights(embed_weight, qkv_weight):
    _, feat, width = embed_weight.shape
    qkv_flat = qkv_weight.reshape(-1, width)
    extra = -qkv_flat.shape[0] % 16
    rows = jnp.concatenate(
        [embed_weight[0], qkv_flat, jnp.zeros((extra, width), qkv_flat.dtype)], axis=0
    )
    gathered = lax.all_gather(rows, "blk", axis=0, tiled=True)
    peers = lax.axis_size("blk")
    gathered = gathered.reshape(peers, rows.shape[0], width)
    embed_rows = gathered[:, :feat, :]
    qkv_rows = gathered[:, feat : feat + qkv_flat.shape[0], :].reshape(peers, *qkv_weight.shape)
    qkv_rows = jnp.moveaxis(qkv_rows, 0, 1).reshape(
        qkv_weight.shape[0], peers * qkv_weight.shape[1], qkv_weight.shape[2]
    )
    return embed_rows, qkv_rows


def with_rim(volume):
    padded = padded_2(volume, (("zslab", 2), ("blk", 0)), DMAX)
    return jnp.pad(padded, ((0, 0), (DMAX, DMAX), (0, 0), (0, 0)))


def apply_offsets(padded, weight, dilate, direction, dims_out):
    x_cells, y_cells, z_cells, channels = dims_out
    summed = jnp.zeros((x_cells * y_cells * z_cells, weight.shape[-1]), jnp.float32)
    for offset_x in (-1, 0, 1):
        pieces = []
        for offset_y in (-1, 0, 1):
            for offset_z in (-1, 0, 1):
                anchor = (
                    DMAX + direction * offset_x * dilate[0],
                    DMAX + direction * offset_y * dilate[1],
                    DMAX + direction * offset_z * dilate[2],
                    jnp.int32(0),
                )
                pieces.append(
                    lax.dynamic_slice(padded, anchor, (x_cells, y_cells, z_cells, channels))
                )
        stacked = jnp.concatenate(pieces, axis=3).reshape(x_cells * y_cells * z_cells, 9 * channels)
        group_rows = weight[(offset_x + 1) * 9 * channels : (offset_x + 2) * 9 * channels]
        summed = summed + jnp.dot(stacked, group_rows, preferred_element_type=jnp.float32)
    return summed.reshape(x_cells, y_cells, z_cells, -1)


def slab_total(term):
    return taken_together(term.astype(jnp.bfloat16), "zslab").astype(jnp.float32)


def local(field, fracture_mask, dilation, conv_weight, embed_weight, qkv_weight, out_grad):
    x_cells, y_cells, z_cells, channels = field.shape
    gate_mask = fracture_mask.astype(jnp.float32)[..., None]
    hidden = field
    conv_outs = []
    for layer_num in range(LAYERS):
        conv_out = apply_offsets(
            with_rim(hidden), conv_weight[layer_num], dilation[layer_num], 1, field.shape
        )
        conv_outs.append(conv_out)
        hidden = (
            hidden.astype(jnp.float32) + gate_mask * (conv_out * jax.nn.sigmoid(conv_out))
        ).astype(jnp.bfloat16)
    slab_view = lax.all_to_all(hidden, "zslab", split_axis=0, concat_axis=2, tiled=True)
    x_local, z_total = (slab_view.shape[0], slab_view.shape[2])
    y_blocks, z_blocks = (y_cells // PY, z_total // PZ)
    patches = slab_view.reshape(x_local, y_blocks, PY, z_blocks, PZ, channels).transpose(
        1, 3, 0, 2, 4, 5
    )
    patches = patches.reshape(y_blocks * z_blocks, x_local, PY * PZ * channels)
    embed_rows, qkv_rows = gather_weights(embed_weight, qkv_weight)
    patches = patches.reshape(patches.shape[0], embed_rows.shape[0], embed_rows.shape[1])
    partial_value = jnp.einsum(
        "tbf,bfd->td", patches, embed_rows, preferred_element_type=jnp.float32
    )
    tokens = slab_total(partial_value).astype(jnp.bfloat16)
    projected = jnp.einsum(
        "td,sde->ste", tokens, qkv_rows, preferred_element_type=jnp.float32
    ).astype(jnp.bfloat16)
    key_rows, value_rows = jnp.split(
        joined_along(copy_for_each(jnp.concatenate([projected[1], projected[2]], axis=1), "blk"), 0),
        2,
        axis=1,
    )
    tok_rows = tokens.shape[0]
    head_cols = projected.shape[2]
    heads_here = head_cols // HD
    inv_root = HD ** (-0.5)
    queries = projected[0].reshape(tok_rows, heads_here, HD)
    key_all = key_rows.reshape(-1, heads_here, HD)
    value_all = value_rows.reshape(-1, heads_here, HD)
    grad_out = out_grad.reshape(tok_rows, heads_here, HD)
    scores = (
        jnp.einsum("qhd,khd->hqk", queries, key_all, preferred_element_type=jnp.float32) * inv_root
    )
    top_score = jnp.max(scores, axis=2, keepdims=True)
    expo = jnp.exp(scores - top_score)
    total = jnp.sum(expo, axis=2, keepdims=True)
    probs = expo / total
    probs_b = probs.astype(jnp.bfloat16)
    attended = jnp.einsum("hqk,khd->qhd", probs_b, value_all, preferred_element_type=jnp.float32)
    row_delta = jnp.sum(grad_out.astype(jnp.float32) * attended, axis=2).T[:, :, None]
    score_grad = jnp.einsum("qhd,khd->hqk", grad_out, value_all, preferred_element_type=jnp.float32)
    dscore = (probs * (score_grad - row_delta) * inv_root).astype(jnp.bfloat16)
    grad_query = jnp.einsum("hqk,khd->qhd", dscore, key_all, preferred_element_type=jnp.float32)
    grad_query = grad_query.astype(jnp.bfloat16).reshape(tok_rows, head_cols)
    key_term = jnp.einsum("hqk,qhd->khd", dscore, queries, preferred_element_type=jnp.float32)
    value_term = jnp.einsum("hqk,qhd->khd", probs_b, grad_out, preferred_element_type=jnp.float32)
    key_value_grad = sum_at_owner(
        jnp.concatenate(
            [
                key_term.reshape(tok_rows * lax.axis_size("blk"), head_cols),
                value_term.reshape(tok_rows * lax.axis_size("blk"), head_cols),
            ],
            axis=1,
        ).astype(jnp.bfloat16),
        "blk",
        0,
    ).astype(jnp.bfloat16)
    grad_key = key_value_grad[:, :head_cols]
    grad_value = key_value_grad[:, head_cols:]
    stacked_grads = jnp.stack([grad_query, grad_key, grad_value])
    partial_grad = jnp.einsum(
        "ste,sde->td", stacked_grads, qkv_rows, preferred_element_type=jnp.float32
    )
    grad_tokens = slab_total(partial_grad).astype(jnp.bfloat16)
    patch_grad = jnp.einsum(
        "td,bfd->tbf", grad_tokens, embed_rows, preferred_element_type=jnp.float32
    ).astype(jnp.bfloat16)
    grid_grad = patch_grad.reshape(y_blocks, z_blocks, x_local, PY, PZ, channels).transpose(
        2, 0, 3, 1, 4, 5
    )
    grid_grad = grid_grad.reshape(x_local, y_cells, z_total, channels)
    grid_grad = lax.all_to_all(grid_grad, "zslab", split_axis=2, concat_axis=0, tiled=True)
    for layer_num in reversed(range(LAYERS)):
        conv_out = conv_outs[layer_num]
        sigma = jax.nn.sigmoid(conv_out)
        slope_grad = (
            gate_mask * sigma * (1.0 + conv_out * (1.0 - sigma)) * grid_grad.astype(jnp.float32)
        ).astype(jnp.bfloat16)
        flipped = (
            conv_weight[layer_num]
            .reshape(27, channels, channels)
            .transpose(0, 2, 1)
            .reshape(27 * channels, channels)
        )
        backward = apply_offsets(
            with_rim(slope_grad), flipped, dilation[layer_num], -1, field.shape
        )
        grid_grad = (grid_grad.astype(jnp.float32) + backward).astype(jnp.bfloat16)
    return grid_grad


def solution(mesh):
    return jax.shard_map(
        local,
        mesh=mesh,
        in_specs=(
            P("blk", None, "zslab", None),
            P("blk", None, "zslab"),
            P(),
            P(),
            P("zslab", "blk", None),
            P(None, "blk", "zslab"),
            P("blk", "zslab"),
        ),
        out_specs=P("blk", None, "zslab", None),
        check_vma=False,
    )
```

```python
import jax
import jax.numpy as jnp
from jax import lax
from jax.sharding import PartitionSpec as P

HD = 128
PY = 8
PZ = 2
LAYERS = 2
DMAX = 2


def padded_2(cells, sides, width):
    for axis, dim in sides:
        count = lax.axis_size(axis)
        ends = count - 1
        head = lax.slice_in_dim(cells, 0, width, axis=dim)
        tail = lax.slice_in_dim(cells, cells.shape[dim] - width, cells.shape[dim], axis=dim)
        cells = jnp.concatenate(
            [
                lax.ppermute(tail, axis, [(i, (i + 1) % count) for i in range(ends)]),
                cells,
                lax.ppermute(head, axis, [((i + 1) % count, i) for i in range(ends)]),
            ],
            axis=dim,
        )
    return cells


def copy_for_each(shard, axis):
    peers = lax.axis_size(axis)
    return lax.all_to_all(
        jnp.broadcast_to(shard[None], (peers, *shard.shape)), axis, 0, 0, tiled=True
    )


def taken_together(shard, axis):
    return copy_for_each(shard, axis).astype(jnp.float32).sum(axis=0)


def joined_along(pieces, dim):
    shape = list(pieces.shape[1:])
    shape[dim] *= pieces.shape[0]
    return jnp.moveaxis(pieces, 0, dim).reshape(shape)


def gather_together(arrays, axis, dims):
    line = jnp.concatenate([a.reshape(-1) for a in arrays])
    lines, at, finished = (lax.all_gather(line, axis), 0, [])
    for a, dim in zip(arrays, dims):
        pieces = lines[:, at : at + a.size].reshape(-1, *a.shape)
        finished.append(joined_along(pieces, dim))
        at += a.size
    return tuple(finished)


def side_by_side(arrays, axis, dim, along):
    ends, at = ([], 0)
    for a in arrays[:-1]:
        at += a.shape[along]
        ends.append(at)
    both = jnp.concatenate(arrays, axis=along)
    return tuple(jnp.split(lax.all_gather(both, axis, axis=dim, tiled=True), ends, axis=along))


def cut_along(shard, dim, peers):
    before, after = (shard.shape[:dim], shard.shape[dim + 1 :])
    return jnp.moveaxis(shard.reshape(*before, peers, -1, *after), dim, 0)


def sum_at_owner(shard, axis, dim):
    peers = lax.axis_size(axis)
    pieces = lax.all_to_all(cut_along(shard, dim, peers), axis, 0, 0, tiled=True)
    return jnp.sum(pieces.astype(jnp.float32), axis=0)


def gather_weights(embed_weight, qkv_weight):
    _, feat, width = embed_weight.shape
    qkv_flat = qkv_weight.reshape(-1, width)
    extra = -qkv_flat.shape[0] % 16
    rows = jnp.concatenate(
        [embed_weight[0], qkv_flat, jnp.zeros((extra, width), qkv_flat.dtype)], axis=0
    )
    gathered = lax.all_gather(rows, "blk", axis=0, tiled=True)
    peers = lax.axis_size("blk")
    gathered = gathered.reshape(peers, rows.shape[0], width)
    embed_rows = gathered[:, :feat, :]
    qkv_rows = gathered[:, feat : feat + qkv_flat.shape[0], :].reshape(peers, *qkv_weight.shape)
    qkv_rows = jnp.moveaxis(qkv_rows, 0, 1).reshape(
        qkv_weight.shape[0], peers * qkv_weight.shape[1], qkv_weight.shape[2]
    )
    return embed_rows, qkv_rows


def with_rim(volume):
    return padded_2(volume, (("zslab", 1), ("blk", 0)), DMAX)


def picked(cells, dim, step, rate, size):
    near = lax.slice_in_dim(cells, DMAX + step, DMAX + step + size, axis=dim)
    if step == 0:
        return near
    far = lax.slice_in_dim(cells, DMAX + 2 * step, DMAX + 2 * step + size, axis=dim)
    return jnp.where(rate == 1, near, far)


def shifted_y(values, step, rate):
    def by(amount):
        cells = values.shape[2]
        zeros = jnp.zeros_like(values[:, :, : abs(amount)])
        if amount > 0:
            return jnp.concatenate([values[:, :, amount:], zeros], axis=2)
        return jnp.concatenate([zeros, values[:, :, : cells + amount]], axis=2)

    if step == 0:
        return values
    return jnp.where(rate == 1, by(step), by(2 * step))


def apply_offsets(padded, weight, dilate, direction, dims_out):
    x_cells, z_cells, y_cells, channels = dims_out
    windows = []
    for offset_x in (-1, 0, 1):
        along_x = picked(padded, 0, direction * offset_x, dilate[0], x_cells)
        for offset_z in (-1, 0, 1):
            windows.append(picked(along_x, 1, direction * offset_z, dilate[2], z_cells))
    stacked = jnp.concatenate(windows, axis=3).reshape(x_cells * z_cells * y_cells, 9 * channels)
    taps = weight.reshape(3, 3, 3, channels, -1)
    summed = None
    for offset_y in (-1, 0, 1):
        rows = taps[:, offset_y + 1].reshape(9 * channels, -1)
        part = jnp.dot(stacked, rows, preferred_element_type=jnp.float32)
        part = shifted_y(part.reshape(x_cells, z_cells, y_cells, -1), direction * offset_y, dilate[1])
        summed = part if summed is None else summed + part
    return summed


def slab_total(term):
    return taken_together(term.astype(jnp.bfloat16), "zslab").astype(jnp.float32)


def local(field, fracture_mask, dilation, conv_weight, embed_weight, qkv_weight, out_grad):
    field = field.transpose(0, 2, 1, 3)
    fracture_mask = fracture_mask.transpose(0, 2, 1)
    x_cells, z_cells, y_cells, channels = field.shape
    gate_mask = fracture_mask.astype(jnp.float32)[..., None]
    hidden = field
    conv_outs = []
    for layer_num in range(LAYERS):
        conv_out = apply_offsets(
            with_rim(hidden), conv_weight[layer_num], dilation[layer_num], 1, field.shape
        )
        conv_outs.append(conv_out)
        hidden = (
            hidden.astype(jnp.float32) + gate_mask * (conv_out * jax.nn.sigmoid(conv_out))
        ).astype(jnp.bfloat16)
    slab_view = lax.all_to_all(hidden, "zslab", split_axis=0, concat_axis=1, tiled=True)
    x_local, z_total = (slab_view.shape[0], slab_view.shape[1])
    y_blocks, z_blocks = (y_cells // PY, z_total // PZ)
    patches = slab_view.reshape(x_local, z_blocks, PZ, y_blocks, PY, channels).transpose(
        3, 1, 0, 4, 2, 5
    )
    patches = patches.reshape(y_blocks * z_blocks, x_local, PY * PZ * channels)
    embed_rows, qkv_rows = gather_weights(embed_weight, qkv_weight)
    patches = patches.reshape(patches.shape[0], embed_rows.shape[0], embed_rows.shape[1])
    partial_value = jnp.einsum(
        "tbf,bfd->td", patches, embed_rows, preferred_element_type=jnp.float32
    )
    tokens = slab_total(partial_value).astype(jnp.bfloat16)
    projected = jnp.einsum(
        "td,sde->ste", tokens, qkv_rows, preferred_element_type=jnp.float32
    ).astype(jnp.bfloat16)
    key_rows, value_rows = jnp.split(
        joined_along(copy_for_each(jnp.concatenate([projected[1], projected[2]], axis=1), "blk"), 0),
        2,
        axis=1,
    )
    tok_rows = tokens.shape[0]
    head_cols = projected.shape[2]
    heads_here = head_cols // HD
    inv_root = HD ** (-0.5)
    queries = projected[0].reshape(tok_rows, heads_here, HD)
    key_all = key_rows.reshape(-1, heads_here, HD)
    value_all = value_rows.reshape(-1, heads_here, HD)
    grad_out = out_grad.reshape(tok_rows, heads_here, HD)
    scores = (
        jnp.einsum("qhd,khd->hqk", queries, key_all, preferred_element_type=jnp.float32) * inv_root
    )
    top_score = jnp.max(scores, axis=2, keepdims=True)
    expo = jnp.exp(scores - top_score)
    total = jnp.sum(expo, axis=2, keepdims=True)
    probs = expo / total
    probs_b = probs.astype(jnp.bfloat16)
    attended = jnp.einsum("hqk,khd->qhd", probs_b, value_all, preferred_element_type=jnp.float32)
    row_delta = jnp.sum(grad_out.astype(jnp.float32) * attended, axis=2).T[:, :, None]
    score_grad = jnp.einsum("qhd,khd->hqk", grad_out, value_all, preferred_element_type=jnp.float32)
    dscore = (probs * (score_grad - row_delta) * inv_root).astype(jnp.bfloat16)
    grad_query = jnp.einsum("hqk,khd->qhd", dscore, key_all, preferred_element_type=jnp.float32)
    grad_query = grad_query.astype(jnp.bfloat16).reshape(tok_rows, head_cols)
    key_term = jnp.einsum("hqk,qhd->khd", dscore, queries, preferred_element_type=jnp.float32)
    value_term = jnp.einsum("hqk,qhd->khd", probs_b, grad_out, preferred_element_type=jnp.float32)
    key_value_grad = sum_at_owner(
        jnp.concatenate(
            [
                key_term.reshape(tok_rows * lax.axis_size("blk"), head_cols),
                value_term.reshape(tok_rows * lax.axis_size("blk"), head_cols),
            ],
            axis=1,
        ).astype(jnp.bfloat16),
        "blk",
        0,
    ).astype(jnp.bfloat16)
    grad_key = key_value_grad[:, :head_cols]
    grad_value = key_value_grad[:, head_cols:]
    stacked_grads = jnp.stack([grad_query, grad_key, grad_value])
    partial_grad = jnp.einsum(
        "ste,sde->td", stacked_grads, qkv_rows, preferred_element_type=jnp.float32
    )
    grad_tokens = slab_total(partial_grad).astype(jnp.bfloat16)
    patch_grad = jnp.einsum(
        "td,bfd->tbf", grad_tokens, embed_rows, preferred_element_type=jnp.float32
    ).astype(jnp.bfloat16)
    grid_grad = patch_grad.reshape(y_blocks, z_blocks, x_local, PY, PZ, channels).transpose(
        2, 1, 4, 0, 3, 5
    )
    grid_grad = grid_grad.reshape(x_local, z_total, y_cells, channels)
    grid_grad = lax.all_to_all(grid_grad, "zslab", split_axis=1, concat_axis=0, tiled=True)
    for layer_num in reversed(range(LAYERS)):
        conv_out = conv_outs[layer_num]
        sigma = jax.nn.sigmoid(conv_out)
        slope_grad = (
            gate_mask * sigma * (1.0 + conv_out * (1.0 - sigma)) * grid_grad.astype(jnp.float32)
        ).astype(jnp.bfloat16)
        flipped = (
            conv_weight[layer_num]
            .reshape(27, channels, channels)
            .transpose(0, 2, 1)
            .reshape(27 * channels, channels)
        )
        backward = apply_offsets(
            with_rim(slope_grad), flipped, dilation[layer_num], -1, field.shape
        )
        grid_grad = (grid_grad.astype(jnp.float32) + backward).astype(jnp.bfloat16)
    return grid_grad.transpose(0, 2, 1, 3)


def solution(mesh):
    return jax.shard_map(
        local,
        mesh=mesh,
        in_specs=(
            P("blk", None, "zslab", None),
            P("blk", None, "zslab"),
            P(),
            P(),
            P("zslab", "blk", None),
            P(None, "blk", "zslab"),
            P("blk", "zslab"),
        ),
        out_specs=P("blk", None, "zslab", None),
        check_vma=False,
    )
```

```python
import jax
import jax.numpy as jnp
from jax import lax
from jax.sharding import PartitionSpec as P

HD = 128
PY = 8
PZ = 2
LAYERS = 2
DMAX = 2


def padded_2(cells, sides, width):
    for axis, dim in sides:
        count = lax.axis_size(axis)
        ends = count - 1
        head = lax.slice_in_dim(cells, 0, width, axis=dim)
        tail = lax.slice_in_dim(cells, cells.shape[dim] - width, cells.shape[dim], axis=dim)
        cells = jnp.concatenate(
            [
                lax.ppermute(tail, axis, [(i, (i + 1) % count) for i in range(ends)]),
                cells,
                lax.ppermute(head, axis, [((i + 1) % count, i) for i in range(ends)]),
            ],
            axis=dim,
        )
    return cells


def copy_for_each(shard, axis):
    peers = lax.axis_size(axis)
    return lax.all_to_all(
        jnp.broadcast_to(shard[None], (peers, *shard.shape)), axis, 0, 0, tiled=True
    )


def taken_together(shard, axis):
    return copy_for_each(shard, axis).astype(jnp.float32).sum(axis=0)


def joined_along(pieces, dim):
    shape = list(pieces.shape[1:])
    shape[dim] *= pieces.shape[0]
    return jnp.moveaxis(pieces, 0, dim).reshape(shape)


def gather_together(arrays, axis, dims):
    line = jnp.concatenate([a.reshape(-1) for a in arrays])
    lines, at, finished = (lax.all_gather(line, axis), 0, [])
    for a, dim in zip(arrays, dims):
        pieces = lines[:, at : at + a.size].reshape(-1, *a.shape)
        finished.append(joined_along(pieces, dim))
        at += a.size
    return tuple(finished)


def side_by_side(arrays, axis, dim, along):
    ends, at = ([], 0)
    for a in arrays[:-1]:
        at += a.shape[along]
        ends.append(at)
    both = jnp.concatenate(arrays, axis=along)
    return tuple(jnp.split(lax.all_gather(both, axis, axis=dim, tiled=True), ends, axis=along))


def cut_along(shard, dim, peers):
    before, after = (shard.shape[:dim], shard.shape[dim + 1 :])
    return jnp.moveaxis(shard.reshape(*before, peers, -1, *after), dim, 0)


def sum_at_owner(shard, axis, dim):
    peers = lax.axis_size(axis)
    pieces = lax.all_to_all(cut_along(shard, dim, peers), axis, 0, 0, tiled=True)
    return jnp.sum(pieces.astype(jnp.float32), axis=0)


def gathered_by_doubling(block, axis):
    peers = lax.axis_size(axis)
    here = lax.axis_index(axis)
    held = block[None]
    distance = peers // 2
    while distance >= 1:
        got = lax.ppermute(held, axis, [(i, i ^ distance) for i in range(peers)])
        upper = (here & distance) != 0
        lower_half = jnp.where(upper, got, held)
        upper_half = jnp.where(upper, held, got)
        held = jnp.stack([lower_half, upper_half], axis=1).reshape(-1, *block.shape)
        distance //= 2
    return held.reshape(peers * block.shape[0], *block.shape[1:])


def gather_weights(embed_weight, qkv_weight):
    _, feat, width = embed_weight.shape
    qkv_flat = qkv_weight.reshape(-1, width)
    extra = -qkv_flat.shape[0] % 16
    rows = jnp.concatenate(
        [embed_weight[0], qkv_flat, jnp.zeros((extra, width), qkv_flat.dtype)], axis=0
    )
    peers = lax.axis_size("blk")
    gathered = gathered_by_doubling(rows, "blk").reshape(peers, rows.shape[0], width)
    embed_rows = gathered[:, :feat, :]
    qkv_rows = gathered[:, feat : feat + qkv_flat.shape[0], :].reshape(peers, *qkv_weight.shape)
    qkv_rows = jnp.moveaxis(qkv_rows, 0, 1).reshape(
        qkv_weight.shape[0], peers * qkv_weight.shape[1], qkv_weight.shape[2]
    )
    return embed_rows, qkv_rows


def with_rim(volume):
    return padded_2(volume, (("zslab", 1), ("blk", 0)), DMAX)


def picked(cells, dim, step, rate, size):
    near = lax.slice_in_dim(cells, DMAX + step, DMAX + step + size, axis=dim)
    if step == 0:
        return near
    far = lax.slice_in_dim(cells, DMAX + 2 * step, DMAX + 2 * step + size, axis=dim)
    return jnp.where(rate == 1, near, far)


def shifted_y(values, step, rate):
    def by(amount):
        cells = values.shape[2]
        zeros = jnp.zeros_like(values[:, :, : abs(amount)])
        if amount > 0:
            return jnp.concatenate([values[:, :, amount:], zeros], axis=2)
        return jnp.concatenate([zeros, values[:, :, : cells + amount]], axis=2)

    if step == 0:
        return values
    return jnp.where(rate == 1, by(step), by(2 * step))


def apply_offsets(padded, weight, dilate, direction, dims_out):
    x_cells, z_cells, y_cells, channels = dims_out
    windows = []
    for offset_x in (-1, 0, 1):
        along_x = picked(padded, 0, direction * offset_x, dilate[0], x_cells)
        for offset_z in (-1, 0, 1):
            windows.append(picked(along_x, 1, direction * offset_z, dilate[2], z_cells))
    stacked = jnp.concatenate(windows, axis=3).reshape(x_cells * z_cells * y_cells, 9 * channels)
    taps = weight.reshape(3, 3, 3, channels, -1)
    summed = None
    for offset_y in (-1, 0, 1):
        rows = taps[:, offset_y + 1].reshape(9 * channels, -1)
        part = jnp.dot(stacked, rows, preferred_element_type=jnp.float32)
        part = shifted_y(part.reshape(x_cells, z_cells, y_cells, -1), direction * offset_y, dilate[1])
        summed = part if summed is None else summed + part
    return summed


def slab_total(term):
    return taken_together(term.astype(jnp.bfloat16), "zslab").astype(jnp.float32)


def local(field, fracture_mask, dilation, conv_weight, embed_weight, qkv_weight, out_grad):
    field = field.transpose(0, 2, 1, 3)
    fracture_mask = fracture_mask.transpose(0, 2, 1)
    x_cells, z_cells, y_cells, channels = field.shape
    gate_mask = fracture_mask.astype(jnp.float32)[..., None]
    hidden = field
    conv_outs = []
    for layer_num in range(LAYERS):
        conv_out = apply_offsets(
            with_rim(hidden), conv_weight[layer_num], dilation[layer_num], 1, field.shape
        )
        conv_outs.append(conv_out)
        hidden = (
            hidden.astype(jnp.float32) + gate_mask * (conv_out * jax.nn.sigmoid(conv_out))
        ).astype(jnp.bfloat16)
    slab_view = lax.all_to_all(hidden, "zslab", split_axis=0, concat_axis=1, tiled=True)
    x_local, z_total = (slab_view.shape[0], slab_view.shape[1])
    y_blocks, z_blocks = (y_cells // PY, z_total // PZ)
    patches = slab_view.reshape(x_local, z_blocks, PZ, y_blocks, PY, channels).transpose(
        3, 1, 0, 4, 2, 5
    )
    patches = patches.reshape(y_blocks * z_blocks, x_local, PY * PZ * channels)
    embed_rows, qkv_rows = gather_weights(embed_weight, qkv_weight)
    patches = patches.reshape(patches.shape[0], embed_rows.shape[0], embed_rows.shape[1])
    partial_value = jnp.einsum(
        "tbf,bfd->td", patches, embed_rows, preferred_element_type=jnp.float32
    )
    tokens = slab_total(partial_value).astype(jnp.bfloat16)
    projected = jnp.einsum(
        "td,sde->ste", tokens, qkv_rows, preferred_element_type=jnp.float32
    ).astype(jnp.bfloat16)
    key_rows, value_rows = jnp.split(
        joined_along(copy_for_each(jnp.concatenate([projected[1], projected[2]], axis=1), "blk"), 0),
        2,
        axis=1,
    )
    tok_rows = tokens.shape[0]
    head_cols = projected.shape[2]
    heads_here = head_cols // HD
    inv_root = HD ** (-0.5)
    queries = projected[0].reshape(tok_rows, heads_here, HD)
    key_all = key_rows.reshape(-1, heads_here, HD)
    value_all = value_rows.reshape(-1, heads_here, HD)
    grad_out = out_grad.reshape(tok_rows, heads_here, HD)
    scores = (
        jnp.einsum("qhd,khd->hqk", queries, key_all, preferred_element_type=jnp.float32) * inv_root
    )
    top_score = jnp.max(scores, axis=2, keepdims=True)
    expo = jnp.exp(scores - top_score)
    total = jnp.sum(expo, axis=2, keepdims=True)
    probs = expo / total
    probs_b = probs.astype(jnp.bfloat16)
    attended = jnp.einsum("hqk,khd->qhd", probs_b, value_all, preferred_element_type=jnp.float32)
    row_delta = jnp.sum(grad_out.astype(jnp.float32) * attended, axis=2).T[:, :, None]
    score_grad = jnp.einsum("qhd,khd->hqk", grad_out, value_all, preferred_element_type=jnp.float32)
    dscore = (probs * (score_grad - row_delta) * inv_root).astype(jnp.bfloat16)
    grad_query = jnp.einsum("hqk,khd->qhd", dscore, key_all, preferred_element_type=jnp.float32)
    grad_query = grad_query.astype(jnp.bfloat16).reshape(tok_rows, head_cols)
    key_term = jnp.einsum("hqk,qhd->khd", dscore, queries, preferred_element_type=jnp.float32)
    value_term = jnp.einsum("hqk,qhd->khd", probs_b, grad_out, preferred_element_type=jnp.float32)
    key_value_grad = sum_at_owner(
        jnp.concatenate(
            [
                key_term.reshape(tok_rows * lax.axis_size("blk"), head_cols),
                value_term.reshape(tok_rows * lax.axis_size("blk"), head_cols),
            ],
            axis=1,
        ).astype(jnp.bfloat16),
        "blk",
        0,
    ).astype(jnp.bfloat16)
    grad_key = key_value_grad[:, :head_cols]
    grad_value = key_value_grad[:, head_cols:]
    stacked_grads = jnp.stack([grad_query, grad_key, grad_value])
    partial_grad = jnp.einsum(
        "ste,sde->td", stacked_grads, qkv_rows, preferred_element_type=jnp.float32
    )
    grad_tokens = slab_total(partial_grad).astype(jnp.bfloat16)
    patch_grad = jnp.einsum(
        "td,bfd->tbf", grad_tokens, embed_rows, preferred_element_type=jnp.float32
    ).astype(jnp.bfloat16)
    grid_grad = patch_grad.reshape(y_blocks, z_blocks, x_local, PY, PZ, channels).transpose(
        2, 1, 4, 0, 3, 5
    )
    grid_grad = grid_grad.reshape(x_local, z_total, y_cells, channels)
    grid_grad = lax.all_to_all(grid_grad, "zslab", split_axis=1, concat_axis=0, tiled=True)
    for layer_num in reversed(range(LAYERS)):
        conv_out = conv_outs[layer_num]
        sigma = jax.nn.sigmoid(conv_out)
        slope_grad = (
            gate_mask * sigma * (1.0 + conv_out * (1.0 - sigma)) * grid_grad.astype(jnp.float32)
        ).astype(jnp.bfloat16)
        flipped = (
            conv_weight[layer_num]
            .reshape(27, channels, channels)
            .transpose(0, 2, 1)
            .reshape(27 * channels, channels)
        )
        backward = apply_offsets(
            with_rim(slope_grad), flipped, dilation[layer_num], -1, field.shape
        )
        grid_grad = (grid_grad.astype(jnp.float32) + backward).astype(jnp.bfloat16)
    return grid_grad.transpose(0, 2, 1, 3)


def solution(mesh):
    return jax.shard_map(
        local,
        mesh=mesh,
        in_specs=(
            P("blk", None, "zslab", None),
            P("blk", None, "zslab"),
            P(),
            P(),
            P("zslab", "blk", None),
            P(None, "blk", "zslab"),
            P("blk", "zslab"),
        ),
        out_specs=P("blk", None, "zslab", None),
        check_vma=False,
    )
```

```python
import jax
import jax.numpy as jnp
from jax import lax
from jax.sharding import PartitionSpec as P

HD = 128
PY = 8
PZ = 2
LAYERS = 2
DMAX = 2


def padded_2(cells, sides, width):
    for axis, dim in sides:
        count = lax.axis_size(axis)
        ends = count - 1
        head = lax.slice_in_dim(cells, 0, width, axis=dim)
        tail = lax.slice_in_dim(cells, cells.shape[dim] - width, cells.shape[dim], axis=dim)
        cells = jnp.concatenate(
            [
                lax.ppermute(tail, axis, [(i, (i + 1) % count) for i in range(ends)]),
                cells,
                lax.ppermute(head, axis, [((i + 1) % count, i) for i in range(ends)]),
            ],
            axis=dim,
        )
    return cells


def copy_for_each(shard, axis):
    peers = lax.axis_size(axis)
    return lax.all_to_all(
        jnp.broadcast_to(shard[None], (peers, *shard.shape)), axis, 0, 0, tiled=True
    )


def taken_together(shard, axis):
    return copy_for_each(shard, axis).astype(jnp.float32).sum(axis=0)


def joined_along(pieces, dim):
    shape = list(pieces.shape[1:])
    shape[dim] *= pieces.shape[0]
    return jnp.moveaxis(pieces, 0, dim).reshape(shape)


def gather_together(arrays, axis, dims):
    line = jnp.concatenate([a.reshape(-1) for a in arrays])
    lines, at, finished = (lax.all_gather(line, axis), 0, [])
    for a, dim in zip(arrays, dims):
        pieces = lines[:, at : at + a.size].reshape(-1, *a.shape)
        finished.append(joined_along(pieces, dim))
        at += a.size
    return tuple(finished)


def side_by_side(arrays, axis, dim, along):
    ends, at = ([], 0)
    for a in arrays[:-1]:
        at += a.shape[along]
        ends.append(at)
    both = jnp.concatenate(arrays, axis=along)
    return tuple(jnp.split(lax.all_gather(both, axis, axis=dim, tiled=True), ends, axis=along))


def cut_along(shard, dim, peers):
    before, after = (shard.shape[:dim], shard.shape[dim + 1 :])
    return jnp.moveaxis(shard.reshape(*before, peers, -1, *after), dim, 0)


def sum_at_owner(shard, axis, dim):
    peers = lax.axis_size(axis)
    pieces = lax.all_to_all(cut_along(shard, dim, peers), axis, 0, 0, tiled=True)
    return jnp.sum(pieces.astype(jnp.float32), axis=0)


def gather_weights(embed_weight, qkv_weight):
    peers = lax.axis_size("blk")
    embed_rows = lax.all_gather(embed_weight[0], "blk", axis=0, tiled=True)
    embed_rows = embed_rows.reshape(peers, embed_weight.shape[1], embed_weight.shape[2])
    qkv_rows = jnp.moveaxis(copy_for_each(qkv_weight, "blk").reshape(peers, *qkv_weight.shape), 0, 1)
    qkv_rows = qkv_rows.reshape(qkv_weight.shape[0], -1, qkv_weight.shape[2])
    return embed_rows, qkv_rows


def with_rim(volume):
    return padded_2(volume, (("zslab", 1), ("blk", 0)), DMAX)


def picked(cells, dim, step, rate, size):
    near = lax.slice_in_dim(cells, DMAX + step, DMAX + step + size, axis=dim)
    if step == 0:
        return near
    far = lax.slice_in_dim(cells, DMAX + 2 * step, DMAX + 2 * step + size, axis=dim)
    return jnp.where(rate == 1, near, far)


def shifted_y(values, step, rate):
    def by(amount):
        cells = values.shape[2]
        zeros = jnp.zeros_like(values[:, :, : abs(amount)])
        if amount > 0:
            return jnp.concatenate([values[:, :, amount:], zeros], axis=2)
        return jnp.concatenate([zeros, values[:, :, : cells + amount]], axis=2)

    if step == 0:
        return values
    return jnp.where(rate == 1, by(step), by(2 * step))


def apply_offsets(padded, weight, dilate, direction, dims_out):
    x_cells, z_cells, y_cells, channels = dims_out
    windows = []
    for offset_x in (-1, 0, 1):
        along_x = picked(padded, 0, direction * offset_x, dilate[0], x_cells)
        for offset_z in (-1, 0, 1):
            windows.append(picked(along_x, 1, direction * offset_z, dilate[2], z_cells))
    stacked = jnp.concatenate(windows, axis=3).reshape(x_cells * z_cells * y_cells, 9 * channels)
    taps = weight.reshape(3, 3, 3, channels, -1)
    summed = None
    for offset_y in (-1, 0, 1):
        rows = taps[:, offset_y + 1].reshape(9 * channels, -1)
        part = jnp.dot(stacked, rows, preferred_element_type=jnp.float32)
        part = shifted_y(part.reshape(x_cells, z_cells, y_cells, -1), direction * offset_y, dilate[1])
        summed = part if summed is None else summed + part
    return summed


def slab_total(term):
    return taken_together(term.astype(jnp.bfloat16), "zslab").astype(jnp.float32)


def local(field, fracture_mask, dilation, conv_weight, embed_weight, qkv_weight, out_grad):
    field = field.transpose(0, 2, 1, 3)
    fracture_mask = fracture_mask.transpose(0, 2, 1)
    x_cells, z_cells, y_cells, channels = field.shape
    gate_mask = fracture_mask.astype(jnp.float32)[..., None]
    hidden = field
    conv_outs = []
    for layer_num in range(LAYERS):
        conv_out = apply_offsets(
            with_rim(hidden), conv_weight[layer_num], dilation[layer_num], 1, field.shape
        )
        conv_outs.append(conv_out)
        hidden = (
            hidden.astype(jnp.float32) + gate_mask * (conv_out * jax.nn.sigmoid(conv_out))
        ).astype(jnp.bfloat16)
    slab_view = lax.all_to_all(hidden, "zslab", split_axis=0, concat_axis=1, tiled=True)
    x_local, z_total = (slab_view.shape[0], slab_view.shape[1])
    y_blocks, z_blocks = (y_cells // PY, z_total // PZ)
    patches = slab_view.reshape(x_local, z_blocks, PZ, y_blocks, PY, channels).transpose(
        3, 1, 0, 4, 2, 5
    )
    patches = patches.reshape(y_blocks * z_blocks, x_local, PY * PZ * channels)
    embed_rows, qkv_rows = gather_weights(embed_weight, qkv_weight)
    patches = patches.reshape(patches.shape[0], embed_rows.shape[0], embed_rows.shape[1])
    patches, qkv_rows = lax.optimization_barrier((patches, qkv_rows))
    partial_value = jnp.einsum(
        "tbf,bfd->td", patches, embed_rows, preferred_element_type=jnp.float32
    )
    tokens = slab_total(partial_value).astype(jnp.bfloat16)
    projected = jnp.einsum(
        "td,sde->ste", tokens, qkv_rows, preferred_element_type=jnp.float32
    ).astype(jnp.bfloat16)
    key_rows, value_rows = jnp.split(
        joined_along(copy_for_each(jnp.concatenate([projected[1], projected[2]], axis=1), "blk"), 0),
        2,
        axis=1,
    )
    tok_rows = tokens.shape[0]
    head_cols = projected.shape[2]
    heads_here = head_cols // HD
    inv_root = HD ** (-0.5)
    queries = projected[0].reshape(tok_rows, heads_here, HD)
    key_all = key_rows.reshape(-1, heads_here, HD)
    value_all = value_rows.reshape(-1, heads_here, HD)
    grad_out = out_grad.reshape(tok_rows, heads_here, HD)
    scores = (
        jnp.einsum("qhd,khd->hqk", queries, key_all, preferred_element_type=jnp.float32) * inv_root
    )
    top_score = jnp.max(scores, axis=2, keepdims=True)
    expo = jnp.exp(scores - top_score)
    total = jnp.sum(expo, axis=2, keepdims=True)
    probs = expo / total
    probs_b = probs.astype(jnp.bfloat16)
    attended = jnp.einsum("hqk,khd->qhd", probs_b, value_all, preferred_element_type=jnp.float32)
    row_delta = jnp.sum(grad_out.astype(jnp.float32) * attended, axis=2).T[:, :, None]
    score_grad = jnp.einsum("qhd,khd->hqk", grad_out, value_all, preferred_element_type=jnp.float32)
    dscore = (probs * (score_grad - row_delta) * inv_root).astype(jnp.bfloat16)
    grad_query = jnp.einsum("hqk,khd->qhd", dscore, key_all, preferred_element_type=jnp.float32)
    grad_query = grad_query.astype(jnp.bfloat16).reshape(tok_rows, head_cols)
    key_term = jnp.einsum("hqk,qhd->khd", dscore, queries, preferred_element_type=jnp.float32)
    value_term = jnp.einsum("hqk,qhd->khd", probs_b, grad_out, preferred_element_type=jnp.float32)
    key_value_grad = sum_at_owner(
        jnp.concatenate(
            [
                key_term.reshape(tok_rows * lax.axis_size("blk"), head_cols),
                value_term.reshape(tok_rows * lax.axis_size("blk"), head_cols),
            ],
            axis=1,
        ).astype(jnp.bfloat16),
        "blk",
        0,
    ).astype(jnp.bfloat16)
    grad_key = key_value_grad[:, :head_cols]
    grad_value = key_value_grad[:, head_cols:]
    stacked_grads = jnp.stack([grad_query, grad_key, grad_value])
    partial_grad = jnp.einsum(
        "ste,sde->td", stacked_grads, qkv_rows, preferred_element_type=jnp.float32
    )
    grad_tokens = slab_total(partial_grad).astype(jnp.bfloat16)
    patch_grad = jnp.einsum(
        "td,bfd->tbf", grad_tokens, embed_rows, preferred_element_type=jnp.float32
    ).astype(jnp.bfloat16)
    grid_grad = patch_grad.reshape(y_blocks, z_blocks, x_local, PY, PZ, channels).transpose(
        2, 1, 4, 0, 3, 5
    )
    grid_grad = grid_grad.reshape(x_local, z_total, y_cells, channels)
    grid_grad = lax.all_to_all(grid_grad, "zslab", split_axis=1, concat_axis=0, tiled=True)
    for layer_num in reversed(range(LAYERS)):
        conv_out = conv_outs[layer_num]
        sigma = jax.nn.sigmoid(conv_out)
        slope_grad = (
            gate_mask * sigma * (1.0 + conv_out * (1.0 - sigma)) * grid_grad.astype(jnp.float32)
        ).astype(jnp.bfloat16)
        flipped = (
            conv_weight[layer_num]
            .reshape(27, channels, channels)
            .transpose(0, 2, 1)
            .reshape(27 * channels, channels)
        )
        backward = apply_offsets(
            with_rim(slope_grad), flipped, dilation[layer_num], -1, field.shape
        )
        grid_grad = (grid_grad.astype(jnp.float32) + backward).astype(jnp.bfloat16)
    return grid_grad.transpose(0, 2, 1, 3)


def solution(mesh):
    return jax.shard_map(
        local,
        mesh=mesh,
        in_specs=(
            P("blk", None, "zslab", None),
            P("blk", None, "zslab"),
            P(),
            P(),
            P("zslab", "blk", None),
            P(None, "blk", "zslab"),
            P("blk", "zslab"),
        ),
        out_specs=P("blk", None, "zslab", None),
        check_vma=False,
    )
```

```python
import jax
import jax.numpy as jnp
from jax import lax
from jax.sharding import PartitionSpec as P

HD = 128
PY = 8
PZ = 2
LAYERS = 2
DMAX = 2


def padded_2(cells, sides, width):
    for axis, dim in sides:
        count = lax.axis_size(axis)
        ends = count - 1
        head = lax.slice_in_dim(cells, 0, width, axis=dim)
        tail = lax.slice_in_dim(cells, cells.shape[dim] - width, cells.shape[dim], axis=dim)
        cells = jnp.concatenate(
            [
                lax.ppermute(tail, axis, [(i, (i + 1) % count) for i in range(ends)]),
                cells,
                lax.ppermute(head, axis, [((i + 1) % count, i) for i in range(ends)]),
            ],
            axis=dim,
        )
    return cells


def copy_for_each(shard, axis):
    peers = lax.axis_size(axis)
    return lax.all_to_all(
        jnp.broadcast_to(shard[None], (peers, *shard.shape)), axis, 0, 0, tiled=True
    )


def taken_together(shard, axis):
    return copy_for_each(shard, axis).astype(jnp.float32).sum(axis=0)


def joined_along(pieces, dim):
    shape = list(pieces.shape[1:])
    shape[dim] *= pieces.shape[0]
    return jnp.moveaxis(pieces, 0, dim).reshape(shape)


def gather_together(arrays, axis, dims):
    line = jnp.concatenate([a.reshape(-1) for a in arrays])
    lines, at, finished = (lax.all_gather(line, axis), 0, [])
    for a, dim in zip(arrays, dims):
        pieces = lines[:, at : at + a.size].reshape(-1, *a.shape)
        finished.append(joined_along(pieces, dim))
        at += a.size
    return tuple(finished)


def side_by_side(arrays, axis, dim, along):
    ends, at = ([], 0)
    for a in arrays[:-1]:
        at += a.shape[along]
        ends.append(at)
    both = jnp.concatenate(arrays, axis=along)
    return tuple(jnp.split(lax.all_gather(both, axis, axis=dim, tiled=True), ends, axis=along))


def cut_along(shard, dim, peers):
    before, after = (shard.shape[:dim], shard.shape[dim + 1 :])
    return jnp.moveaxis(shard.reshape(*before, peers, -1, *after), dim, 0)


def sum_at_owner(shard, axis, dim):
    peers = lax.axis_size(axis)
    pieces = lax.all_to_all(cut_along(shard, dim, peers), axis, 0, 0, tiled=True)
    return jnp.sum(pieces.astype(jnp.float32), axis=0)


def gather_weights(embed_weight, qkv_weight):
    _, feat, width = embed_weight.shape
    qkv_flat = qkv_weight.reshape(-1, width)
    extra = -qkv_flat.shape[0] % 16
    rows = jnp.concatenate(
        [embed_weight[0], qkv_flat, jnp.zeros((extra, width), qkv_flat.dtype)], axis=0
    )
    peers = lax.axis_size("blk")
    groups = [list(range(core, peers, 2)) for core in (0, 1)]
    own = lax.all_gather(rows, "blk", axis=0, tiled=True, axis_index_groups=groups)
    other = lax.ppermute(own, "blk", [(i, i ^ 1) for i in range(peers)])
    odd = (lax.axis_index("blk") & 1) != 0
    own = own.reshape(peers // 2, rows.shape[0], width)
    other = other.reshape(peers // 2, rows.shape[0], width)
    gathered = jnp.stack([jnp.where(odd, other, own), jnp.where(odd, own, other)], axis=1)
    gathered = gathered.reshape(peers, rows.shape[0], width)
    embed_rows = gathered[:, :feat, :]
    qkv_rows = gathered[:, feat : feat + qkv_flat.shape[0], :].reshape(peers, *qkv_weight.shape)
    qkv_rows = jnp.moveaxis(qkv_rows, 0, 1).reshape(
        qkv_weight.shape[0], peers * qkv_weight.shape[1], qkv_weight.shape[2]
    )
    return embed_rows, qkv_rows


def with_rim(volume):
    return padded_2(volume, (("zslab", 1), ("blk", 0)), DMAX)


def picked(cells, dim, step, rate, size):
    near = lax.slice_in_dim(cells, DMAX + step, DMAX + step + size, axis=dim)
    if step == 0:
        return near
    far = lax.slice_in_dim(cells, DMAX + 2 * step, DMAX + 2 * step + size, axis=dim)
    return jnp.where(rate == 1, near, far)


def shifted_y(values, step, rate):
    def by(amount):
        cells = values.shape[2]
        zeros = jnp.zeros_like(values[:, :, : abs(amount)])
        if amount > 0:
            return jnp.concatenate([values[:, :, amount:], zeros], axis=2)
        return jnp.concatenate([zeros, values[:, :, : cells + amount]], axis=2)

    if step == 0:
        return values
    return jnp.where(rate == 1, by(step), by(2 * step))


def apply_offsets(padded, weight, dilate, direction, dims_out):
    x_cells, z_cells, y_cells, channels = dims_out
    windows = []
    for offset_x in (-1, 0, 1):
        along_x = picked(padded, 0, direction * offset_x, dilate[0], x_cells)
        for offset_z in (-1, 0, 1):
            windows.append(picked(along_x, 1, direction * offset_z, dilate[2], z_cells))
    stacked = jnp.concatenate(windows, axis=3).reshape(x_cells * z_cells * y_cells, 9 * channels)
    taps = weight.reshape(3, 3, 3, channels, -1)
    summed = None
    for offset_y in (-1, 0, 1):
        rows = taps[:, offset_y + 1].reshape(9 * channels, -1)
        part = jnp.dot(stacked, rows, preferred_element_type=jnp.float32)
        part = shifted_y(part.reshape(x_cells, z_cells, y_cells, -1), direction * offset_y, dilate[1])
        summed = part if summed is None else summed + part
    return summed


def slab_total(term):
    return taken_together(term.astype(jnp.bfloat16), "zslab").astype(jnp.float32)


def local(field, fracture_mask, dilation, conv_weight, embed_weight, qkv_weight, out_grad):
    field = field.transpose(0, 2, 1, 3)
    fracture_mask = fracture_mask.transpose(0, 2, 1)
    x_cells, z_cells, y_cells, channels = field.shape
    gate_mask = fracture_mask.astype(jnp.float32)[..., None]
    hidden = field
    conv_outs = []
    for layer_num in range(LAYERS):
        conv_out = apply_offsets(
            with_rim(hidden), conv_weight[layer_num], dilation[layer_num], 1, field.shape
        )
        conv_outs.append(conv_out)
        hidden = (
            hidden.astype(jnp.float32) + gate_mask * (conv_out * jax.nn.sigmoid(conv_out))
        ).astype(jnp.bfloat16)
    slab_view = lax.all_to_all(hidden, "zslab", split_axis=0, concat_axis=1, tiled=True)
    x_local, z_total = (slab_view.shape[0], slab_view.shape[1])
    y_blocks, z_blocks = (y_cells // PY, z_total // PZ)
    patches = slab_view.reshape(x_local, z_blocks, PZ, y_blocks, PY, channels).transpose(
        3, 1, 0, 4, 2, 5
    )
    patches = patches.reshape(y_blocks * z_blocks, x_local, PY * PZ * channels)
    embed_rows, qkv_rows = gather_weights(embed_weight, qkv_weight)
    patches = patches.reshape(patches.shape[0], embed_rows.shape[0], embed_rows.shape[1])
    partial_value = jnp.einsum(
        "tbf,bfd->td", patches, embed_rows, preferred_element_type=jnp.float32
    )
    tokens = slab_total(partial_value).astype(jnp.bfloat16)
    projected = jnp.einsum(
        "td,sde->ste", tokens, qkv_rows, preferred_element_type=jnp.float32
    ).astype(jnp.bfloat16)
    key_rows, value_rows = jnp.split(
        joined_along(copy_for_each(jnp.concatenate([projected[1], projected[2]], axis=1), "blk"), 0),
        2,
        axis=1,
    )
    tok_rows = tokens.shape[0]
    head_cols = projected.shape[2]
    heads_here = head_cols // HD
    inv_root = HD ** (-0.5)
    queries = projected[0].reshape(tok_rows, heads_here, HD)
    key_all = key_rows.reshape(-1, heads_here, HD)
    value_all = value_rows.reshape(-1, heads_here, HD)
    grad_out = out_grad.reshape(tok_rows, heads_here, HD)
    scores = (
        jnp.einsum("qhd,khd->hqk", queries, key_all, preferred_element_type=jnp.float32) * inv_root
    )
    top_score = jnp.max(scores, axis=2, keepdims=True)
    expo = jnp.exp(scores - top_score)
    total = jnp.sum(expo, axis=2, keepdims=True)
    probs = expo / total
    probs_b = probs.astype(jnp.bfloat16)
    attended = jnp.einsum("hqk,khd->qhd", probs_b, value_all, preferred_element_type=jnp.float32)
    row_delta = jnp.sum(grad_out.astype(jnp.float32) * attended, axis=2).T[:, :, None]
    score_grad = jnp.einsum("qhd,khd->hqk", grad_out, value_all, preferred_element_type=jnp.float32)
    dscore = (probs * (score_grad - row_delta) * inv_root).astype(jnp.bfloat16)
    grad_query = jnp.einsum("hqk,khd->qhd", dscore, key_all, preferred_element_type=jnp.float32)
    grad_query = grad_query.astype(jnp.bfloat16).reshape(tok_rows, head_cols)
    key_term = jnp.einsum("hqk,qhd->khd", dscore, queries, preferred_element_type=jnp.float32)
    value_term = jnp.einsum("hqk,qhd->khd", probs_b, grad_out, preferred_element_type=jnp.float32)
    key_value_grad = sum_at_owner(
        jnp.concatenate(
            [
                key_term.reshape(tok_rows * lax.axis_size("blk"), head_cols),
                value_term.reshape(tok_rows * lax.axis_size("blk"), head_cols),
            ],
            axis=1,
        ).astype(jnp.bfloat16),
        "blk",
        0,
    ).astype(jnp.bfloat16)
    grad_key = key_value_grad[:, :head_cols]
    grad_value = key_value_grad[:, head_cols:]
    stacked_grads = jnp.stack([grad_query, grad_key, grad_value])
    partial_grad = jnp.einsum(
        "ste,sde->td", stacked_grads, qkv_rows, preferred_element_type=jnp.float32
    )
    grad_tokens = slab_total(partial_grad).astype(jnp.bfloat16)
    patch_grad = jnp.einsum(
        "td,bfd->tbf", grad_tokens, embed_rows, preferred_element_type=jnp.float32
    ).astype(jnp.bfloat16)
    grid_grad = patch_grad.reshape(y_blocks, z_blocks, x_local, PY, PZ, channels).transpose(
        2, 1, 4, 0, 3, 5
    )
    grid_grad = grid_grad.reshape(x_local, z_total, y_cells, channels)
    grid_grad = lax.all_to_all(grid_grad, "zslab", split_axis=1, concat_axis=0, tiled=True)
    for layer_num in reversed(range(LAYERS)):
        conv_out = conv_outs[layer_num]
        sigma = jax.nn.sigmoid(conv_out)
        slope_grad = (
            gate_mask * sigma * (1.0 + conv_out * (1.0 - sigma)) * grid_grad.astype(jnp.float32)
        ).astype(jnp.bfloat16)
        flipped = (
            conv_weight[layer_num]
            .reshape(27, channels, channels)
            .transpose(0, 2, 1)
            .reshape(27 * channels, channels)
        )
        backward = apply_offsets(
            with_rim(slope_grad), flipped, dilation[layer_num], -1, field.shape
        )
        grid_grad = (grid_grad.astype(jnp.float32) + backward).astype(jnp.bfloat16)
    return grid_grad.transpose(0, 2, 1, 3)


def solution(mesh):
    return jax.shard_map(
        local,
        mesh=mesh,
        in_specs=(
            P("blk", None, "zslab", None),
            P("blk", None, "zslab"),
            P(),
            P(),
            P("zslab", "blk", None),
            P(None, "blk", "zslab"),
            P("blk", "zslab"),
        ),
        out_specs=P("blk", None, "zslab", None),
        check_vma=False,
    )
```

```python
import jax
import jax.numpy as jnp
from jax import lax
from jax.sharding import PartitionSpec as P

HD = 128
PY = 8
PZ = 2
LAYERS = 2
DMAX = 2


def padded_2(cells, sides, width):
    for axis, dim in sides:
        count = lax.axis_size(axis)
        ends = count - 1
        head = lax.slice_in_dim(cells, 0, width, axis=dim)
        tail = lax.slice_in_dim(cells, cells.shape[dim] - width, cells.shape[dim], axis=dim)
        cells = jnp.concatenate(
            [
                lax.ppermute(tail, axis, [(i, (i + 1) % count) for i in range(ends)]),
                cells,
                lax.ppermute(head, axis, [((i + 1) % count, i) for i in range(ends)]),
            ],
            axis=dim,
        )
    return cells


def copy_for_each(shard, axis):
    peers = lax.axis_size(axis)
    return lax.all_to_all(
        jnp.broadcast_to(shard[None], (peers, *shard.shape)), axis, 0, 0, tiled=True
    )


def taken_together(shard, axis):
    return copy_for_each(shard, axis).astype(jnp.float32).sum(axis=0)


def joined_along(pieces, dim):
    shape = list(pieces.shape[1:])
    shape[dim] *= pieces.shape[0]
    return jnp.moveaxis(pieces, 0, dim).reshape(shape)


def gather_together(arrays, axis, dims):
    line = jnp.concatenate([a.reshape(-1) for a in arrays])
    lines, at, finished = (lax.all_gather(line, axis), 0, [])
    for a, dim in zip(arrays, dims):
        pieces = lines[:, at : at + a.size].reshape(-1, *a.shape)
        finished.append(joined_along(pieces, dim))
        at += a.size
    return tuple(finished)


def side_by_side(arrays, axis, dim, along):
    ends, at = ([], 0)
    for a in arrays[:-1]:
        at += a.shape[along]
        ends.append(at)
    both = jnp.concatenate(arrays, axis=along)
    return tuple(jnp.split(lax.all_gather(both, axis, axis=dim, tiled=True), ends, axis=along))


def cut_along(shard, dim, peers):
    before, after = (shard.shape[:dim], shard.shape[dim + 1 :])
    return jnp.moveaxis(shard.reshape(*before, peers, -1, *after), dim, 0)


def sum_at_owner(shard, axis, dim):
    peers = lax.axis_size(axis)
    pieces = lax.all_to_all(cut_along(shard, dim, peers), axis, 0, 0, tiled=True)
    return jnp.sum(pieces.astype(jnp.float32), axis=0)


def gather_weights(embed_weight, qkv_weight):
    _, feat, width = embed_weight.shape
    qkv_flat = qkv_weight.reshape(-1, width)
    extra = -qkv_flat.shape[0] % 16
    rows = jnp.concatenate(
        [embed_weight[0], qkv_flat, jnp.zeros((extra, width), qkv_flat.dtype)], axis=0
    )
    peers = lax.axis_size("blk")
    near = [list(range(start, start + 4)) for start in range(0, peers, 4)]
    far = [list(range(start, peers, 4)) for start in range(4)]
    gathered = lax.all_gather(rows, "blk", axis=0, tiled=True, axis_index_groups=near)
    gathered = lax.all_gather(gathered, "blk", axis=0, tiled=True, axis_index_groups=far)
    gathered = gathered.reshape(peers, rows.shape[0], width)
    embed_rows = gathered[:, :feat, :]
    qkv_rows = gathered[:, feat : feat + qkv_flat.shape[0], :].reshape(peers, *qkv_weight.shape)
    qkv_rows = jnp.moveaxis(qkv_rows, 0, 1).reshape(
        qkv_weight.shape[0], peers * qkv_weight.shape[1], qkv_weight.shape[2]
    )
    return embed_rows, qkv_rows


def with_rim(volume):
    return padded_2(volume, (("zslab", 1), ("blk", 0)), DMAX)


def picked(cells, dim, step, rate, size):
    near = lax.slice_in_dim(cells, DMAX + step, DMAX + step + size, axis=dim)
    if step == 0:
        return near
    far = lax.slice_in_dim(cells, DMAX + 2 * step, DMAX + 2 * step + size, axis=dim)
    return jnp.where(rate == 1, near, far)


def shifted_y(values, step, rate):
    def by(amount):
        cells = values.shape[2]
        zeros = jnp.zeros_like(values[:, :, : abs(amount)])
        if amount > 0:
            return jnp.concatenate([values[:, :, amount:], zeros], axis=2)
        return jnp.concatenate([zeros, values[:, :, : cells + amount]], axis=2)

    if step == 0:
        return values
    return jnp.where(rate == 1, by(step), by(2 * step))


def apply_offsets(padded, weight, dilate, direction, dims_out):
    x_cells, z_cells, y_cells, channels = dims_out
    windows = []
    for offset_x in (-1, 0, 1):
        along_x = picked(padded, 0, direction * offset_x, dilate[0], x_cells)
        for offset_z in (-1, 0, 1):
            windows.append(picked(along_x, 1, direction * offset_z, dilate[2], z_cells))
    stacked = jnp.concatenate(windows, axis=3).reshape(x_cells * z_cells * y_cells, 9 * channels)
    taps = weight.reshape(3, 3, 3, channels, -1)
    summed = None
    for offset_y in (-1, 0, 1):
        rows = taps[:, offset_y + 1].reshape(9 * channels, -1)
        part = jnp.dot(stacked, rows, preferred_element_type=jnp.float32)
        part = shifted_y(part.reshape(x_cells, z_cells, y_cells, -1), direction * offset_y, dilate[1])
        summed = part if summed is None else summed + part
    return summed


def slab_total(term):
    return taken_together(term.astype(jnp.bfloat16), "zslab").astype(jnp.float32)


def local(field, fracture_mask, dilation, conv_weight, embed_weight, qkv_weight, out_grad):
    field = field.transpose(0, 2, 1, 3)
    fracture_mask = fracture_mask.transpose(0, 2, 1)
    x_cells, z_cells, y_cells, channels = field.shape
    gate_mask = fracture_mask.astype(jnp.float32)[..., None]
    hidden = field
    conv_outs = []
    for layer_num in range(LAYERS):
        conv_out = apply_offsets(
            with_rim(hidden), conv_weight[layer_num], dilation[layer_num], 1, field.shape
        )
        conv_outs.append(conv_out)
        hidden = (
            hidden.astype(jnp.float32) + gate_mask * (conv_out * jax.nn.sigmoid(conv_out))
        ).astype(jnp.bfloat16)
    slab_view = lax.all_to_all(hidden, "zslab", split_axis=0, concat_axis=1, tiled=True)
    x_local, z_total = (slab_view.shape[0], slab_view.shape[1])
    y_blocks, z_blocks = (y_cells // PY, z_total // PZ)
    patches = slab_view.reshape(x_local, z_blocks, PZ, y_blocks, PY, channels).transpose(
        3, 1, 0, 4, 2, 5
    )
    patches = patches.reshape(y_blocks * z_blocks, x_local, PY * PZ * channels)
    embed_rows, qkv_rows = gather_weights(embed_weight, qkv_weight)
    patches = patches.reshape(patches.shape[0], embed_rows.shape[0], embed_rows.shape[1])
    partial_value = jnp.einsum(
        "tbf,bfd->td", patches, embed_rows, preferred_element_type=jnp.float32
    )
    tokens = slab_total(partial_value).astype(jnp.bfloat16)
    projected = jnp.einsum(
        "td,sde->ste", tokens, qkv_rows, preferred_element_type=jnp.float32
    ).astype(jnp.bfloat16)
    key_rows, value_rows = jnp.split(
        joined_along(copy_for_each(jnp.concatenate([projected[1], projected[2]], axis=1), "blk"), 0),
        2,
        axis=1,
    )
    tok_rows = tokens.shape[0]
    head_cols = projected.shape[2]
    heads_here = head_cols // HD
    inv_root = HD ** (-0.5)
    queries = projected[0].reshape(tok_rows, heads_here, HD)
    key_all = key_rows.reshape(-1, heads_here, HD)
    value_all = value_rows.reshape(-1, heads_here, HD)
    grad_out = out_grad.reshape(tok_rows, heads_here, HD)
    scores = (
        jnp.einsum("qhd,khd->hqk", queries, key_all, preferred_element_type=jnp.float32) * inv_root
    )
    top_score = jnp.max(scores, axis=2, keepdims=True)
    expo = jnp.exp(scores - top_score)
    total = jnp.sum(expo, axis=2, keepdims=True)
    probs = expo / total
    probs_b = probs.astype(jnp.bfloat16)
    attended = jnp.einsum("hqk,khd->qhd", probs_b, value_all, preferred_element_type=jnp.float32)
    row_delta = jnp.sum(grad_out.astype(jnp.float32) * attended, axis=2).T[:, :, None]
    score_grad = jnp.einsum("qhd,khd->hqk", grad_out, value_all, preferred_element_type=jnp.float32)
    dscore = (probs * (score_grad - row_delta) * inv_root).astype(jnp.bfloat16)
    grad_query = jnp.einsum("hqk,khd->qhd", dscore, key_all, preferred_element_type=jnp.float32)
    grad_query = grad_query.astype(jnp.bfloat16).reshape(tok_rows, head_cols)
    key_term = jnp.einsum("hqk,qhd->khd", dscore, queries, preferred_element_type=jnp.float32)
    value_term = jnp.einsum("hqk,qhd->khd", probs_b, grad_out, preferred_element_type=jnp.float32)
    key_value_grad = sum_at_owner(
        jnp.concatenate(
            [
                key_term.reshape(tok_rows * lax.axis_size("blk"), head_cols),
                value_term.reshape(tok_rows * lax.axis_size("blk"), head_cols),
            ],
            axis=1,
        ).astype(jnp.bfloat16),
        "blk",
        0,
    ).astype(jnp.bfloat16)
    grad_key = key_value_grad[:, :head_cols]
    grad_value = key_value_grad[:, head_cols:]
    stacked_grads = jnp.stack([grad_query, grad_key, grad_value])
    partial_grad = jnp.einsum(
        "ste,sde->td", stacked_grads, qkv_rows, preferred_element_type=jnp.float32
    )
    grad_tokens = slab_total(partial_grad).astype(jnp.bfloat16)
    patch_grad = jnp.einsum(
        "td,bfd->tbf", grad_tokens, embed_rows, preferred_element_type=jnp.float32
    ).astype(jnp.bfloat16)
    grid_grad = patch_grad.reshape(y_blocks, z_blocks, x_local, PY, PZ, channels).transpose(
        2, 1, 4, 0, 3, 5
    )
    grid_grad = grid_grad.reshape(x_local, z_total, y_cells, channels)
    grid_grad = lax.all_to_all(grid_grad, "zslab", split_axis=1, concat_axis=0, tiled=True)
    for layer_num in reversed(range(LAYERS)):
        conv_out = conv_outs[layer_num]
        sigma = jax.nn.sigmoid(conv_out)
        slope_grad = (
            gate_mask * sigma * (1.0 + conv_out * (1.0 - sigma)) * grid_grad.astype(jnp.float32)
        ).astype(jnp.bfloat16)
        flipped = (
            conv_weight[layer_num]
            .reshape(27, channels, channels)
            .transpose(0, 2, 1)
            .reshape(27 * channels, channels)
        )
        backward = apply_offsets(
            with_rim(slope_grad), flipped, dilation[layer_num], -1, field.shape
        )
        grid_grad = (grid_grad.astype(jnp.float32) + backward).astype(jnp.bfloat16)
    return grid_grad.transpose(0, 2, 1, 3)


def solution(mesh):
    return jax.shard_map(
        local,
        mesh=mesh,
        in_specs=(
            P("blk", None, "zslab", None),
            P("blk", None, "zslab"),
            P(),
            P(),
            P("zslab", "blk", None),
            P(None, "blk", "zslab"),
            P("blk", "zslab"),
        ),
        out_specs=P("blk", None, "zslab", None),
        check_vma=False,
    )
```

```python
import jax
import jax.numpy as jnp
from jax import lax
from jax.sharding import PartitionSpec as P

HD = 128
PY = 8
PZ = 2
LAYERS = 2
DMAX = 2


def padded_2(cells, sides, width):
    for axis, dim in sides:
        count = lax.axis_size(axis)
        ends = count - 1
        head = lax.slice_in_dim(cells, 0, width, axis=dim)
        tail = lax.slice_in_dim(cells, cells.shape[dim] - width, cells.shape[dim], axis=dim)
        cells = jnp.concatenate(
            [
                lax.ppermute(tail, axis, [(i, (i + 1) % count) for i in range(ends)]),
                cells,
                lax.ppermute(head, axis, [((i + 1) % count, i) for i in range(ends)]),
            ],
            axis=dim,
        )
    return cells


def copy_for_each(shard, axis):
    peers = lax.axis_size(axis)
    return lax.all_to_all(
        jnp.broadcast_to(shard[None], (peers, *shard.shape)), axis, 0, 0, tiled=True
    )


def taken_together(shard, axis):
    return copy_for_each(shard, axis).astype(jnp.float32).sum(axis=0)


def joined_along(pieces, dim):
    shape = list(pieces.shape[1:])
    shape[dim] *= pieces.shape[0]
    return jnp.moveaxis(pieces, 0, dim).reshape(shape)


def gather_together(arrays, axis, dims):
    line = jnp.concatenate([a.reshape(-1) for a in arrays])
    lines, at, finished = (lax.all_gather(line, axis), 0, [])
    for a, dim in zip(arrays, dims):
        pieces = lines[:, at : at + a.size].reshape(-1, *a.shape)
        finished.append(joined_along(pieces, dim))
        at += a.size
    return tuple(finished)


def side_by_side(arrays, axis, dim, along):
    ends, at = ([], 0)
    for a in arrays[:-1]:
        at += a.shape[along]
        ends.append(at)
    both = jnp.concatenate(arrays, axis=along)
    return tuple(jnp.split(lax.all_gather(both, axis, axis=dim, tiled=True), ends, axis=along))


def cut_along(shard, dim, peers):
    before, after = (shard.shape[:dim], shard.shape[dim + 1 :])
    return jnp.moveaxis(shard.reshape(*before, peers, -1, *after), dim, 0)


def sum_at_owner(shard, axis, dim):
    peers = lax.axis_size(axis)
    pieces = lax.all_to_all(cut_along(shard, dim, peers), axis, 0, 0, tiled=True)
    return jnp.sum(pieces.astype(jnp.float32), axis=0)


def gather_weights(embed_weight, qkv_weight):
    _, feat, width = embed_weight.shape
    qkv_flat = qkv_weight.reshape(-1, width)
    extra = -qkv_flat.shape[0] % 16
    rows = jnp.concatenate(
        [embed_weight[0], qkv_flat, jnp.zeros((extra, width), qkv_flat.dtype)], axis=0
    )
    peers = lax.axis_size("blk")
    near = [list(range(start, start + 4)) for start in range(0, peers, 4)]
    far = [list(range(start, peers, 4)) for start in range(4)]
    gathered = lax.all_gather(rows, "blk", axis=0, tiled=True, axis_index_groups=near)
    half = gathered.shape[0] // 2
    odd = (lax.axis_index("blk") & 1) != 0
    mine = jnp.where(odd, gathered[half:], gathered[:half])
    own = lax.all_gather(mine, "blk", axis=0, tiled=True, axis_index_groups=far)
    other = lax.ppermute(own, "blk", [(i, i ^ 1) for i in range(peers)])
    own = own.reshape(len(far[0]), half, width)
    other = other.reshape(len(far[0]), half, width)
    gathered = jnp.concatenate(
        [jnp.where(odd, other, own), jnp.where(odd, own, other)], axis=1
    )
    gathered = gathered.reshape(peers, rows.shape[0], width)
    embed_rows = gathered[:, :feat, :]
    qkv_rows = gathered[:, feat : feat + qkv_flat.shape[0], :].reshape(peers, *qkv_weight.shape)
    qkv_rows = jnp.moveaxis(qkv_rows, 0, 1).reshape(
        qkv_weight.shape[0], peers * qkv_weight.shape[1], qkv_weight.shape[2]
    )
    return embed_rows, qkv_rows


def with_rim(volume):
    return padded_2(volume, (("zslab", 1), ("blk", 0)), DMAX)


def picked(cells, dim, step, rate, size):
    near = lax.slice_in_dim(cells, DMAX + step, DMAX + step + size, axis=dim)
    if step == 0:
        return near
    far = lax.slice_in_dim(cells, DMAX + 2 * step, DMAX + 2 * step + size, axis=dim)
    return jnp.where(rate == 1, near, far)


def shifted_y(values, step, rate):
    def by(amount):
        cells = values.shape[2]
        zeros = jnp.zeros_like(values[:, :, : abs(amount)])
        if amount > 0:
            return jnp.concatenate([values[:, :, amount:], zeros], axis=2)
        return jnp.concatenate([zeros, values[:, :, : cells + amount]], axis=2)

    if step == 0:
        return values
    return jnp.where(rate == 1, by(step), by(2 * step))


def apply_offsets(padded, weight, dilate, direction, dims_out):
    x_cells, z_cells, y_cells, channels = dims_out
    windows = []
    for offset_x in (-1, 0, 1):
        along_x = picked(padded, 0, direction * offset_x, dilate[0], x_cells)
        for offset_z in (-1, 0, 1):
            windows.append(picked(along_x, 1, direction * offset_z, dilate[2], z_cells))
    stacked = jnp.concatenate(windows, axis=3).reshape(x_cells * z_cells * y_cells, 9 * channels)
    taps = weight.reshape(3, 3, 3, channels, -1)
    summed = None
    for offset_y in (-1, 0, 1):
        rows = taps[:, offset_y + 1].reshape(9 * channels, -1)
        part = jnp.dot(stacked, rows, preferred_element_type=jnp.float32)
        part = shifted_y(part.reshape(x_cells, z_cells, y_cells, -1), direction * offset_y, dilate[1])
        summed = part if summed is None else summed + part
    return summed


def slab_total(term):
    return taken_together(term.astype(jnp.bfloat16), "zslab").astype(jnp.float32)


def local(field, fracture_mask, dilation, conv_weight, embed_weight, qkv_weight, out_grad):
    field = field.transpose(0, 2, 1, 3)
    fracture_mask = fracture_mask.transpose(0, 2, 1)
    x_cells, z_cells, y_cells, channels = field.shape
    gate_mask = fracture_mask.astype(jnp.float32)[..., None]
    hidden = field
    conv_outs = []
    for layer_num in range(LAYERS):
        conv_out = apply_offsets(
            with_rim(hidden), conv_weight[layer_num], dilation[layer_num], 1, field.shape
        )
        conv_outs.append(conv_out)
        hidden = (
            hidden.astype(jnp.float32) + gate_mask * (conv_out * jax.nn.sigmoid(conv_out))
        ).astype(jnp.bfloat16)
    slab_view = lax.all_to_all(hidden, "zslab", split_axis=0, concat_axis=1, tiled=True)
    x_local, z_total = (slab_view.shape[0], slab_view.shape[1])
    y_blocks, z_blocks = (y_cells // PY, z_total // PZ)
    patches = slab_view.reshape(x_local, z_blocks, PZ, y_blocks, PY, channels).transpose(
        3, 1, 0, 4, 2, 5
    )
    patches = patches.reshape(y_blocks * z_blocks, x_local, PY * PZ * channels)
    embed_rows, qkv_rows = gather_weights(embed_weight, qkv_weight)
    patches = patches.reshape(patches.shape[0], embed_rows.shape[0], embed_rows.shape[1])
    partial_value = jnp.einsum(
        "tbf,bfd->td", patches, embed_rows, preferred_element_type=jnp.float32
    )
    tokens = slab_total(partial_value).astype(jnp.bfloat16)
    projected = jnp.einsum(
        "td,sde->ste", tokens, qkv_rows, preferred_element_type=jnp.float32
    ).astype(jnp.bfloat16)
    key_rows, value_rows = jnp.split(
        joined_along(copy_for_each(jnp.concatenate([projected[1], projected[2]], axis=1), "blk"), 0),
        2,
        axis=1,
    )
    tok_rows = tokens.shape[0]
    head_cols = projected.shape[2]
    heads_here = head_cols // HD
    inv_root = HD ** (-0.5)
    queries = projected[0].reshape(tok_rows, heads_here, HD)
    key_all = key_rows.reshape(-1, heads_here, HD)
    value_all = value_rows.reshape(-1, heads_here, HD)
    grad_out = out_grad.reshape(tok_rows, heads_here, HD)
    scores = (
        jnp.einsum("qhd,khd->hqk", queries, key_all, preferred_element_type=jnp.float32) * inv_root
    )
    top_score = jnp.max(scores, axis=2, keepdims=True)
    expo = jnp.exp(scores - top_score)
    total = jnp.sum(expo, axis=2, keepdims=True)
    probs = expo / total
    probs_b = probs.astype(jnp.bfloat16)
    attended = jnp.einsum("hqk,khd->qhd", probs_b, value_all, preferred_element_type=jnp.float32)
    row_delta = jnp.sum(grad_out.astype(jnp.float32) * attended, axis=2).T[:, :, None]
    score_grad = jnp.einsum("qhd,khd->hqk", grad_out, value_all, preferred_element_type=jnp.float32)
    dscore = (probs * (score_grad - row_delta) * inv_root).astype(jnp.bfloat16)
    grad_query = jnp.einsum("hqk,khd->qhd", dscore, key_all, preferred_element_type=jnp.float32)
    grad_query = grad_query.astype(jnp.bfloat16).reshape(tok_rows, head_cols)
    key_term = jnp.einsum("hqk,qhd->khd", dscore, queries, preferred_element_type=jnp.float32)
    value_term = jnp.einsum("hqk,qhd->khd", probs_b, grad_out, preferred_element_type=jnp.float32)
    key_value_grad = sum_at_owner(
        jnp.concatenate(
            [
                key_term.reshape(tok_rows * lax.axis_size("blk"), head_cols),
                value_term.reshape(tok_rows * lax.axis_size("blk"), head_cols),
            ],
            axis=1,
        ).astype(jnp.bfloat16),
        "blk",
        0,
    ).astype(jnp.bfloat16)
    grad_key = key_value_grad[:, :head_cols]
    grad_value = key_value_grad[:, head_cols:]
    stacked_grads = jnp.stack([grad_query, grad_key, grad_value])
    partial_grad = jnp.einsum(
        "ste,sde->td", stacked_grads, qkv_rows, preferred_element_type=jnp.float32
    )
    grad_tokens = slab_total(partial_grad).astype(jnp.bfloat16)
    patch_grad = jnp.einsum(
        "td,bfd->tbf", grad_tokens, embed_rows, preferred_element_type=jnp.float32
    ).astype(jnp.bfloat16)
    grid_grad = patch_grad.reshape(y_blocks, z_blocks, x_local, PY, PZ, channels).transpose(
        2, 1, 4, 0, 3, 5
    )
    grid_grad = grid_grad.reshape(x_local, z_total, y_cells, channels)
    grid_grad = lax.all_to_all(grid_grad, "zslab", split_axis=1, concat_axis=0, tiled=True)
    for layer_num in reversed(range(LAYERS)):
        conv_out = conv_outs[layer_num]
        sigma = jax.nn.sigmoid(conv_out)
        slope_grad = (
            gate_mask * sigma * (1.0 + conv_out * (1.0 - sigma)) * grid_grad.astype(jnp.float32)
        ).astype(jnp.bfloat16)
        flipped = (
            conv_weight[layer_num]
            .reshape(27, channels, channels)
            .transpose(0, 2, 1)
            .reshape(27 * channels, channels)
        )
        backward = apply_offsets(
            with_rim(slope_grad), flipped, dilation[layer_num], -1, field.shape
        )
        grid_grad = (grid_grad.astype(jnp.float32) + backward).astype(jnp.bfloat16)
    return grid_grad.transpose(0, 2, 1, 3)


def solution(mesh):
    return jax.shard_map(
        local,
        mesh=mesh,
        in_specs=(
            P("blk", None, "zslab", None),
            P("blk", None, "zslab"),
            P(),
            P(),
            P("zslab", "blk", None),
            P(None, "blk", "zslab"),
            P("blk", "zslab"),
        ),
        out_specs=P("blk", None, "zslab", None),
        check_vma=False,
    )
```

```python
import jax
import jax.numpy as jnp
from jax import lax
from jax.sharding import PartitionSpec as P

HD = 128
PY = 8
PZ = 2
LAYERS = 2
DMAX = 2


def padded_2(cells, sides, width):
    for axis, dim in sides:
        count = lax.axis_size(axis)
        ends = count - 1
        head = lax.slice_in_dim(cells, 0, width, axis=dim)
        tail = lax.slice_in_dim(cells, cells.shape[dim] - width, cells.shape[dim], axis=dim)
        cells = jnp.concatenate(
            [
                lax.ppermute(tail, axis, [(i, (i + 1) % count) for i in range(ends)]),
                cells,
                lax.ppermute(head, axis, [((i + 1) % count, i) for i in range(ends)]),
            ],
            axis=dim,
        )
    return cells


def copy_for_each(shard, axis):
    peers = lax.axis_size(axis)
    return lax.all_to_all(
        jnp.broadcast_to(shard[None], (peers, *shard.shape)), axis, 0, 0, tiled=True
    )


def taken_together(shard, axis):
    return copy_for_each(shard, axis).astype(jnp.float32).sum(axis=0)


def joined_along(pieces, dim):
    shape = list(pieces.shape[1:])
    shape[dim] *= pieces.shape[0]
    return jnp.moveaxis(pieces, 0, dim).reshape(shape)


def gather_together(arrays, axis, dims):
    line = jnp.concatenate([a.reshape(-1) for a in arrays])
    lines, at, finished = (lax.all_gather(line, axis), 0, [])
    for a, dim in zip(arrays, dims):
        pieces = lines[:, at : at + a.size].reshape(-1, *a.shape)
        finished.append(joined_along(pieces, dim))
        at += a.size
    return tuple(finished)


def side_by_side(arrays, axis, dim, along):
    ends, at = ([], 0)
    for a in arrays[:-1]:
        at += a.shape[along]
        ends.append(at)
    both = jnp.concatenate(arrays, axis=along)
    return tuple(jnp.split(lax.all_gather(both, axis, axis=dim, tiled=True), ends, axis=along))


def cut_along(shard, dim, peers):
    before, after = (shard.shape[:dim], shard.shape[dim + 1 :])
    return jnp.moveaxis(shard.reshape(*before, peers, -1, *after), dim, 0)


def sum_at_owner(shard, axis, dim):
    peers = lax.axis_size(axis)
    pieces = lax.all_to_all(cut_along(shard, dim, peers), axis, 0, 0, tiled=True)
    return jnp.sum(pieces.astype(jnp.float32), axis=0)


def gathered_in_stages(rows, axis):
    peers = lax.axis_size(axis)
    near = [list(range(start, start + 4)) for start in range(0, peers, 4)]
    far = [list(range(start, peers, 4)) for start in range(4)]
    rows = lax.all_gather(rows, axis, axis=0, tiled=True, axis_index_groups=near)
    return lax.all_gather(rows, axis, axis=0, tiled=True, axis_index_groups=far)


def gather_weights(embed_weight, qkv_weight):
    _, feat, width = embed_weight.shape
    qkv_flat = qkv_weight.reshape(-1, width)
    extra = -qkv_flat.shape[0] % 16
    rows = jnp.concatenate(
        [embed_weight[0], qkv_flat, jnp.zeros((extra, width), qkv_flat.dtype)], axis=0
    )
    peers = lax.axis_size("blk")
    gathered = gathered_in_stages(rows, "blk")
    gathered = gathered.reshape(peers, rows.shape[0], width)
    embed_rows = gathered[:, :feat, :]
    qkv_rows = gathered[:, feat : feat + qkv_flat.shape[0], :].reshape(peers, *qkv_weight.shape)
    qkv_rows = jnp.moveaxis(qkv_rows, 0, 1).reshape(
        qkv_weight.shape[0], peers * qkv_weight.shape[1], qkv_weight.shape[2]
    )
    return embed_rows, qkv_rows


def with_rim(volume):
    return padded_2(volume, (("zslab", 1), ("blk", 0)), DMAX)


def picked(cells, dim, step, rate, size):
    near = lax.slice_in_dim(cells, DMAX + step, DMAX + step + size, axis=dim)
    if step == 0:
        return near
    far = lax.slice_in_dim(cells, DMAX + 2 * step, DMAX + 2 * step + size, axis=dim)
    return jnp.where(rate == 1, near, far)


def shifted_y(values, step, rate):
    def by(amount):
        cells = values.shape[2]
        zeros = jnp.zeros_like(values[:, :, : abs(amount)])
        if amount > 0:
            return jnp.concatenate([values[:, :, amount:], zeros], axis=2)
        return jnp.concatenate([zeros, values[:, :, : cells + amount]], axis=2)

    if step == 0:
        return values
    return jnp.where(rate == 1, by(step), by(2 * step))


def apply_offsets(padded, weight, dilate, direction, dims_out):
    x_cells, z_cells, y_cells, channels = dims_out
    windows = []
    for offset_x in (-1, 0, 1):
        along_x = picked(padded, 0, direction * offset_x, dilate[0], x_cells)
        for offset_z in (-1, 0, 1):
            windows.append(picked(along_x, 1, direction * offset_z, dilate[2], z_cells))
    stacked = jnp.concatenate(windows, axis=3).reshape(x_cells * z_cells * y_cells, 9 * channels)
    taps = weight.reshape(3, 3, 3, channels, -1)
    summed = None
    for offset_y in (-1, 0, 1):
        rows = taps[:, offset_y + 1].reshape(9 * channels, -1)
        part = jnp.dot(stacked, rows, preferred_element_type=jnp.float32)
        part = shifted_y(part.reshape(x_cells, z_cells, y_cells, -1), direction * offset_y, dilate[1])
        summed = part if summed is None else summed + part
    return summed


def slab_total(term):
    return taken_together(term.astype(jnp.bfloat16), "zslab").astype(jnp.float32)


def local(field, fracture_mask, dilation, conv_weight, embed_weight, qkv_weight, out_grad):
    field = field.transpose(0, 2, 1, 3)
    fracture_mask = fracture_mask.transpose(0, 2, 1)
    x_cells, z_cells, y_cells, channels = field.shape
    gate_mask = fracture_mask.astype(jnp.float32)[..., None]
    hidden = field
    conv_outs = []
    for layer_num in range(LAYERS):
        conv_out = apply_offsets(
            with_rim(hidden), conv_weight[layer_num], dilation[layer_num], 1, field.shape
        )
        conv_outs.append(conv_out)
        hidden = (
            hidden.astype(jnp.float32) + gate_mask * (conv_out * jax.nn.sigmoid(conv_out))
        ).astype(jnp.bfloat16)
    slab_view = lax.all_to_all(hidden, "zslab", split_axis=0, concat_axis=1, tiled=True)
    x_local, z_total = (slab_view.shape[0], slab_view.shape[1])
    y_blocks, z_blocks = (y_cells // PY, z_total // PZ)
    patches = slab_view.reshape(x_local, z_blocks, PZ, y_blocks, PY, channels).transpose(
        3, 1, 0, 4, 2, 5
    )
    patches = patches.reshape(y_blocks * z_blocks, x_local, PY * PZ * channels)
    embed_rows, qkv_rows = gather_weights(embed_weight, qkv_weight)
    patches = patches.reshape(patches.shape[0], embed_rows.shape[0], embed_rows.shape[1])
    partial_value = jnp.einsum(
        "tbf,bfd->td", patches, embed_rows, preferred_element_type=jnp.float32
    )
    tokens = slab_total(partial_value).astype(jnp.bfloat16)
    projected = jnp.einsum(
        "td,sde->ste", tokens, qkv_rows, preferred_element_type=jnp.float32
    ).astype(jnp.bfloat16)
    key_rows, value_rows = jnp.split(
        gathered_in_stages(jnp.concatenate([projected[1], projected[2]], axis=1), "blk"), 2, axis=1
    )
    tok_rows = tokens.shape[0]
    head_cols = projected.shape[2]
    heads_here = head_cols // HD
    inv_root = HD ** (-0.5)
    queries = projected[0].reshape(tok_rows, heads_here, HD)
    key_all = key_rows.reshape(-1, heads_here, HD)
    value_all = value_rows.reshape(-1, heads_here, HD)
    grad_out = out_grad.reshape(tok_rows, heads_here, HD)
    scores = (
        jnp.einsum("qhd,khd->hqk", queries, key_all, preferred_element_type=jnp.float32) * inv_root
    )
    top_score = jnp.max(scores, axis=2, keepdims=True)
    expo = jnp.exp(scores - top_score)
    total = jnp.sum(expo, axis=2, keepdims=True)
    probs = expo / total
    probs_b = probs.astype(jnp.bfloat16)
    attended = jnp.einsum("hqk,khd->qhd", probs_b, value_all, preferred_element_type=jnp.float32)
    row_delta = jnp.sum(grad_out.astype(jnp.float32) * attended, axis=2).T[:, :, None]
    score_grad = jnp.einsum("qhd,khd->hqk", grad_out, value_all, preferred_element_type=jnp.float32)
    dscore = (probs * (score_grad - row_delta) * inv_root).astype(jnp.bfloat16)
    grad_query = jnp.einsum("hqk,khd->qhd", dscore, key_all, preferred_element_type=jnp.float32)
    grad_query = grad_query.astype(jnp.bfloat16).reshape(tok_rows, head_cols)
    key_term = jnp.einsum("hqk,qhd->khd", dscore, queries, preferred_element_type=jnp.float32)
    value_term = jnp.einsum("hqk,qhd->khd", probs_b, grad_out, preferred_element_type=jnp.float32)
    key_value_grad = sum_at_owner(
        jnp.concatenate(
            [
                key_term.reshape(tok_rows * lax.axis_size("blk"), head_cols),
                value_term.reshape(tok_rows * lax.axis_size("blk"), head_cols),
            ],
            axis=1,
        ).astype(jnp.bfloat16),
        "blk",
        0,
    ).astype(jnp.bfloat16)
    grad_key = key_value_grad[:, :head_cols]
    grad_value = key_value_grad[:, head_cols:]
    stacked_grads = jnp.stack([grad_query, grad_key, grad_value])
    partial_grad = jnp.einsum(
        "ste,sde->td", stacked_grads, qkv_rows, preferred_element_type=jnp.float32
    )
    grad_tokens = slab_total(partial_grad).astype(jnp.bfloat16)
    patch_grad = jnp.einsum(
        "td,bfd->tbf", grad_tokens, embed_rows, preferred_element_type=jnp.float32
    ).astype(jnp.bfloat16)
    grid_grad = patch_grad.reshape(y_blocks, z_blocks, x_local, PY, PZ, channels).transpose(
        2, 1, 4, 0, 3, 5
    )
    grid_grad = grid_grad.reshape(x_local, z_total, y_cells, channels)
    grid_grad = lax.all_to_all(grid_grad, "zslab", split_axis=1, concat_axis=0, tiled=True)
    for layer_num in reversed(range(LAYERS)):
        conv_out = conv_outs[layer_num]
        sigma = jax.nn.sigmoid(conv_out)
        slope_grad = (
            gate_mask * sigma * (1.0 + conv_out * (1.0 - sigma)) * grid_grad.astype(jnp.float32)
        ).astype(jnp.bfloat16)
        flipped = (
            conv_weight[layer_num]
            .reshape(27, channels, channels)
            .transpose(0, 2, 1)
            .reshape(27 * channels, channels)
        )
        backward = apply_offsets(
            with_rim(slope_grad), flipped, dilation[layer_num], -1, field.shape
        )
        grid_grad = (grid_grad.astype(jnp.float32) + backward).astype(jnp.bfloat16)
    return grid_grad.transpose(0, 2, 1, 3)


def solution(mesh):
    return jax.shard_map(
        local,
        mesh=mesh,
        in_specs=(
            P("blk", None, "zslab", None),
            P("blk", None, "zslab"),
            P(),
            P(),
            P("zslab", "blk", None),
            P(None, "blk", "zslab"),
            P("blk", "zslab"),
        ),
        out_specs=P("blk", None, "zslab", None),
        check_vma=False,
    )
```

```python
import jax
import jax.numpy as jnp
from jax import lax
from jax.sharding import PartitionSpec as P

HD = 128
PY = 8
PZ = 2
LAYERS = 2
DMAX = 2


def padded_2(cells, sides, width):
    for axis, dim in sides:
        count = lax.axis_size(axis)
        ends = count - 1
        head = lax.slice_in_dim(cells, 0, width, axis=dim)
        tail = lax.slice_in_dim(cells, cells.shape[dim] - width, cells.shape[dim], axis=dim)
        cells = jnp.concatenate(
            [
                lax.ppermute(tail, axis, [(i, (i + 1) % count) for i in range(ends)]),
                cells,
                lax.ppermute(head, axis, [((i + 1) % count, i) for i in range(ends)]),
            ],
            axis=dim,
        )
    return cells


def copy_for_each(shard, axis):
    peers = lax.axis_size(axis)
    return lax.all_to_all(
        jnp.broadcast_to(shard[None], (peers, *shard.shape)), axis, 0, 0, tiled=True
    )


def taken_together(shard, axis):
    return copy_for_each(shard, axis).astype(jnp.float32).sum(axis=0)


def joined_along(pieces, dim):
    shape = list(pieces.shape[1:])
    shape[dim] *= pieces.shape[0]
    return jnp.moveaxis(pieces, 0, dim).reshape(shape)


def gather_together(arrays, axis, dims):
    line = jnp.concatenate([a.reshape(-1) for a in arrays])
    lines, at, finished = (lax.all_gather(line, axis), 0, [])
    for a, dim in zip(arrays, dims):
        pieces = lines[:, at : at + a.size].reshape(-1, *a.shape)
        finished.append(joined_along(pieces, dim))
        at += a.size
    return tuple(finished)


def side_by_side(arrays, axis, dim, along):
    ends, at = ([], 0)
    for a in arrays[:-1]:
        at += a.shape[along]
        ends.append(at)
    both = jnp.concatenate(arrays, axis=along)
    return tuple(jnp.split(lax.all_gather(both, axis, axis=dim, tiled=True), ends, axis=along))


def cut_along(shard, dim, peers):
    before, after = (shard.shape[:dim], shard.shape[dim + 1 :])
    return jnp.moveaxis(shard.reshape(*before, peers, -1, *after), dim, 0)


def sum_at_owner(shard, axis, dim):
    peers = lax.axis_size(axis)
    pieces = lax.all_to_all(cut_along(shard, dim, peers), axis, 0, 0, tiled=True)
    return jnp.sum(pieces.astype(jnp.float32), axis=0)


def gather_weights(embed_weight, qkv_weight):
    _, feat, width = embed_weight.shape
    qkv_flat = qkv_weight.reshape(-1, width)
    extra = -qkv_flat.shape[0] % 16
    rows = jnp.concatenate(
        [embed_weight[0], qkv_flat, jnp.zeros((extra, width), qkv_flat.dtype)], axis=0
    )
    peers = lax.axis_size("blk")
    near = [list(range(start, start + 4)) for start in range(0, peers, 4)]
    far = [list(range(start, peers, 4)) for start in range(4)]
    gathered = lax.all_gather(rows, "blk", axis=0, tiled=True, axis_index_groups=near)
    gathered = lax.all_gather(gathered, "blk", axis=0, tiled=True, axis_index_groups=far)
    gathered = gathered.reshape(peers, rows.shape[0], width)
    embed_rows = gathered[:, :feat, :]
    qkv_rows = gathered[:, feat : feat + qkv_flat.shape[0], :].reshape(peers, *qkv_weight.shape)
    qkv_rows = jnp.moveaxis(qkv_rows, 0, 1).reshape(
        qkv_weight.shape[0], peers * qkv_weight.shape[1], qkv_weight.shape[2]
    )
    return embed_rows, qkv_rows


def with_rim(volume):
    return padded_2(volume, (("zslab", 1), ("blk", 0)), DMAX)


def picked(cells, dim, step, rate, size):
    near = lax.slice_in_dim(cells, DMAX + step, DMAX + step + size, axis=dim)
    if step == 0:
        return near
    far = lax.slice_in_dim(cells, DMAX + 2 * step, DMAX + 2 * step + size, axis=dim)
    return jnp.where(rate == 1, near, far)


def shifted_y(values, step, rate):
    def by(amount):
        cells = values.shape[2]
        zeros = jnp.zeros_like(values[:, :, : abs(amount)])
        if amount > 0:
            return jnp.concatenate([values[:, :, amount:], zeros], axis=2)
        return jnp.concatenate([zeros, values[:, :, : cells + amount]], axis=2)

    if step == 0:
        return values
    return jnp.where(rate == 1, by(step), by(2 * step))


def apply_offsets(padded, weight, dilate, direction, dims_out):
    x_cells, z_cells, y_cells, channels = dims_out
    windows = []
    for offset_x in (-1, 0, 1):
        along_x = picked(padded, 0, direction * offset_x, dilate[0], x_cells)
        for offset_z in (-1, 0, 1):
            windows.append(picked(along_x, 1, direction * offset_z, dilate[2], z_cells))
    stacked = jnp.concatenate(windows, axis=3).reshape(x_cells * z_cells * y_cells, 9 * channels)
    taps = weight.reshape(3, 3, 3, channels, -1)
    summed = None
    for offset_y in (-1, 0, 1):
        rows = taps[:, offset_y + 1].reshape(9 * channels, -1)
        part = jnp.dot(stacked, rows, preferred_element_type=jnp.float32)
        part = shifted_y(part.reshape(x_cells, z_cells, y_cells, -1), direction * offset_y, dilate[1])
        summed = part if summed is None else summed + part
    return summed


def slab_total(term):
    return taken_together(term.astype(jnp.bfloat16), "zslab").astype(jnp.float32)


def local(field, fracture_mask, dilation, conv_weight, embed_weight, qkv_weight, out_grad):
    field = field.transpose(0, 2, 1, 3)
    fracture_mask = fracture_mask.transpose(0, 2, 1)
    x_cells, z_cells, y_cells, channels = field.shape
    gate_mask = fracture_mask.astype(jnp.float32)[..., None]
    hidden = field
    conv_outs = []
    for layer_num in range(LAYERS):
        conv_out = apply_offsets(
            with_rim(hidden), conv_weight[layer_num], dilation[layer_num], 1, field.shape
        )
        conv_outs.append(conv_out)
        hidden = (
            hidden.astype(jnp.float32) + gate_mask * (conv_out * jax.nn.sigmoid(conv_out))
        ).astype(jnp.bfloat16)
    slab_view = lax.all_to_all(hidden, "zslab", split_axis=0, concat_axis=1, tiled=True)
    x_local, z_total = (slab_view.shape[0], slab_view.shape[1])
    y_blocks, z_blocks = (y_cells // PY, z_total // PZ)
    patches = slab_view.reshape(x_local, z_blocks, PZ, y_blocks, PY, channels).transpose(
        3, 1, 0, 4, 2, 5
    )
    patches = patches.reshape(y_blocks * z_blocks, x_local, PY * PZ * channels)
    embed_rows, qkv_rows = gather_weights(embed_weight, qkv_weight)
    patches = patches.reshape(patches.shape[0], embed_rows.shape[0], embed_rows.shape[1])
    partial_value = jnp.einsum(
        "tbf,bfd->td", patches, embed_rows, preferred_element_type=jnp.float32
    )
    tokens = slab_total(partial_value).astype(jnp.bfloat16)
    projected = jnp.einsum(
        "td,sde->ste", tokens, qkv_rows, preferred_element_type=jnp.float32
    ).astype(jnp.bfloat16)
    key_rows, value_rows = jnp.split(
        joined_along(copy_for_each(jnp.concatenate([projected[1], projected[2]], axis=1), "blk"), 0),
        2,
        axis=1,
    )
    tok_rows = tokens.shape[0]
    head_cols = projected.shape[2]
    heads_here = head_cols // HD
    inv_root = HD ** (-0.5)
    queries = projected[0].reshape(tok_rows, heads_here, HD)
    key_all = key_rows.reshape(-1, heads_here, HD)
    value_all = value_rows.reshape(-1, heads_here, HD)
    grad_out = out_grad.reshape(tok_rows, heads_here, HD)
    scores = (
        jnp.einsum("qhd,khd->hqk", queries, key_all, preferred_element_type=jnp.float32) * inv_root
    )
    top_score = jnp.max(scores, axis=2, keepdims=True)
    expo = jnp.exp(scores - top_score)
    total = jnp.sum(expo, axis=2, keepdims=True)
    probs = expo / total
    probs_b = probs.astype(jnp.bfloat16)
    attended = jnp.einsum("hqk,khd->qhd", probs_b, value_all, preferred_element_type=jnp.float32)
    row_delta = jnp.sum(grad_out.astype(jnp.float32) * attended, axis=2).T[:, :, None]
    score_grad = jnp.einsum("qhd,khd->hqk", grad_out, value_all, preferred_element_type=jnp.float32)
    dscore = (probs * (score_grad - row_delta) * inv_root).astype(jnp.bfloat16)
    grad_query = jnp.einsum("hqk,khd->qhd", dscore, key_all, preferred_element_type=jnp.float32)
    grad_query = grad_query.astype(jnp.bfloat16).reshape(tok_rows, head_cols)
    key_term = jnp.einsum("hqk,qhd->khd", dscore, queries, preferred_element_type=jnp.float32)
    value_term = jnp.einsum("hqk,qhd->khd", probs_b, grad_out, preferred_element_type=jnp.float32)
    key_value_grad = sum_at_owner(
        jnp.concatenate(
            [
                key_term.reshape(tok_rows * lax.axis_size("blk"), head_cols),
                value_term.reshape(tok_rows * lax.axis_size("blk"), head_cols),
            ],
            axis=1,
        ).astype(jnp.bfloat16),
        "blk",
        0,
    ).astype(jnp.bfloat16)
    grad_key = key_value_grad[:, :head_cols]
    grad_value = key_value_grad[:, head_cols:]
    stacked_grads = jnp.stack([grad_query, grad_key, grad_value])
    partial_grad = jnp.einsum(
        "ste,sde->td", stacked_grads, qkv_rows, preferred_element_type=jnp.float32
    )
    grad_tokens = slab_total(partial_grad).astype(jnp.bfloat16)
    patch_grad = jnp.einsum(
        "td,bfd->tbf", grad_tokens, embed_rows, preferred_element_type=jnp.float32
    ).astype(jnp.bfloat16)
    grid_grad = patch_grad.reshape(y_blocks, z_blocks, x_local, PY, PZ, channels).transpose(
        2, 1, 4, 0, 3, 5
    )
    grid_grad = grid_grad.reshape(x_local, z_total, y_cells, channels)
    slabs = lax.axis_size("zslab")
    grid_grad = jnp.pad(grid_grad, ((0, 0), (DMAX, DMAX), (0, 0), (0, 0)))
    grid_grad = jnp.stack(
        [grid_grad[:, k * z_cells : (k + 1) * z_cells + 2 * DMAX] for k in range(slabs)]
    )
    wide_grad = lax.all_to_all(grid_grad, "zslab", split_axis=0, concat_axis=1, tiled=True)
    wide_grad = wide_grad.reshape(x_cells, z_cells + 2 * DMAX, y_cells, channels)
    grid_grad = wide_grad[:, DMAX : DMAX + z_cells]
    for layer_num in reversed(range(LAYERS)):
        conv_out = conv_outs[layer_num]
        sigma = jax.nn.sigmoid(conv_out)
        if layer_num == LAYERS - 1:
            slope = padded_2(
                gate_mask * sigma * (1.0 + conv_out * (1.0 - sigma)), (("zslab", 1),), DMAX
            )
            slope_grad = (slope * wide_grad.astype(jnp.float32)).astype(jnp.bfloat16)
            padded = padded_2(slope_grad, (("blk", 0),), DMAX)
        else:
            slope_grad = (
                gate_mask * sigma * (1.0 + conv_out * (1.0 - sigma)) * grid_grad.astype(jnp.float32)
            ).astype(jnp.bfloat16)
            padded = with_rim(slope_grad)
        flipped = (
            conv_weight[layer_num]
            .reshape(27, channels, channels)
            .transpose(0, 2, 1)
            .reshape(27 * channels, channels)
        )
        backward = apply_offsets(padded, flipped, dilation[layer_num], -1, field.shape)
        grid_grad = (grid_grad.astype(jnp.float32) + backward).astype(jnp.bfloat16)
    return grid_grad.transpose(0, 2, 1, 3)


def solution(mesh):
    return jax.shard_map(
        local,
        mesh=mesh,
        in_specs=(
            P("blk", None, "zslab", None),
            P("blk", None, "zslab"),
            P(),
            P(),
            P("zslab", "blk", None),
            P(None, "blk", "zslab"),
            P("blk", "zslab"),
        ),
        out_specs=P("blk", None, "zslab", None),
        check_vma=False,
    )
```

```python
import jax
import jax.numpy as jnp
from jax import lax
from jax.sharding import PartitionSpec as P

HD = 128
PY = 8
PZ = 2
LAYERS = 2
DMAX = 2


def padded_2(cells, sides, width):
    for axis, dim in sides:
        count = lax.axis_size(axis)
        ends = count - 1
        head = lax.slice_in_dim(cells, 0, width, axis=dim)
        tail = lax.slice_in_dim(cells, cells.shape[dim] - width, cells.shape[dim], axis=dim)
        cells = jnp.concatenate(
            [
                lax.ppermute(tail, axis, [(i, (i + 1) % count) for i in range(ends)]),
                cells,
                lax.ppermute(head, axis, [((i + 1) % count, i) for i in range(ends)]),
            ],
            axis=dim,
        )
    return cells


def copy_for_each(shard, axis):
    peers = lax.axis_size(axis)
    return lax.all_to_all(
        jnp.broadcast_to(shard[None], (peers, *shard.shape)), axis, 0, 0, tiled=True
    )


def taken_together(shard, axis):
    return copy_for_each(shard, axis).astype(jnp.float32).sum(axis=0)


def joined_along(pieces, dim):
    shape = list(pieces.shape[1:])
    shape[dim] *= pieces.shape[0]
    return jnp.moveaxis(pieces, 0, dim).reshape(shape)


def gather_together(arrays, axis, dims):
    line = jnp.concatenate([a.reshape(-1) for a in arrays])
    lines, at, finished = (lax.all_gather(line, axis), 0, [])
    for a, dim in zip(arrays, dims):
        pieces = lines[:, at : at + a.size].reshape(-1, *a.shape)
        finished.append(joined_along(pieces, dim))
        at += a.size
    return tuple(finished)


def side_by_side(arrays, axis, dim, along):
    ends, at = ([], 0)
    for a in arrays[:-1]:
        at += a.shape[along]
        ends.append(at)
    both = jnp.concatenate(arrays, axis=along)
    return tuple(jnp.split(lax.all_gather(both, axis, axis=dim, tiled=True), ends, axis=along))


def cut_along(shard, dim, peers):
    before, after = (shard.shape[:dim], shard.shape[dim + 1 :])
    return jnp.moveaxis(shard.reshape(*before, peers, -1, *after), dim, 0)


def sum_at_owner(shard, axis, dim):
    peers = lax.axis_size(axis)
    pieces = lax.all_to_all(cut_along(shard, dim, peers), axis, 0, 0, tiled=True)
    return jnp.sum(pieces.astype(jnp.float32), axis=0)


def gather_weights(embed_weight, qkv_weight):
    _, feat, width = embed_weight.shape
    qkv_flat = qkv_weight.reshape(-1, width)
    extra = -qkv_flat.shape[0] % 16
    rows = jnp.concatenate(
        [embed_weight[0], qkv_flat, jnp.zeros((extra, width), qkv_flat.dtype)], axis=0
    )
    peers = lax.axis_size("blk")
    near = [list(range(start, start + 4)) for start in range(0, peers, 4)]
    far = [list(range(start, peers, 4)) for start in range(4)]
    gathered = lax.all_gather(rows, "blk", axis=0, tiled=True, axis_index_groups=near)
    gathered = lax.all_gather(gathered, "blk", axis=0, tiled=True, axis_index_groups=far)
    gathered = gathered.reshape(peers, rows.shape[0], width)
    embed_rows = gathered[:, :feat, :]
    qkv_rows = gathered[:, feat : feat + qkv_flat.shape[0], :].reshape(peers, *qkv_weight.shape)
    qkv_rows = jnp.moveaxis(qkv_rows, 0, 1).reshape(
        qkv_weight.shape[0], peers * qkv_weight.shape[1], qkv_weight.shape[2]
    )
    return embed_rows, qkv_rows


def with_rim(volume):
    return padded_2(volume, (("zslab", 1), ("blk", 0)), DMAX)


def picked(cells, dim, step, rate, size):
    near = lax.slice_in_dim(cells, DMAX + step, DMAX + step + size, axis=dim)
    if step == 0:
        return near
    far = lax.slice_in_dim(cells, DMAX + 2 * step, DMAX + 2 * step + size, axis=dim)
    return jnp.where(rate == 1, near, far)


def shifted_y(values, step, rate):
    def by(amount):
        cells = values.shape[2]
        zeros = jnp.zeros_like(values[:, :, : abs(amount)])
        if amount > 0:
            return jnp.concatenate([values[:, :, amount:], zeros], axis=2)
        return jnp.concatenate([zeros, values[:, :, : cells + amount]], axis=2)

    if step == 0:
        return values
    return jnp.where(rate == 1, by(step), by(2 * step))


def apply_offsets(padded, weight, dilate, direction, dims_out):
    x_cells, z_cells, y_cells, channels = dims_out
    windows = []
    for offset_x in (-1, 0, 1):
        along_x = picked(padded, 0, direction * offset_x, dilate[0], x_cells)
        for offset_z in (-1, 0, 1):
            windows.append(picked(along_x, 1, direction * offset_z, dilate[2], z_cells))
    stacked = jnp.concatenate(windows, axis=3).reshape(x_cells * z_cells * y_cells, 9 * channels)
    taps = weight.reshape(3, 3, 3, channels, -1)
    summed = None
    for offset_y in (-1, 0, 1):
        rows = taps[:, offset_y + 1].reshape(9 * channels, -1)
        part = jnp.dot(stacked, rows, preferred_element_type=jnp.float32)
        part = shifted_y(part.reshape(x_cells, z_cells, y_cells, -1), direction * offset_y, dilate[1])
        summed = part if summed is None else summed + part
    return summed


def slab_total(term):
    return taken_together(term.astype(jnp.bfloat16), "zslab").astype(jnp.float32)


def local(field, fracture_mask, dilation, conv_weight, embed_weight, qkv_weight, out_grad):
    field = field.transpose(0, 2, 1, 3)
    fracture_mask = fracture_mask.transpose(0, 2, 1)
    x_cells, z_cells, y_cells, channels = field.shape
    gate_mask = fracture_mask.astype(jnp.float32)[..., None]
    hidden = field
    conv_outs = []
    for layer_num in range(LAYERS):
        conv_out = apply_offsets(
            with_rim(hidden), conv_weight[layer_num], dilation[layer_num], 1, field.shape
        )
        conv_outs.append(conv_out)
        hidden = (
            hidden.astype(jnp.float32) + gate_mask * (conv_out * jax.nn.sigmoid(conv_out))
        ).astype(jnp.bfloat16)
    sigma = jax.nn.sigmoid(conv_outs[-1])
    slope = padded_2(
        gate_mask * sigma * (1.0 + conv_outs[-1] * (1.0 - sigma)), (("zslab", 1),), DMAX
    )
    hidden, slope = lax.optimization_barrier((hidden, slope))
    slab_view = lax.all_to_all(hidden, "zslab", split_axis=0, concat_axis=1, tiled=True)
    x_local, z_total = (slab_view.shape[0], slab_view.shape[1])
    y_blocks, z_blocks = (y_cells // PY, z_total // PZ)
    patches = slab_view.reshape(x_local, z_blocks, PZ, y_blocks, PY, channels).transpose(
        3, 1, 0, 4, 2, 5
    )
    patches = patches.reshape(y_blocks * z_blocks, x_local, PY * PZ * channels)
    embed_rows, qkv_rows = gather_weights(embed_weight, qkv_weight)
    patches = patches.reshape(patches.shape[0], embed_rows.shape[0], embed_rows.shape[1])
    partial_value = jnp.einsum(
        "tbf,bfd->td", patches, embed_rows, preferred_element_type=jnp.float32
    )
    tokens = slab_total(partial_value).astype(jnp.bfloat16)
    projected = jnp.einsum(
        "td,sde->ste", tokens, qkv_rows, preferred_element_type=jnp.float32
    ).astype(jnp.bfloat16)
    key_rows, value_rows = jnp.split(
        joined_along(copy_for_each(jnp.concatenate([projected[1], projected[2]], axis=1), "blk"), 0),
        2,
        axis=1,
    )
    tok_rows = tokens.shape[0]
    head_cols = projected.shape[2]
    heads_here = head_cols // HD
    inv_root = HD ** (-0.5)
    queries = projected[0].reshape(tok_rows, heads_here, HD)
    key_all = key_rows.reshape(-1, heads_here, HD)
    value_all = value_rows.reshape(-1, heads_here, HD)
    grad_out = out_grad.reshape(tok_rows, heads_here, HD)
    scores = (
        jnp.einsum("qhd,khd->hqk", queries, key_all, preferred_element_type=jnp.float32) * inv_root
    )
    top_score = jnp.max(scores, axis=2, keepdims=True)
    expo = jnp.exp(scores - top_score)
    total = jnp.sum(expo, axis=2, keepdims=True)
    probs = expo / total
    probs_b = probs.astype(jnp.bfloat16)
    attended = jnp.einsum("hqk,khd->qhd", probs_b, value_all, preferred_element_type=jnp.float32)
    row_delta = jnp.sum(grad_out.astype(jnp.float32) * attended, axis=2).T[:, :, None]
    score_grad = jnp.einsum("qhd,khd->hqk", grad_out, value_all, preferred_element_type=jnp.float32)
    dscore = (probs * (score_grad - row_delta) * inv_root).astype(jnp.bfloat16)
    grad_query = jnp.einsum("hqk,khd->qhd", dscore, key_all, preferred_element_type=jnp.float32)
    grad_query = grad_query.astype(jnp.bfloat16).reshape(tok_rows, head_cols)
    key_term = jnp.einsum("hqk,qhd->khd", dscore, queries, preferred_element_type=jnp.float32)
    value_term = jnp.einsum("hqk,qhd->khd", probs_b, grad_out, preferred_element_type=jnp.float32)
    key_value_grad = sum_at_owner(
        jnp.concatenate(
            [
                key_term.reshape(tok_rows * lax.axis_size("blk"), head_cols),
                value_term.reshape(tok_rows * lax.axis_size("blk"), head_cols),
            ],
            axis=1,
        ).astype(jnp.bfloat16),
        "blk",
        0,
    ).astype(jnp.bfloat16)
    grad_key = key_value_grad[:, :head_cols]
    grad_value = key_value_grad[:, head_cols:]
    stacked_grads = jnp.stack([grad_query, grad_key, grad_value])
    partial_grad = jnp.einsum(
        "ste,sde->td", stacked_grads, qkv_rows, preferred_element_type=jnp.float32
    )
    grad_tokens = slab_total(partial_grad).astype(jnp.bfloat16)
    patch_grad = jnp.einsum(
        "td,bfd->tbf", grad_tokens, embed_rows, preferred_element_type=jnp.float32
    ).astype(jnp.bfloat16)
    grid_grad = patch_grad.reshape(y_blocks, z_blocks, x_local, PY, PZ, channels).transpose(
        2, 1, 4, 0, 3, 5
    )
    grid_grad = grid_grad.reshape(x_local, z_total, y_cells, channels)
    slabs = lax.axis_size("zslab")
    grid_grad = jnp.pad(grid_grad, ((0, 0), (DMAX, DMAX), (0, 0), (0, 0)))
    grid_grad = jnp.stack(
        [grid_grad[:, k * z_cells : (k + 1) * z_cells + 2 * DMAX] for k in range(slabs)]
    )
    wide_grad = lax.all_to_all(grid_grad, "zslab", split_axis=0, concat_axis=1, tiled=True)
    wide_grad = wide_grad.reshape(x_cells, z_cells + 2 * DMAX, y_cells, channels)
    grid_grad = wide_grad[:, DMAX : DMAX + z_cells]
    for layer_num in reversed(range(LAYERS)):
        conv_out = conv_outs[layer_num]
        sigma = jax.nn.sigmoid(conv_out)
        if layer_num == LAYERS - 1:
            slope_grad = (slope * wide_grad.astype(jnp.float32)).astype(jnp.bfloat16)
            padded = padded_2(slope_grad, (("blk", 0),), DMAX)
        else:
            slope_grad = (
                gate_mask * sigma * (1.0 + conv_out * (1.0 - sigma)) * grid_grad.astype(jnp.float32)
            ).astype(jnp.bfloat16)
            padded = with_rim(slope_grad)
        flipped = (
            conv_weight[layer_num]
            .reshape(27, channels, channels)
            .transpose(0, 2, 1)
            .reshape(27 * channels, channels)
        )
        backward = apply_offsets(padded, flipped, dilation[layer_num], -1, field.shape)
        grid_grad = (grid_grad.astype(jnp.float32) + backward).astype(jnp.bfloat16)
    return grid_grad.transpose(0, 2, 1, 3)


def solution(mesh):
    return jax.shard_map(
        local,
        mesh=mesh,
        in_specs=(
            P("blk", None, "zslab", None),
            P("blk", None, "zslab"),
            P(),
            P(),
            P("zslab", "blk", None),
            P(None, "blk", "zslab"),
            P("blk", "zslab"),
        ),
        out_specs=P("blk", None, "zslab", None),
        check_vma=False,
    )
```

```python
import jax
import jax.numpy as jnp
from jax import lax
from jax.sharding import PartitionSpec as P

HD = 128
PY = 8
PZ = 2
LAYERS = 2
DMAX = 2


def padded_2(cells, sides, width):
    for axis, dim in sides:
        count = lax.axis_size(axis)
        ends = count - 1
        head = lax.slice_in_dim(cells, 0, width, axis=dim)
        tail = lax.slice_in_dim(cells, cells.shape[dim] - width, cells.shape[dim], axis=dim)
        cells = jnp.concatenate(
            [
                lax.ppermute(tail, axis, [(i, (i + 1) % count) for i in range(ends)]),
                cells,
                lax.ppermute(head, axis, [((i + 1) % count, i) for i in range(ends)]),
            ],
            axis=dim,
        )
    return cells


def copy_for_each(shard, axis):
    peers = lax.axis_size(axis)
    return lax.all_to_all(
        jnp.broadcast_to(shard[None], (peers, *shard.shape)), axis, 0, 0, tiled=True
    )


def taken_together(shard, axis):
    return copy_for_each(shard, axis).astype(jnp.float32).sum(axis=0)


def joined_along(pieces, dim):
    shape = list(pieces.shape[1:])
    shape[dim] *= pieces.shape[0]
    return jnp.moveaxis(pieces, 0, dim).reshape(shape)


def gather_together(arrays, axis, dims):
    line = jnp.concatenate([a.reshape(-1) for a in arrays])
    lines, at, finished = (lax.all_gather(line, axis), 0, [])
    for a, dim in zip(arrays, dims):
        pieces = lines[:, at : at + a.size].reshape(-1, *a.shape)
        finished.append(joined_along(pieces, dim))
        at += a.size
    return tuple(finished)


def side_by_side(arrays, axis, dim, along):
    ends, at = ([], 0)
    for a in arrays[:-1]:
        at += a.shape[along]
        ends.append(at)
    both = jnp.concatenate(arrays, axis=along)
    return tuple(jnp.split(lax.all_gather(both, axis, axis=dim, tiled=True), ends, axis=along))


def cut_along(shard, dim, peers):
    before, after = (shard.shape[:dim], shard.shape[dim + 1 :])
    return jnp.moveaxis(shard.reshape(*before, peers, -1, *after), dim, 0)


def sum_at_owner(shard, axis, dim):
    peers = lax.axis_size(axis)
    pieces = lax.all_to_all(cut_along(shard, dim, peers), axis, 0, 0, tiled=True)
    return jnp.sum(pieces.astype(jnp.float32), axis=0)


def gather_weights(embed_weight, qkv_weight):
    _, feat, width = embed_weight.shape
    qkv_flat = qkv_weight.reshape(-1, width)
    extra = -qkv_flat.shape[0] % 16
    rows = jnp.concatenate(
        [embed_weight[0], qkv_flat, jnp.zeros((extra, width), qkv_flat.dtype)], axis=0
    )
    peers = lax.axis_size("blk")
    near = [list(range(start, start + 4)) for start in range(0, peers, 4)]
    far = [list(range(start, peers, 4)) for start in range(4)]
    gathered = lax.all_gather(rows, "blk", axis=0, tiled=True, axis_index_groups=near)
    gathered = lax.all_gather(gathered, "blk", axis=0, tiled=True, axis_index_groups=far)
    gathered = gathered.reshape(peers, rows.shape[0], width)
    embed_rows = gathered[:, :feat, :]
    qkv_rows = gathered[:, feat : feat + qkv_flat.shape[0], :].reshape(peers, *qkv_weight.shape)
    qkv_rows = jnp.moveaxis(qkv_rows, 0, 1).reshape(
        qkv_weight.shape[0], peers * qkv_weight.shape[1], qkv_weight.shape[2]
    )
    return embed_rows, qkv_rows


def with_rim(volume):
    return padded_2(volume, (("zslab", 1), ("blk", 0)), DMAX)


def picked(cells, dim, step, rate, size):
    near = lax.slice_in_dim(cells, DMAX + step, DMAX + step + size, axis=dim)
    if step == 0:
        return near
    far = lax.slice_in_dim(cells, DMAX + 2 * step, DMAX + 2 * step + size, axis=dim)
    return jnp.where(rate == 1, near, far)


def shifted_y(values, step, rate):
    def by(amount):
        cells = values.shape[2]
        zeros = jnp.zeros_like(values[:, :, : abs(amount)])
        if amount > 0:
            return jnp.concatenate([values[:, :, amount:], zeros], axis=2)
        return jnp.concatenate([zeros, values[:, :, : cells + amount]], axis=2)

    if step == 0:
        return values
    return jnp.where(rate == 1, by(step), by(2 * step))


def apply_offsets(padded, weight, dilate, direction, dims_out):
    x_cells, z_cells, y_cells, channels = dims_out
    windows = []
    for offset_x in (-1, 0, 1):
        along_x = picked(padded, 0, direction * offset_x, dilate[0], x_cells)
        for offset_z in (-1, 0, 1):
            windows.append(picked(along_x, 1, direction * offset_z, dilate[2], z_cells))
    stacked = jnp.concatenate(windows, axis=3).reshape(x_cells * z_cells * y_cells, 9 * channels)
    taps = weight.reshape(3, 3, 3, channels, -1)
    summed = None
    for offset_y in (-1, 0, 1):
        rows = taps[:, offset_y + 1].reshape(9 * channels, -1)
        part = jnp.dot(stacked, rows, preferred_element_type=jnp.float32)
        part = shifted_y(part.reshape(x_cells, z_cells, y_cells, -1), direction * offset_y, dilate[1])
        summed = part if summed is None else summed + part
    return summed


def slab_total(term):
    return taken_together(term.astype(jnp.bfloat16), "zslab").astype(jnp.float32)


def local(field, fracture_mask, dilation, conv_weight, embed_weight, qkv_weight, out_grad):
    field = field.transpose(0, 2, 1, 3)
    fracture_mask = fracture_mask.transpose(0, 2, 1)
    x_cells, z_cells, y_cells, channels = field.shape
    gate_mask = fracture_mask.astype(jnp.float32)[..., None]
    hidden = field
    conv_outs = []
    for layer_num in range(LAYERS):
        conv_out = apply_offsets(
            with_rim(hidden), conv_weight[layer_num], dilation[layer_num], 1, field.shape
        )
        conv_outs.append(conv_out)
        hidden = (
            hidden.astype(jnp.float32) + gate_mask * (conv_out * jax.nn.sigmoid(conv_out))
        ).astype(jnp.bfloat16)
    slab_view = lax.all_to_all(hidden, "zslab", split_axis=0, concat_axis=1, tiled=True)
    x_local, z_total = (slab_view.shape[0], slab_view.shape[1])
    y_blocks, z_blocks = (y_cells // PY, z_total // PZ)
    patches = slab_view.reshape(x_local, z_blocks, PZ, y_blocks, PY, channels).transpose(
        3, 1, 0, 4, 2, 5
    )
    patches = patches.reshape(y_blocks * z_blocks, x_local, PY * PZ * channels)
    embed_rows, qkv_rows = gather_weights(embed_weight, qkv_weight)
    patches = patches.reshape(patches.shape[0], embed_rows.shape[0], embed_rows.shape[1])
    partial_value = jnp.einsum(
        "tbf,bfd->td", patches, embed_rows, preferred_element_type=jnp.float32
    )
    tokens = slab_total(partial_value).astype(jnp.bfloat16)
    projected = jnp.einsum(
        "td,sde->ste", tokens, qkv_rows, preferred_element_type=jnp.float32
    ).astype(jnp.bfloat16)
    tok_rows = tokens.shape[0]
    head_cols = projected.shape[2]
    heads_here = head_cols // HD
    inv_root = HD ** (-0.5)
    everything = joined_along(
        copy_for_each(
            jnp.concatenate([projected[0], projected[1], projected[2], out_grad], axis=1), "blk"
        ),
        0,
    )
    query_all, key_all, value_all, grad_all = [
        part.reshape(-1, heads_here, HD) for part in jnp.split(everything, 4, axis=1)
    ]
    first = lax.axis_index("blk") * tok_rows
    grad_out = out_grad.reshape(tok_rows, heads_here, HD)
    values_here = projected[2].reshape(tok_rows, heads_here, HD)
    scores = (
        jnp.einsum("qhd,khd->hqk", query_all, key_all, preferred_element_type=jnp.float32) * inv_root
    )
    top_score = jnp.max(scores, axis=2, keepdims=True)
    expo = jnp.exp(scores - top_score)
    total = jnp.sum(expo, axis=2, keepdims=True)
    probs = expo / total
    probs_b = probs.astype(jnp.bfloat16)
    attended = jnp.einsum("hqk,khd->qhd", probs_b, value_all, preferred_element_type=jnp.float32)
    row_delta = jnp.sum(grad_all.astype(jnp.float32) * attended, axis=2).T[:, :, None]
    probs_rows = lax.dynamic_slice_in_dim(probs, first, tok_rows, axis=1)
    delta_rows = lax.dynamic_slice_in_dim(row_delta, first, tok_rows, axis=1)
    grad_rows = jnp.einsum("qhd,khd->hqk", grad_out, value_all, preferred_element_type=jnp.float32)
    dscore_rows = (probs_rows * (grad_rows - delta_rows) * inv_root).astype(jnp.bfloat16)
    grad_query = jnp.einsum("hqk,khd->qhd", dscore_rows, key_all, preferred_element_type=jnp.float32)
    grad_query = grad_query.astype(jnp.bfloat16).reshape(tok_rows, head_cols)
    probs_cols = lax.dynamic_slice_in_dim(probs, first, tok_rows, axis=2)
    grad_cols = jnp.einsum("qhd,khd->hqk", grad_all, values_here, preferred_element_type=jnp.float32)
    dscore_cols = (probs_cols * (grad_cols - row_delta) * inv_root).astype(jnp.bfloat16)
    grad_key = jnp.einsum("hqk,qhd->khd", dscore_cols, query_all, preferred_element_type=jnp.float32)
    grad_key = grad_key.astype(jnp.bfloat16).reshape(tok_rows, head_cols)
    grad_value = jnp.einsum(
        "hqk,qhd->khd", probs_cols.astype(jnp.bfloat16), grad_all, preferred_element_type=jnp.float32
    )
    grad_value = grad_value.astype(jnp.bfloat16).reshape(tok_rows, head_cols)
    stacked_grads = jnp.stack([grad_query, grad_key, grad_value])
    partial_grad = jnp.einsum(
        "ste,sde->td", stacked_grads, qkv_rows, preferred_element_type=jnp.float32
    )
    grad_tokens = slab_total(partial_grad).astype(jnp.bfloat16)
    patch_grad = jnp.einsum(
        "td,bfd->tbf", grad_tokens, embed_rows, preferred_element_type=jnp.float32
    ).astype(jnp.bfloat16)
    grid_grad = patch_grad.reshape(y_blocks, z_blocks, x_local, PY, PZ, channels).transpose(
        2, 1, 4, 0, 3, 5
    )
    grid_grad = grid_grad.reshape(x_local, z_total, y_cells, channels)
    grid_grad = lax.all_to_all(grid_grad, "zslab", split_axis=1, concat_axis=0, tiled=True)
    for layer_num in reversed(range(LAYERS)):
        conv_out = conv_outs[layer_num]
        sigma = jax.nn.sigmoid(conv_out)
        slope_grad = (
            gate_mask * sigma * (1.0 + conv_out * (1.0 - sigma)) * grid_grad.astype(jnp.float32)
        ).astype(jnp.bfloat16)
        flipped = (
            conv_weight[layer_num]
            .reshape(27, channels, channels)
            .transpose(0, 2, 1)
            .reshape(27 * channels, channels)
        )
        backward = apply_offsets(
            with_rim(slope_grad), flipped, dilation[layer_num], -1, field.shape
        )
        grid_grad = (grid_grad.astype(jnp.float32) + backward).astype(jnp.bfloat16)
    return grid_grad.transpose(0, 2, 1, 3)


def solution(mesh):
    return jax.shard_map(
        local,
        mesh=mesh,
        in_specs=(
            P("blk", None, "zslab", None),
            P("blk", None, "zslab"),
            P(),
            P(),
            P("zslab", "blk", None),
            P(None, "blk", "zslab"),
            P("blk", "zslab"),
        ),
        out_specs=P("blk", None, "zslab", None),
        check_vma=False,
    )
```

```python
import jax
import jax.numpy as jnp
from jax import lax
from jax.sharding import PartitionSpec as P

HD = 128
PY = 8
PZ = 2
LAYERS = 2
DMAX = 2


def padded_2(cells, sides, width):
    for axis, dim in sides:
        count = lax.axis_size(axis)
        ends = count - 1
        head = lax.slice_in_dim(cells, 0, width, axis=dim)
        tail = lax.slice_in_dim(cells, cells.shape[dim] - width, cells.shape[dim], axis=dim)
        cells = jnp.concatenate(
            [
                lax.ppermute(tail, axis, [(i, (i + 1) % count) for i in range(ends)]),
                cells,
                lax.ppermute(head, axis, [((i + 1) % count, i) for i in range(ends)]),
            ],
            axis=dim,
        )
    return cells


def copy_for_each(shard, axis):
    peers = lax.axis_size(axis)
    return lax.all_to_all(
        jnp.broadcast_to(shard[None], (peers, *shard.shape)), axis, 0, 0, tiled=True
    )


def taken_together(shard, axis):
    return copy_for_each(shard, axis).astype(jnp.float32).sum(axis=0)


def joined_along(pieces, dim):
    shape = list(pieces.shape[1:])
    shape[dim] *= pieces.shape[0]
    return jnp.moveaxis(pieces, 0, dim).reshape(shape)


def gather_together(arrays, axis, dims):
    line = jnp.concatenate([a.reshape(-1) for a in arrays])
    lines, at, finished = (lax.all_gather(line, axis), 0, [])
    for a, dim in zip(arrays, dims):
        pieces = lines[:, at : at + a.size].reshape(-1, *a.shape)
        finished.append(joined_along(pieces, dim))
        at += a.size
    return tuple(finished)


def side_by_side(arrays, axis, dim, along):
    ends, at = ([], 0)
    for a in arrays[:-1]:
        at += a.shape[along]
        ends.append(at)
    both = jnp.concatenate(arrays, axis=along)
    return tuple(jnp.split(lax.all_gather(both, axis, axis=dim, tiled=True), ends, axis=along))


def cut_along(shard, dim, peers):
    before, after = (shard.shape[:dim], shard.shape[dim + 1 :])
    return jnp.moveaxis(shard.reshape(*before, peers, -1, *after), dim, 0)


def sum_at_owner(shard, axis, dim):
    peers = lax.axis_size(axis)
    pieces = lax.all_to_all(cut_along(shard, dim, peers), axis, 0, 0, tiled=True)
    return jnp.sum(pieces.astype(jnp.float32), axis=0)


def gather_weights(embed_weight, qkv_weight, after):
    _, feat, width = embed_weight.shape
    qkv_flat = qkv_weight.reshape(-1, width)
    extra = -qkv_flat.shape[0] % 16
    rows = jnp.concatenate(
        [embed_weight[0], qkv_flat, jnp.zeros((extra, width), qkv_flat.dtype)], axis=0
    )
    peers = lax.axis_size("blk")
    near = [list(range(start, start + 4)) for start in range(0, peers, 4)]
    far = [list(range(start, peers, 4)) for start in range(4)]
    gathered = lax.all_gather(rows, "blk", axis=0, tiled=True, axis_index_groups=near)
    half = gathered.shape[0] // 2
    odd = (lax.axis_index("blk") & 1) != 0
    mine = jnp.where(odd, gathered[half:], gathered[:half])
    own = lax.all_gather(mine, "blk", axis=0, tiled=True, axis_index_groups=far)
    own, after = lax.optimization_barrier((own, after))
    other = lax.ppermute(own, "blk", [(i, i ^ 1) for i in range(peers)])
    own = own.reshape(len(far[0]), half, width)
    other = other.reshape(len(far[0]), half, width)
    gathered = jnp.concatenate(
        [jnp.where(odd, other, own), jnp.where(odd, own, other)], axis=1
    )
    gathered = gathered.reshape(peers, rows.shape[0], width)
    embed_rows = gathered[:, :feat, :]
    qkv_rows = gathered[:, feat : feat + qkv_flat.shape[0], :].reshape(peers, *qkv_weight.shape)
    qkv_rows = jnp.moveaxis(qkv_rows, 0, 1).reshape(
        qkv_weight.shape[0], peers * qkv_weight.shape[1], qkv_weight.shape[2]
    )
    return embed_rows, qkv_rows, after


def with_rim(volume):
    return padded_2(volume, (("zslab", 1), ("blk", 0)), DMAX)


def picked(cells, dim, step, rate, size):
    near = lax.slice_in_dim(cells, DMAX + step, DMAX + step + size, axis=dim)
    if step == 0:
        return near
    far = lax.slice_in_dim(cells, DMAX + 2 * step, DMAX + 2 * step + size, axis=dim)
    return jnp.where(rate == 1, near, far)


def shifted_y(values, step, rate):
    def by(amount):
        cells = values.shape[2]
        zeros = jnp.zeros_like(values[:, :, : abs(amount)])
        if amount > 0:
            return jnp.concatenate([values[:, :, amount:], zeros], axis=2)
        return jnp.concatenate([zeros, values[:, :, : cells + amount]], axis=2)

    if step == 0:
        return values
    return jnp.where(rate == 1, by(step), by(2 * step))


def apply_offsets(padded, weight, dilate, direction, dims_out):
    x_cells, z_cells, y_cells, channels = dims_out
    windows = []
    for offset_x in (-1, 0, 1):
        along_x = picked(padded, 0, direction * offset_x, dilate[0], x_cells)
        for offset_z in (-1, 0, 1):
            windows.append(picked(along_x, 1, direction * offset_z, dilate[2], z_cells))
    stacked = jnp.concatenate(windows, axis=3).reshape(x_cells * z_cells * y_cells, 9 * channels)
    taps = weight.reshape(3, 3, 3, channels, -1)
    summed = None
    for offset_y in (-1, 0, 1):
        rows = taps[:, offset_y + 1].reshape(9 * channels, -1)
        part = jnp.dot(stacked, rows, preferred_element_type=jnp.float32)
        part = shifted_y(part.reshape(x_cells, z_cells, y_cells, -1), direction * offset_y, dilate[1])
        summed = part if summed is None else summed + part
    return summed


def slab_total(term):
    return taken_together(term.astype(jnp.bfloat16), "zslab").astype(jnp.float32)


def local(field, fracture_mask, dilation, conv_weight, embed_weight, qkv_weight, out_grad):
    field = field.transpose(0, 2, 1, 3)
    fracture_mask = fracture_mask.transpose(0, 2, 1)
    x_cells, z_cells, y_cells, channels = field.shape
    gate_mask = fracture_mask.astype(jnp.float32)[..., None]
    hidden = field
    conv_outs = []
    for layer_num in range(LAYERS):
        conv_out = apply_offsets(
            with_rim(hidden), conv_weight[layer_num], dilation[layer_num], 1, field.shape
        )
        conv_outs.append(conv_out)
        hidden = (
            hidden.astype(jnp.float32) + gate_mask * (conv_out * jax.nn.sigmoid(conv_out))
        ).astype(jnp.bfloat16)
    slab_view = lax.all_to_all(hidden, "zslab", split_axis=0, concat_axis=1, tiled=True)
    embed_rows, qkv_rows, slab_view = gather_weights(embed_weight, qkv_weight, slab_view)
    x_local, z_total = (slab_view.shape[0], slab_view.shape[1])
    y_blocks, z_blocks = (y_cells // PY, z_total // PZ)
    patches = slab_view.reshape(x_local, z_blocks, PZ, y_blocks, PY, channels).transpose(
        3, 1, 0, 4, 2, 5
    )
    patches = patches.reshape(y_blocks * z_blocks, x_local, PY * PZ * channels)
    patches = patches.reshape(patches.shape[0], embed_rows.shape[0], embed_rows.shape[1])
    partial_value = jnp.einsum(
        "tbf,bfd->td", patches, embed_rows, preferred_element_type=jnp.float32
    )
    tokens = slab_total(partial_value).astype(jnp.bfloat16)
    projected = jnp.einsum(
        "td,sde->ste", tokens, qkv_rows, preferred_element_type=jnp.float32
    ).astype(jnp.bfloat16)
    tok_rows = tokens.shape[0]
    head_cols = projected.shape[2]
    heads_here = head_cols // HD
    inv_root = HD ** (-0.5)
    everything = joined_along(
        copy_for_each(
            jnp.concatenate([projected[0], projected[1], projected[2], out_grad], axis=1), "blk"
        ),
        0,
    )
    query_all, key_all, value_all, grad_all = [
        part.reshape(-1, heads_here, HD) for part in jnp.split(everything, 4, axis=1)
    ]
    first = lax.axis_index("blk") * tok_rows
    grad_out = out_grad.reshape(tok_rows, heads_here, HD)
    values_here = projected[2].reshape(tok_rows, heads_here, HD)
    scores = (
        jnp.einsum("qhd,khd->hqk", query_all, key_all, preferred_element_type=jnp.float32) * inv_root
    )
    top_score = jnp.max(scores, axis=2, keepdims=True)
    expo = jnp.exp(scores - top_score)
    total = jnp.sum(expo, axis=2, keepdims=True)
    probs = expo / total
    probs_b = probs.astype(jnp.bfloat16)
    attended = jnp.einsum("hqk,khd->qhd", probs_b, value_all, preferred_element_type=jnp.float32)
    row_delta = jnp.sum(grad_all.astype(jnp.float32) * attended, axis=2).T[:, :, None]
    probs_rows = lax.dynamic_slice_in_dim(probs, first, tok_rows, axis=1)
    delta_rows = lax.dynamic_slice_in_dim(row_delta, first, tok_rows, axis=1)
    grad_rows = jnp.einsum("qhd,khd->hqk", grad_out, value_all, preferred_element_type=jnp.float32)
    dscore_rows = (probs_rows * (grad_rows - delta_rows) * inv_root).astype(jnp.bfloat16)
    grad_query = jnp.einsum("hqk,khd->qhd", dscore_rows, key_all, preferred_element_type=jnp.float32)
    grad_query = grad_query.astype(jnp.bfloat16).reshape(tok_rows, head_cols)
    probs_cols = lax.dynamic_slice_in_dim(probs, first, tok_rows, axis=2)
    grad_cols = jnp.einsum("qhd,khd->hqk", grad_all, values_here, preferred_element_type=jnp.float32)
    dscore_cols = (probs_cols * (grad_cols - row_delta) * inv_root).astype(jnp.bfloat16)
    grad_key = jnp.einsum("hqk,qhd->khd", dscore_cols, query_all, preferred_element_type=jnp.float32)
    grad_key = grad_key.astype(jnp.bfloat16).reshape(tok_rows, head_cols)
    grad_value = jnp.einsum(
        "hqk,qhd->khd", probs_cols.astype(jnp.bfloat16), grad_all, preferred_element_type=jnp.float32
    )
    grad_value = grad_value.astype(jnp.bfloat16).reshape(tok_rows, head_cols)
    stacked_grads = jnp.stack([grad_query, grad_key, grad_value])
    partial_grad = jnp.einsum(
        "ste,sde->td", stacked_grads, qkv_rows, preferred_element_type=jnp.float32
    )
    grad_tokens = slab_total(partial_grad).astype(jnp.bfloat16)
    patch_grad = jnp.einsum(
        "td,bfd->tbf", grad_tokens, embed_rows, preferred_element_type=jnp.float32
    ).astype(jnp.bfloat16)
    grid_grad = patch_grad.reshape(y_blocks, z_blocks, x_local, PY, PZ, channels).transpose(
        2, 1, 4, 0, 3, 5
    )
    grid_grad = grid_grad.reshape(x_local, z_total, y_cells, channels)
    grid_grad = lax.all_to_all(grid_grad, "zslab", split_axis=1, concat_axis=0, tiled=True)
    for layer_num in reversed(range(LAYERS)):
        conv_out = conv_outs[layer_num]
        sigma = jax.nn.sigmoid(conv_out)
        slope_grad = (
            gate_mask * sigma * (1.0 + conv_out * (1.0 - sigma)) * grid_grad.astype(jnp.float32)
        ).astype(jnp.bfloat16)
        flipped = (
            conv_weight[layer_num]
            .reshape(27, channels, channels)
            .transpose(0, 2, 1)
            .reshape(27 * channels, channels)
        )
        backward = apply_offsets(
            with_rim(slope_grad), flipped, dilation[layer_num], -1, field.shape
        )
        grid_grad = (grid_grad.astype(jnp.float32) + backward).astype(jnp.bfloat16)
    return grid_grad.transpose(0, 2, 1, 3)


def solution(mesh):
    return jax.shard_map(
        local,
        mesh=mesh,
        in_specs=(
            P("blk", None, "zslab", None),
            P("blk", None, "zslab"),
            P(),
            P(),
            P("zslab", "blk", None),
            P(None, "blk", "zslab"),
            P("blk", "zslab"),
        ),
        out_specs=P("blk", None, "zslab", None),
        check_vma=False,
    )
```

```python
import jax
import jax.numpy as jnp
from jax import lax
from jax.sharding import PartitionSpec as P

HD = 128
PY = 8
PZ = 2
LAYERS = 2
DMAX = 2


def padded_2(cells, sides, width):
    for axis, dim in sides:
        count = lax.axis_size(axis)
        ends = count - 1
        head = lax.slice_in_dim(cells, 0, width, axis=dim)
        tail = lax.slice_in_dim(cells, cells.shape[dim] - width, cells.shape[dim], axis=dim)
        cells = jnp.concatenate(
            [
                lax.ppermute(tail, axis, [(i, (i + 1) % count) for i in range(ends)]),
                cells,
                lax.ppermute(head, axis, [((i + 1) % count, i) for i in range(ends)]),
            ],
            axis=dim,
        )
    return cells


def copy_for_each(shard, axis):
    peers = lax.axis_size(axis)
    return lax.all_to_all(
        jnp.broadcast_to(shard[None], (peers, *shard.shape)), axis, 0, 0, tiled=True
    )


def taken_together(shard, axis):
    return copy_for_each(shard, axis).astype(jnp.float32).sum(axis=0)


def joined_along(pieces, dim):
    shape = list(pieces.shape[1:])
    shape[dim] *= pieces.shape[0]
    return jnp.moveaxis(pieces, 0, dim).reshape(shape)


def gather_together(arrays, axis, dims):
    line = jnp.concatenate([a.reshape(-1) for a in arrays])
    lines, at, finished = (lax.all_gather(line, axis), 0, [])
    for a, dim in zip(arrays, dims):
        pieces = lines[:, at : at + a.size].reshape(-1, *a.shape)
        finished.append(joined_along(pieces, dim))
        at += a.size
    return tuple(finished)


def side_by_side(arrays, axis, dim, along):
    ends, at = ([], 0)
    for a in arrays[:-1]:
        at += a.shape[along]
        ends.append(at)
    both = jnp.concatenate(arrays, axis=along)
    return tuple(jnp.split(lax.all_gather(both, axis, axis=dim, tiled=True), ends, axis=along))


def cut_along(shard, dim, peers):
    before, after = (shard.shape[:dim], shard.shape[dim + 1 :])
    return jnp.moveaxis(shard.reshape(*before, peers, -1, *after), dim, 0)


def sum_at_owner(shard, axis, dim):
    peers = lax.axis_size(axis)
    pieces = lax.all_to_all(cut_along(shard, dim, peers), axis, 0, 0, tiled=True)
    return jnp.sum(pieces.astype(jnp.float32), axis=0)


def gather_weights(embed_weight, qkv_weight, after):
    _, feat, width = embed_weight.shape
    qkv_flat = qkv_weight.reshape(-1, width)
    extra = -qkv_flat.shape[0] % 16
    rows = jnp.concatenate(
        [embed_weight[0], qkv_flat, jnp.zeros((extra, width), qkv_flat.dtype)], axis=0
    )
    peers = lax.axis_size("blk")
    near = [list(range(start, start + 4)) for start in range(0, peers, 4)]
    far = [list(range(start, peers, 4)) for start in range(4)]
    gathered = lax.all_gather(rows, "blk", axis=0, tiled=True, axis_index_groups=near)
    half = gathered.shape[0] // 2
    odd = (lax.axis_index("blk") & 1) != 0
    mine = jnp.where(odd, gathered[half:], gathered[:half])
    own = lax.all_gather(mine, "blk", axis=0, tiled=True, axis_index_groups=far)
    own, after = lax.optimization_barrier((own, after))
    other = lax.ppermute(own, "blk", [(i, i ^ 1) for i in range(peers)])
    own = own.reshape(len(far[0]), half, width)
    other = other.reshape(len(far[0]), half, width)
    gathered = jnp.concatenate(
        [jnp.where(odd, other, own), jnp.where(odd, own, other)], axis=1
    )
    gathered = gathered.reshape(peers, rows.shape[0], width)
    embed_rows = gathered[:, :feat, :]
    qkv_rows = gathered[:, feat : feat + qkv_flat.shape[0], :].reshape(peers, *qkv_weight.shape)
    qkv_rows = jnp.moveaxis(qkv_rows, 0, 1).reshape(
        qkv_weight.shape[0], peers * qkv_weight.shape[1], qkv_weight.shape[2]
    )
    return embed_rows, qkv_rows, after


def with_rim(volume):
    return padded_2(volume, (("zslab", 1), ("blk", 0)), DMAX)


def picked(cells, dim, step, rate, size):
    near = lax.slice_in_dim(cells, DMAX + step, DMAX + step + size, axis=dim)
    if step == 0:
        return near
    far = lax.slice_in_dim(cells, DMAX + 2 * step, DMAX + 2 * step + size, axis=dim)
    return jnp.where(rate == 1, near, far)


def shifted_y(values, step, rate):
    def by(amount):
        cells = values.shape[2]
        zeros = jnp.zeros_like(values[:, :, : abs(amount)])
        if amount > 0:
            return jnp.concatenate([values[:, :, amount:], zeros], axis=2)
        return jnp.concatenate([zeros, values[:, :, : cells + amount]], axis=2)

    if step == 0:
        return values
    return jnp.where(rate == 1, by(step), by(2 * step))


def apply_offsets(padded, weight, dilate, direction, dims_out):
    x_cells, z_cells, y_cells, channels = dims_out
    windows = []
    for offset_x in (-1, 0, 1):
        along_x = picked(padded, 0, direction * offset_x, dilate[0], x_cells)
        for offset_z in (-1, 0, 1):
            windows.append(picked(along_x, 1, direction * offset_z, dilate[2], z_cells))
    stacked = jnp.concatenate(windows, axis=3).reshape(x_cells * z_cells * y_cells, 9 * channels)
    taps = weight.reshape(3, 3, 3, channels, -1)
    summed = None
    for offset_y in (-1, 0, 1):
        rows = taps[:, offset_y + 1].reshape(9 * channels, -1)
        part = jnp.dot(stacked, rows, preferred_element_type=jnp.float32)
        part = shifted_y(part.reshape(x_cells, z_cells, y_cells, -1), direction * offset_y, dilate[1])
        summed = part if summed is None else summed + part
    return summed


def slab_total(term):
    return taken_together(term.astype(jnp.bfloat16), "zslab").astype(jnp.float32)


def local(field, fracture_mask, dilation, conv_weight, embed_weight, qkv_weight, out_grad):
    field = field.transpose(0, 2, 1, 3)
    fracture_mask = fracture_mask.transpose(0, 2, 1)
    x_cells, z_cells, y_cells, channels = field.shape
    gate_mask = fracture_mask.astype(jnp.float32)[..., None]
    hidden = field
    conv_outs = []
    for layer_num in range(LAYERS):
        conv_out = apply_offsets(
            with_rim(hidden), conv_weight[layer_num], dilation[layer_num], 1, field.shape
        )
        conv_outs.append(conv_out)
        hidden = (
            hidden.astype(jnp.float32) + gate_mask * (conv_out * jax.nn.sigmoid(conv_out))
        ).astype(jnp.bfloat16)
    slab_view = lax.all_to_all(hidden, "zslab", split_axis=0, concat_axis=1, tiled=True)
    embed_rows, qkv_rows, slab_view = gather_weights(embed_weight, qkv_weight, slab_view)
    x_local, z_total = (slab_view.shape[0], slab_view.shape[1])
    y_blocks, z_blocks = (y_cells // PY, z_total // PZ)
    patches = slab_view.reshape(x_local, z_blocks, PZ, y_blocks, PY, channels).transpose(
        3, 1, 0, 4, 2, 5
    )
    patches = patches.reshape(y_blocks * z_blocks, x_local, PY * PZ * channels)
    patches = patches.reshape(patches.shape[0], embed_rows.shape[0], embed_rows.shape[1])
    partial_value = jnp.einsum(
        "tbf,bfd->td", patches, embed_rows, preferred_element_type=jnp.float32
    )
    tokens = slab_total(partial_value).astype(jnp.bfloat16)
    projected = jnp.einsum(
        "td,sde->ste", tokens, qkv_rows, preferred_element_type=jnp.float32
    ).astype(jnp.bfloat16)
    key_rows, value_rows = jnp.split(
        joined_along(copy_for_each(jnp.concatenate([projected[1], projected[2]], axis=1), "blk"), 0),
        2,
        axis=1,
    )
    tok_rows = tokens.shape[0]
    head_cols = projected.shape[2]
    heads_here = head_cols // HD
    inv_root = HD ** (-0.5)
    queries = projected[0].reshape(tok_rows, heads_here, HD)
    key_all = key_rows.reshape(-1, heads_here, HD)
    value_all = value_rows.reshape(-1, heads_here, HD)
    grad_out = out_grad.reshape(tok_rows, heads_here, HD)
    scores = (
        jnp.einsum("qhd,khd->hqk", queries, key_all, preferred_element_type=jnp.float32) * inv_root
    )
    top_score = jnp.max(scores, axis=2, keepdims=True)
    expo = jnp.exp(scores - top_score)
    total = jnp.sum(expo, axis=2, keepdims=True)
    probs = expo / total
    probs_b = probs.astype(jnp.bfloat16)
    attended = jnp.einsum("hqk,khd->qhd", probs_b, value_all, preferred_element_type=jnp.float32)
    row_delta = jnp.sum(grad_out.astype(jnp.float32) * attended, axis=2).T[:, :, None]
    score_grad = jnp.einsum("qhd,khd->hqk", grad_out, value_all, preferred_element_type=jnp.float32)
    dscore = (probs * (score_grad - row_delta) * inv_root).astype(jnp.bfloat16)
    grad_query = jnp.einsum("hqk,khd->qhd", dscore, key_all, preferred_element_type=jnp.float32)
    grad_query = grad_query.astype(jnp.bfloat16).reshape(tok_rows, head_cols)
    key_term = jnp.einsum("hqk,qhd->khd", dscore, queries, preferred_element_type=jnp.float32)
    value_term = jnp.einsum("hqk,qhd->khd", probs_b, grad_out, preferred_element_type=jnp.float32)
    key_value_grad = sum_at_owner(
        jnp.concatenate(
            [
                key_term.reshape(tok_rows * lax.axis_size("blk"), head_cols),
                value_term.reshape(tok_rows * lax.axis_size("blk"), head_cols),
            ],
            axis=1,
        ).astype(jnp.bfloat16),
        "blk",
        0,
    ).astype(jnp.bfloat16)
    grad_key = key_value_grad[:, :head_cols]
    grad_value = key_value_grad[:, head_cols:]
    stacked_grads = jnp.stack([grad_query, grad_key, grad_value])
    partial_grad = jnp.einsum(
        "ste,sde->td", stacked_grads, qkv_rows, preferred_element_type=jnp.float32
    )
    grad_tokens = slab_total(partial_grad).astype(jnp.bfloat16)
    patch_grad = jnp.einsum(
        "td,bfd->tbf", grad_tokens, embed_rows, preferred_element_type=jnp.float32
    ).astype(jnp.bfloat16)
    grid_grad = patch_grad.reshape(y_blocks, z_blocks, x_local, PY, PZ, channels).transpose(
        2, 1, 4, 0, 3, 5
    )
    grid_grad = grid_grad.reshape(x_local, z_total, y_cells, channels)
    grid_grad = lax.all_to_all(grid_grad, "zslab", split_axis=1, concat_axis=0, tiled=True)
    for layer_num in reversed(range(LAYERS)):
        conv_out = conv_outs[layer_num]
        sigma = jax.nn.sigmoid(conv_out)
        slope_grad = (
            gate_mask * sigma * (1.0 + conv_out * (1.0 - sigma)) * grid_grad.astype(jnp.float32)
        ).astype(jnp.bfloat16)
        flipped = (
            conv_weight[layer_num]
            .reshape(27, channels, channels)
            .transpose(0, 2, 1)
            .reshape(27 * channels, channels)
        )
        backward = apply_offsets(
            with_rim(slope_grad), flipped, dilation[layer_num], -1, field.shape
        )
        grid_grad = (grid_grad.astype(jnp.float32) + backward).astype(jnp.bfloat16)
    return grid_grad.transpose(0, 2, 1, 3)


def solution(mesh):
    return jax.shard_map(
        local,
        mesh=mesh,
        in_specs=(
            P("blk", None, "zslab", None),
            P("blk", None, "zslab"),
            P(),
            P(),
            P("zslab", "blk", None),
            P(None, "blk", "zslab"),
            P("blk", "zslab"),
        ),
        out_specs=P("blk", None, "zslab", None),
        check_vma=False,
    )
```

```python
import jax
import jax.numpy as jnp
from jax import lax
from jax.sharding import PartitionSpec as P

HD = 128
PY = 8
PZ = 2
LAYERS = 2
DMAX = 2


def padded_2(cells, sides, width):
    for axis, dim in sides:
        count = lax.axis_size(axis)
        ends = count - 1
        head = lax.slice_in_dim(cells, 0, width, axis=dim)
        tail = lax.slice_in_dim(cells, cells.shape[dim] - width, cells.shape[dim], axis=dim)
        cells = jnp.concatenate(
            [
                lax.ppermute(tail, axis, [(i, (i + 1) % count) for i in range(ends)]),
                cells,
                lax.ppermute(head, axis, [((i + 1) % count, i) for i in range(ends)]),
            ],
            axis=dim,
        )
    return cells


def copy_for_each(shard, axis):
    peers = lax.axis_size(axis)
    return lax.all_to_all(
        jnp.broadcast_to(shard[None], (peers, *shard.shape)), axis, 0, 0, tiled=True
    )


def taken_together(shard, axis):
    return copy_for_each(shard, axis).astype(jnp.float32).sum(axis=0)


def joined_along(pieces, dim):
    shape = list(pieces.shape[1:])
    shape[dim] *= pieces.shape[0]
    return jnp.moveaxis(pieces, 0, dim).reshape(shape)


def gather_together(arrays, axis, dims):
    line = jnp.concatenate([a.reshape(-1) for a in arrays])
    lines, at, finished = (lax.all_gather(line, axis), 0, [])
    for a, dim in zip(arrays, dims):
        pieces = lines[:, at : at + a.size].reshape(-1, *a.shape)
        finished.append(joined_along(pieces, dim))
        at += a.size
    return tuple(finished)


def side_by_side(arrays, axis, dim, along):
    ends, at = ([], 0)
    for a in arrays[:-1]:
        at += a.shape[along]
        ends.append(at)
    both = jnp.concatenate(arrays, axis=along)
    return tuple(jnp.split(lax.all_gather(both, axis, axis=dim, tiled=True), ends, axis=along))


def cut_along(shard, dim, peers):
    before, after = (shard.shape[:dim], shard.shape[dim + 1 :])
    return jnp.moveaxis(shard.reshape(*before, peers, -1, *after), dim, 0)


def sum_at_owner(shard, axis, dim):
    peers = lax.axis_size(axis)
    pieces = lax.all_to_all(cut_along(shard, dim, peers), axis, 0, 0, tiled=True)
    return jnp.sum(pieces.astype(jnp.float32), axis=0)


def gathered_in_stages(rows, axis):
    peers = lax.axis_size(axis)
    near = [list(range(start, start + 4)) for start in range(0, peers, 4)]
    far = [list(range(start, peers, 4)) for start in range(4)]
    rows = lax.all_gather(rows, axis, axis=0, tiled=True, axis_index_groups=near)
    return lax.all_gather(rows, axis, axis=0, tiled=True, axis_index_groups=far)


def gather_weights(embed_weight, qkv_weight):
    _, feat, width = embed_weight.shape
    peers = lax.axis_size("blk")
    embed_rows = gathered_in_stages(embed_weight[0], "blk").reshape(peers, feat, width)
    qkv_flat = qkv_weight.reshape(-1, width)
    extra = -qkv_flat.shape[0] % 16
    rows = jnp.concatenate([qkv_flat, jnp.zeros((extra, width), qkv_flat.dtype)], axis=0)
    gathered = gathered_in_stages(rows, "blk").reshape(peers, rows.shape[0], width)
    qkv_rows = gathered[:, : qkv_flat.shape[0], :].reshape(peers, *qkv_weight.shape)
    qkv_rows = jnp.moveaxis(qkv_rows, 0, 1).reshape(
        qkv_weight.shape[0], peers * qkv_weight.shape[1], qkv_weight.shape[2]
    )
    return embed_rows, qkv_rows


def with_rim(volume):
    return padded_2(volume, (("zslab", 1), ("blk", 0)), DMAX)


def picked(cells, dim, step, rate, size):
    near = lax.slice_in_dim(cells, DMAX + step, DMAX + step + size, axis=dim)
    if step == 0:
        return near
    far = lax.slice_in_dim(cells, DMAX + 2 * step, DMAX + 2 * step + size, axis=dim)
    return jnp.where(rate == 1, near, far)


def shifted_y(values, step, rate):
    def by(amount):
        cells = values.shape[2]
        zeros = jnp.zeros_like(values[:, :, : abs(amount)])
        if amount > 0:
            return jnp.concatenate([values[:, :, amount:], zeros], axis=2)
        return jnp.concatenate([zeros, values[:, :, : cells + amount]], axis=2)

    if step == 0:
        return values
    return jnp.where(rate == 1, by(step), by(2 * step))


def apply_offsets(padded, weight, dilate, direction, dims_out):
    x_cells, z_cells, y_cells, channels = dims_out
    windows = []
    for offset_x in (-1, 0, 1):
        along_x = picked(padded, 0, direction * offset_x, dilate[0], x_cells)
        for offset_z in (-1, 0, 1):
            windows.append(picked(along_x, 1, direction * offset_z, dilate[2], z_cells))
    stacked = jnp.concatenate(windows, axis=3).reshape(x_cells * z_cells * y_cells, 9 * channels)
    taps = weight.reshape(3, 3, 3, channels, -1)
    summed = None
    for offset_y in (-1, 0, 1):
        rows = taps[:, offset_y + 1].reshape(9 * channels, -1)
        part = jnp.dot(stacked, rows, preferred_element_type=jnp.float32)
        part = shifted_y(part.reshape(x_cells, z_cells, y_cells, -1), direction * offset_y, dilate[1])
        summed = part if summed is None else summed + part
    return summed


def slab_total(term):
    return taken_together(term.astype(jnp.bfloat16), "zslab").astype(jnp.float32)


def local(field, fracture_mask, dilation, conv_weight, embed_weight, qkv_weight, out_grad):
    field = field.transpose(0, 2, 1, 3)
    fracture_mask = fracture_mask.transpose(0, 2, 1)
    x_cells, z_cells, y_cells, channels = field.shape
    gate_mask = fracture_mask.astype(jnp.float32)[..., None]
    hidden = field
    conv_outs = []
    for layer_num in range(LAYERS):
        conv_out = apply_offsets(
            with_rim(hidden), conv_weight[layer_num], dilation[layer_num], 1, field.shape
        )
        conv_outs.append(conv_out)
        hidden = (
            hidden.astype(jnp.float32) + gate_mask * (conv_out * jax.nn.sigmoid(conv_out))
        ).astype(jnp.bfloat16)
    slab_view = lax.all_to_all(hidden, "zslab", split_axis=0, concat_axis=1, tiled=True)
    x_local, z_total = (slab_view.shape[0], slab_view.shape[1])
    y_blocks, z_blocks = (y_cells // PY, z_total // PZ)
    patches = slab_view.reshape(x_local, z_blocks, PZ, y_blocks, PY, channels).transpose(
        3, 1, 0, 4, 2, 5
    )
    patches = patches.reshape(y_blocks * z_blocks, x_local, PY * PZ * channels)
    embed_rows, qkv_rows = gather_weights(embed_weight, qkv_weight)
    patches = patches.reshape(patches.shape[0], embed_rows.shape[0], embed_rows.shape[1])
    partial_value = jnp.einsum(
        "tbf,bfd->td", patches, embed_rows, preferred_element_type=jnp.float32
    )
    tokens = slab_total(partial_value).astype(jnp.bfloat16)
    projected = jnp.einsum(
        "td,sde->ste", tokens, qkv_rows, preferred_element_type=jnp.float32
    ).astype(jnp.bfloat16)
    key_rows, value_rows = jnp.split(
        joined_along(copy_for_each(jnp.concatenate([projected[1], projected[2]], axis=1), "blk"), 0),
        2,
        axis=1,
    )
    tok_rows = tokens.shape[0]
    head_cols = projected.shape[2]
    heads_here = head_cols // HD
    inv_root = HD ** (-0.5)
    queries = projected[0].reshape(tok_rows, heads_here, HD)
    key_all = key_rows.reshape(-1, heads_here, HD)
    value_all = value_rows.reshape(-1, heads_here, HD)
    grad_out = out_grad.reshape(tok_rows, heads_here, HD)
    scores = (
        jnp.einsum("qhd,khd->hqk", queries, key_all, preferred_element_type=jnp.float32) * inv_root
    )
    top_score = jnp.max(scores, axis=2, keepdims=True)
    expo = jnp.exp(scores - top_score)
    total = jnp.sum(expo, axis=2, keepdims=True)
    probs = expo / total
    probs_b = probs.astype(jnp.bfloat16)
    attended = jnp.einsum("hqk,khd->qhd", probs_b, value_all, preferred_element_type=jnp.float32)
    row_delta = jnp.sum(grad_out.astype(jnp.float32) * attended, axis=2).T[:, :, None]
    score_grad = jnp.einsum("qhd,khd->hqk", grad_out, value_all, preferred_element_type=jnp.float32)
    dscore = (probs * (score_grad - row_delta) * inv_root).astype(jnp.bfloat16)
    grad_query = jnp.einsum("hqk,khd->qhd", dscore, key_all, preferred_element_type=jnp.float32)
    grad_query = grad_query.astype(jnp.bfloat16).reshape(tok_rows, head_cols)
    key_term = jnp.einsum("hqk,qhd->khd", dscore, queries, preferred_element_type=jnp.float32)
    value_term = jnp.einsum("hqk,qhd->khd", probs_b, grad_out, preferred_element_type=jnp.float32)
    key_value_grad = sum_at_owner(
        jnp.concatenate(
            [
                key_term.reshape(tok_rows * lax.axis_size("blk"), head_cols),
                value_term.reshape(tok_rows * lax.axis_size("blk"), head_cols),
            ],
            axis=1,
        ).astype(jnp.bfloat16),
        "blk",
        0,
    ).astype(jnp.bfloat16)
    grad_key = key_value_grad[:, :head_cols]
    grad_value = key_value_grad[:, head_cols:]
    stacked_grads = jnp.stack([grad_query, grad_key, grad_value])
    partial_grad = jnp.einsum(
        "ste,sde->td", stacked_grads, qkv_rows, preferred_element_type=jnp.float32
    )
    grad_tokens = slab_total(partial_grad).astype(jnp.bfloat16)
    patch_grad = jnp.einsum(
        "td,bfd->tbf", grad_tokens, embed_rows, preferred_element_type=jnp.float32
    ).astype(jnp.bfloat16)
    grid_grad = patch_grad.reshape(y_blocks, z_blocks, x_local, PY, PZ, channels).transpose(
        2, 1, 4, 0, 3, 5
    )
    grid_grad = grid_grad.reshape(x_local, z_total, y_cells, channels)
    grid_grad = lax.all_to_all(grid_grad, "zslab", split_axis=1, concat_axis=0, tiled=True)
    for layer_num in reversed(range(LAYERS)):
        conv_out = conv_outs[layer_num]
        sigma = jax.nn.sigmoid(conv_out)
        slope_grad = (
            gate_mask * sigma * (1.0 + conv_out * (1.0 - sigma)) * grid_grad.astype(jnp.float32)
        ).astype(jnp.bfloat16)
        flipped = (
            conv_weight[layer_num]
            .reshape(27, channels, channels)
            .transpose(0, 2, 1)
            .reshape(27 * channels, channels)
        )
        backward = apply_offsets(
            with_rim(slope_grad), flipped, dilation[layer_num], -1, field.shape
        )
        grid_grad = (grid_grad.astype(jnp.float32) + backward).astype(jnp.bfloat16)
    return grid_grad.transpose(0, 2, 1, 3)


def solution(mesh):
    return jax.shard_map(
        local,
        mesh=mesh,
        in_specs=(
            P("blk", None, "zslab", None),
            P("blk", None, "zslab"),
            P(),
            P(),
            P("zslab", "blk", None),
            P(None, "blk", "zslab"),
            P("blk", "zslab"),
        ),
        out_specs=P("blk", None, "zslab", None),
        check_vma=False,
    )
```

```python
import jax
import jax.numpy as jnp
from jax import lax
from jax.sharding import PartitionSpec as P

HD = 128
PY = 8
PZ = 2
LAYERS = 2
DMAX = 2


def padded_2(cells, sides, width):
    for axis, dim in sides:
        count = lax.axis_size(axis)
        ends = count - 1
        head = lax.slice_in_dim(cells, 0, width, axis=dim)
        tail = lax.slice_in_dim(cells, cells.shape[dim] - width, cells.shape[dim], axis=dim)
        cells = jnp.concatenate(
            [
                lax.ppermute(tail, axis, [(i, (i + 1) % count) for i in range(ends)]),
                cells,
                lax.ppermute(head, axis, [((i + 1) % count, i) for i in range(ends)]),
            ],
            axis=dim,
        )
    return cells


def copy_for_each(shard, axis):
    peers = lax.axis_size(axis)
    return lax.all_to_all(
        jnp.broadcast_to(shard[None], (peers, *shard.shape)), axis, 0, 0, tiled=True
    )


def taken_together(shard, axis):
    return copy_for_each(shard, axis).astype(jnp.float32).sum(axis=0)


def joined_along(pieces, dim):
    shape = list(pieces.shape[1:])
    shape[dim] *= pieces.shape[0]
    return jnp.moveaxis(pieces, 0, dim).reshape(shape)


def gather_together(arrays, axis, dims):
    line = jnp.concatenate([a.reshape(-1) for a in arrays])
    lines, at, finished = (lax.all_gather(line, axis), 0, [])
    for a, dim in zip(arrays, dims):
        pieces = lines[:, at : at + a.size].reshape(-1, *a.shape)
        finished.append(joined_along(pieces, dim))
        at += a.size
    return tuple(finished)


def side_by_side(arrays, axis, dim, along):
    ends, at = ([], 0)
    for a in arrays[:-1]:
        at += a.shape[along]
        ends.append(at)
    both = jnp.concatenate(arrays, axis=along)
    return tuple(jnp.split(lax.all_gather(both, axis, axis=dim, tiled=True), ends, axis=along))


def cut_along(shard, dim, peers):
    before, after = (shard.shape[:dim], shard.shape[dim + 1 :])
    return jnp.moveaxis(shard.reshape(*before, peers, -1, *after), dim, 0)


def sum_at_owner(shard, axis, dim):
    peers = lax.axis_size(axis)
    pieces = lax.all_to_all(cut_along(shard, dim, peers), axis, 0, 0, tiled=True)
    return jnp.sum(pieces.astype(jnp.float32), axis=0)


def gathered_near_then_far(rows, axis):
    peers = lax.axis_size(axis)
    near = [list(range(start, start + 4)) for start in range(0, peers, 4)]
    far = [list(range(start, peers, 4)) for start in range(4)]
    rows = lax.all_gather(rows, axis, axis=0, tiled=True, axis_index_groups=near)
    copies = jnp.broadcast_to(rows[None], (len(far[0]), *rows.shape))
    copies = lax.all_to_all(copies, axis, 0, 0, tiled=True, axis_index_groups=far)
    return copies.reshape(-1, *rows.shape[1:])


def gather_weights(embed_weight, qkv_weight):
    _, feat, width = embed_weight.shape
    qkv_flat = qkv_weight.reshape(-1, width)
    extra = -qkv_flat.shape[0] % 16
    rows = jnp.concatenate(
        [embed_weight[0], qkv_flat, jnp.zeros((extra, width), qkv_flat.dtype)], axis=0
    )
    peers = lax.axis_size("blk")
    near = [list(range(start, start + 4)) for start in range(0, peers, 4)]
    far = [list(range(start, peers, 4)) for start in range(4)]
    gathered = lax.all_gather(rows, "blk", axis=0, tiled=True, axis_index_groups=near)
    gathered = lax.all_gather(gathered, "blk", axis=0, tiled=True, axis_index_groups=far)
    gathered = gathered.reshape(peers, rows.shape[0], width)
    embed_rows = gathered[:, :feat, :]
    qkv_rows = gathered[:, feat : feat + qkv_flat.shape[0], :].reshape(peers, *qkv_weight.shape)
    qkv_rows = jnp.moveaxis(qkv_rows, 0, 1).reshape(
        qkv_weight.shape[0], peers * qkv_weight.shape[1], qkv_weight.shape[2]
    )
    return embed_rows, qkv_rows


def with_rim(volume):
    return padded_2(volume, (("zslab", 1), ("blk", 0)), DMAX)


def picked(cells, dim, step, rate, size):
    near = lax.slice_in_dim(cells, DMAX + step, DMAX + step + size, axis=dim)
    if step == 0:
        return near
    far = lax.slice_in_dim(cells, DMAX + 2 * step, DMAX + 2 * step + size, axis=dim)
    return jnp.where(rate == 1, near, far)


def shifted_y(values, step, rate):
    def by(amount):
        cells = values.shape[2]
        zeros = jnp.zeros_like(values[:, :, : abs(amount)])
        if amount > 0:
            return jnp.concatenate([values[:, :, amount:], zeros], axis=2)
        return jnp.concatenate([zeros, values[:, :, : cells + amount]], axis=2)

    if step == 0:
        return values
    return jnp.where(rate == 1, by(step), by(2 * step))


def apply_offsets(padded, weight, dilate, direction, dims_out):
    x_cells, z_cells, y_cells, channels = dims_out
    windows = []
    for offset_x in (-1, 0, 1):
        along_x = picked(padded, 0, direction * offset_x, dilate[0], x_cells)
        for offset_z in (-1, 0, 1):
            windows.append(picked(along_x, 1, direction * offset_z, dilate[2], z_cells))
    stacked = jnp.concatenate(windows, axis=3).reshape(x_cells * z_cells * y_cells, 9 * channels)
    taps = weight.reshape(3, 3, 3, channels, -1)
    summed = None
    for offset_y in (-1, 0, 1):
        rows = taps[:, offset_y + 1].reshape(9 * channels, -1)
        part = jnp.dot(stacked, rows, preferred_element_type=jnp.float32)
        part = shifted_y(part.reshape(x_cells, z_cells, y_cells, -1), direction * offset_y, dilate[1])
        summed = part if summed is None else summed + part
    return summed


def slab_total(term):
    return taken_together(term.astype(jnp.bfloat16), "zslab").astype(jnp.float32)


def local(field, fracture_mask, dilation, conv_weight, embed_weight, qkv_weight, out_grad):
    field = field.transpose(0, 2, 1, 3)
    fracture_mask = fracture_mask.transpose(0, 2, 1)
    x_cells, z_cells, y_cells, channels = field.shape
    gate_mask = fracture_mask.astype(jnp.float32)[..., None]
    hidden = field
    conv_outs = []
    for layer_num in range(LAYERS):
        conv_out = apply_offsets(
            with_rim(hidden), conv_weight[layer_num], dilation[layer_num], 1, field.shape
        )
        conv_outs.append(conv_out)
        hidden = (
            hidden.astype(jnp.float32) + gate_mask * (conv_out * jax.nn.sigmoid(conv_out))
        ).astype(jnp.bfloat16)
    slab_view = lax.all_to_all(hidden, "zslab", split_axis=0, concat_axis=1, tiled=True)
    x_local, z_total = (slab_view.shape[0], slab_view.shape[1])
    y_blocks, z_blocks = (y_cells // PY, z_total // PZ)
    patches = slab_view.reshape(x_local, z_blocks, PZ, y_blocks, PY, channels).transpose(
        3, 1, 0, 4, 2, 5
    )
    patches = patches.reshape(y_blocks * z_blocks, x_local, PY * PZ * channels)
    embed_rows, qkv_rows = gather_weights(embed_weight, qkv_weight)
    patches = patches.reshape(patches.shape[0], embed_rows.shape[0], embed_rows.shape[1])
    partial_value = jnp.einsum(
        "tbf,bfd->td", patches, embed_rows, preferred_element_type=jnp.float32
    )
    tokens = slab_total(partial_value).astype(jnp.bfloat16)
    projected = jnp.einsum(
        "td,sde->ste", tokens, qkv_rows, preferred_element_type=jnp.float32
    ).astype(jnp.bfloat16)
    key_rows, value_rows = jnp.split(
        gathered_near_then_far(jnp.concatenate([projected[1], projected[2]], axis=1), "blk"), 2, axis=1
    )
    tok_rows = tokens.shape[0]
    head_cols = projected.shape[2]
    heads_here = head_cols // HD
    inv_root = HD ** (-0.5)
    queries = projected[0].reshape(tok_rows, heads_here, HD)
    key_all = key_rows.reshape(-1, heads_here, HD)
    value_all = value_rows.reshape(-1, heads_here, HD)
    grad_out = out_grad.reshape(tok_rows, heads_here, HD)
    scores = (
        jnp.einsum("qhd,khd->hqk", queries, key_all, preferred_element_type=jnp.float32) * inv_root
    )
    top_score = jnp.max(scores, axis=2, keepdims=True)
    expo = jnp.exp(scores - top_score)
    total = jnp.sum(expo, axis=2, keepdims=True)
    probs = expo / total
    probs_b = probs.astype(jnp.bfloat16)
    attended = jnp.einsum("hqk,khd->qhd", probs_b, value_all, preferred_element_type=jnp.float32)
    row_delta = jnp.sum(grad_out.astype(jnp.float32) * attended, axis=2).T[:, :, None]
    score_grad = jnp.einsum("qhd,khd->hqk", grad_out, value_all, preferred_element_type=jnp.float32)
    dscore = (probs * (score_grad - row_delta) * inv_root).astype(jnp.bfloat16)
    grad_query = jnp.einsum("hqk,khd->qhd", dscore, key_all, preferred_element_type=jnp.float32)
    grad_query = grad_query.astype(jnp.bfloat16).reshape(tok_rows, head_cols)
    key_term = jnp.einsum("hqk,qhd->khd", dscore, queries, preferred_element_type=jnp.float32)
    value_term = jnp.einsum("hqk,qhd->khd", probs_b, grad_out, preferred_element_type=jnp.float32)
    key_value_grad = sum_at_owner(
        jnp.concatenate(
            [
                key_term.reshape(tok_rows * lax.axis_size("blk"), head_cols),
                value_term.reshape(tok_rows * lax.axis_size("blk"), head_cols),
            ],
            axis=1,
        ).astype(jnp.bfloat16),
        "blk",
        0,
    ).astype(jnp.bfloat16)
    grad_key = key_value_grad[:, :head_cols]
    grad_value = key_value_grad[:, head_cols:]
    stacked_grads = jnp.stack([grad_query, grad_key, grad_value])
    partial_grad = jnp.einsum(
        "ste,sde->td", stacked_grads, qkv_rows, preferred_element_type=jnp.float32
    )
    grad_tokens = slab_total(partial_grad).astype(jnp.bfloat16)
    patch_grad = jnp.einsum(
        "td,bfd->tbf", grad_tokens, embed_rows, preferred_element_type=jnp.float32
    ).astype(jnp.bfloat16)
    grid_grad = patch_grad.reshape(y_blocks, z_blocks, x_local, PY, PZ, channels).transpose(
        2, 1, 4, 0, 3, 5
    )
    grid_grad = grid_grad.reshape(x_local, z_total, y_cells, channels)
    grid_grad = lax.all_to_all(grid_grad, "zslab", split_axis=1, concat_axis=0, tiled=True)
    for layer_num in reversed(range(LAYERS)):
        conv_out = conv_outs[layer_num]
        sigma = jax.nn.sigmoid(conv_out)
        slope_grad = (
            gate_mask * sigma * (1.0 + conv_out * (1.0 - sigma)) * grid_grad.astype(jnp.float32)
        ).astype(jnp.bfloat16)
        flipped = (
            conv_weight[layer_num]
            .reshape(27, channels, channels)
            .transpose(0, 2, 1)
            .reshape(27 * channels, channels)
        )
        backward = apply_offsets(
            with_rim(slope_grad), flipped, dilation[layer_num], -1, field.shape
        )
        grid_grad = (grid_grad.astype(jnp.float32) + backward).astype(jnp.bfloat16)
    return grid_grad.transpose(0, 2, 1, 3)


def solution(mesh):
    return jax.shard_map(
        local,
        mesh=mesh,
        in_specs=(
            P("blk", None, "zslab", None),
            P("blk", None, "zslab"),
            P(),
            P(),
            P("zslab", "blk", None),
            P(None, "blk", "zslab"),
            P("blk", "zslab"),
        ),
        out_specs=P("blk", None, "zslab", None),
        check_vma=False,
    )
```

```python
import jax
import jax.numpy as jnp
from jax import lax
from jax.sharding import PartitionSpec as P

HD = 128
PY = 8
PZ = 2
LAYERS = 2
DMAX = 2


def padded_2(cells, sides, width):
    for axis, dim in sides:
        count = lax.axis_size(axis)
        ends = count - 1
        head = lax.slice_in_dim(cells, 0, width, axis=dim)
        tail = lax.slice_in_dim(cells, cells.shape[dim] - width, cells.shape[dim], axis=dim)
        cells = jnp.concatenate(
            [
                lax.ppermute(tail, axis, [(i, (i + 1) % count) for i in range(ends)]),
                cells,
                lax.ppermute(head, axis, [((i + 1) % count, i) for i in range(ends)]),
            ],
            axis=dim,
        )
    return cells


def copy_for_each(shard, axis):
    peers = lax.axis_size(axis)
    return lax.all_to_all(
        jnp.broadcast_to(shard[None], (peers, *shard.shape)), axis, 0, 0, tiled=True
    )


def taken_together(shard, axis):
    return copy_for_each(shard, axis).astype(jnp.float32).sum(axis=0)


def joined_along(pieces, dim):
    shape = list(pieces.shape[1:])
    shape[dim] *= pieces.shape[0]
    return jnp.moveaxis(pieces, 0, dim).reshape(shape)


def gather_together(arrays, axis, dims):
    line = jnp.concatenate([a.reshape(-1) for a in arrays])
    lines, at, finished = (lax.all_gather(line, axis), 0, [])
    for a, dim in zip(arrays, dims):
        pieces = lines[:, at : at + a.size].reshape(-1, *a.shape)
        finished.append(joined_along(pieces, dim))
        at += a.size
    return tuple(finished)


def side_by_side(arrays, axis, dim, along):
    ends, at = ([], 0)
    for a in arrays[:-1]:
        at += a.shape[along]
        ends.append(at)
    both = jnp.concatenate(arrays, axis=along)
    return tuple(jnp.split(lax.all_gather(both, axis, axis=dim, tiled=True), ends, axis=along))


def cut_along(shard, dim, peers):
    before, after = (shard.shape[:dim], shard.shape[dim + 1 :])
    return jnp.moveaxis(shard.reshape(*before, peers, -1, *after), dim, 0)


def sum_at_owner(shard, axis, dim):
    peers = lax.axis_size(axis)
    pieces = lax.all_to_all(cut_along(shard, dim, peers), axis, 0, 0, tiled=True)
    return jnp.sum(pieces.astype(jnp.float32), axis=0)


def gather_weights(embed_weight, qkv_weight):
    _, feat, width = embed_weight.shape
    qkv_flat = qkv_weight.reshape(-1, width)
    extra = -qkv_flat.shape[0] % 16
    rows = jnp.concatenate(
        [embed_weight[0], qkv_flat, jnp.zeros((extra, width), qkv_flat.dtype)], axis=0
    )
    peers = lax.axis_size("blk")
    near = [list(range(start, start + 8)) for start in range(0, peers, 8)]
    far = [list(range(start, peers, 8)) for start in range(8)]
    gathered = lax.all_gather(rows, "blk", axis=0, tiled=True, axis_index_groups=near)
    gathered = lax.all_gather(gathered, "blk", axis=0, tiled=True, axis_index_groups=far)
    gathered = gathered.reshape(peers, rows.shape[0], width)
    embed_rows = gathered[:, :feat, :]
    qkv_rows = gathered[:, feat : feat + qkv_flat.shape[0], :].reshape(peers, *qkv_weight.shape)
    qkv_rows = jnp.moveaxis(qkv_rows, 0, 1).reshape(
        qkv_weight.shape[0], peers * qkv_weight.shape[1], qkv_weight.shape[2]
    )
    return embed_rows, qkv_rows


def with_rim(volume):
    return padded_2(volume, (("zslab", 1), ("blk", 0)), DMAX)


def picked(cells, dim, step, rate, size):
    near = lax.slice_in_dim(cells, DMAX + step, DMAX + step + size, axis=dim)
    if step == 0:
        return near
    far = lax.slice_in_dim(cells, DMAX + 2 * step, DMAX + 2 * step + size, axis=dim)
    return jnp.where(rate == 1, near, far)


def shifted_y(values, step, rate):
    def by(amount):
        cells = values.shape[2]
        zeros = jnp.zeros_like(values[:, :, : abs(amount)])
        if amount > 0:
            return jnp.concatenate([values[:, :, amount:], zeros], axis=2)
        return jnp.concatenate([zeros, values[:, :, : cells + amount]], axis=2)

    if step == 0:
        return values
    return jnp.where(rate == 1, by(step), by(2 * step))


def apply_offsets(padded, weight, dilate, direction, dims_out):
    x_cells, z_cells, y_cells, channels = dims_out
    windows = []
    for offset_x in (-1, 0, 1):
        along_x = picked(padded, 0, direction * offset_x, dilate[0], x_cells)
        for offset_z in (-1, 0, 1):
            windows.append(picked(along_x, 1, direction * offset_z, dilate[2], z_cells))
    stacked = jnp.concatenate(windows, axis=3).reshape(x_cells * z_cells * y_cells, 9 * channels)
    taps = weight.reshape(3, 3, 3, channels, -1)
    summed = None
    for offset_y in (-1, 0, 1):
        rows = taps[:, offset_y + 1].reshape(9 * channels, -1)
        part = jnp.dot(stacked, rows, preferred_element_type=jnp.float32)
        part = shifted_y(part.reshape(x_cells, z_cells, y_cells, -1), direction * offset_y, dilate[1])
        summed = part if summed is None else summed + part
    return summed


def slab_total(term):
    return taken_together(term.astype(jnp.bfloat16), "zslab").astype(jnp.float32)


def local(field, fracture_mask, dilation, conv_weight, embed_weight, qkv_weight, out_grad):
    field = field.transpose(0, 2, 1, 3)
    fracture_mask = fracture_mask.transpose(0, 2, 1)
    x_cells, z_cells, y_cells, channels = field.shape
    gate_mask = fracture_mask.astype(jnp.float32)[..., None]
    hidden = field
    conv_outs = []
    for layer_num in range(LAYERS):
        conv_out = apply_offsets(
            with_rim(hidden), conv_weight[layer_num], dilation[layer_num], 1, field.shape
        )
        conv_outs.append(conv_out)
        hidden = (
            hidden.astype(jnp.float32) + gate_mask * (conv_out * jax.nn.sigmoid(conv_out))
        ).astype(jnp.bfloat16)
    slab_view = lax.all_to_all(hidden, "zslab", split_axis=0, concat_axis=1, tiled=True)
    x_local, z_total = (slab_view.shape[0], slab_view.shape[1])
    y_blocks, z_blocks = (y_cells // PY, z_total // PZ)
    patches = slab_view.reshape(x_local, z_blocks, PZ, y_blocks, PY, channels).transpose(
        3, 1, 0, 4, 2, 5
    )
    patches = patches.reshape(y_blocks * z_blocks, x_local, PY * PZ * channels)
    embed_rows, qkv_rows = gather_weights(embed_weight, qkv_weight)
    patches = patches.reshape(patches.shape[0], embed_rows.shape[0], embed_rows.shape[1])
    partial_value = jnp.einsum(
        "tbf,bfd->td", patches, embed_rows, preferred_element_type=jnp.float32
    )
    tokens = slab_total(partial_value).astype(jnp.bfloat16)
    projected = jnp.einsum(
        "td,sde->ste", tokens, qkv_rows, preferred_element_type=jnp.float32
    ).astype(jnp.bfloat16)
    key_rows, value_rows = jnp.split(
        joined_along(copy_for_each(jnp.concatenate([projected[1], projected[2]], axis=1), "blk"), 0),
        2,
        axis=1,
    )
    tok_rows = tokens.shape[0]
    head_cols = projected.shape[2]
    heads_here = head_cols // HD
    inv_root = HD ** (-0.5)
    queries = projected[0].reshape(tok_rows, heads_here, HD)
    key_all = key_rows.reshape(-1, heads_here, HD)
    value_all = value_rows.reshape(-1, heads_here, HD)
    grad_out = out_grad.reshape(tok_rows, heads_here, HD)
    scores = (
        jnp.einsum("qhd,khd->hqk", queries, key_all, preferred_element_type=jnp.float32) * inv_root
    )
    top_score = jnp.max(scores, axis=2, keepdims=True)
    expo = jnp.exp(scores - top_score)
    total = jnp.sum(expo, axis=2, keepdims=True)
    probs = expo / total
    probs_b = probs.astype(jnp.bfloat16)
    attended = jnp.einsum("hqk,khd->qhd", probs_b, value_all, preferred_element_type=jnp.float32)
    row_delta = jnp.sum(grad_out.astype(jnp.float32) * attended, axis=2).T[:, :, None]
    score_grad = jnp.einsum("qhd,khd->hqk", grad_out, value_all, preferred_element_type=jnp.float32)
    dscore = (probs * (score_grad - row_delta) * inv_root).astype(jnp.bfloat16)
    grad_query = jnp.einsum("hqk,khd->qhd", dscore, key_all, preferred_element_type=jnp.float32)
    grad_query = grad_query.astype(jnp.bfloat16).reshape(tok_rows, head_cols)
    key_term = jnp.einsum("hqk,qhd->khd", dscore, queries, preferred_element_type=jnp.float32)
    value_term = jnp.einsum("hqk,qhd->khd", probs_b, grad_out, preferred_element_type=jnp.float32)
    key_value_grad = sum_at_owner(
        jnp.concatenate(
            [
                key_term.reshape(tok_rows * lax.axis_size("blk"), head_cols),
                value_term.reshape(tok_rows * lax.axis_size("blk"), head_cols),
            ],
            axis=1,
        ).astype(jnp.bfloat16),
        "blk",
        0,
    ).astype(jnp.bfloat16)
    grad_key = key_value_grad[:, :head_cols]
    grad_value = key_value_grad[:, head_cols:]
    stacked_grads = jnp.stack([grad_query, grad_key, grad_value])
    partial_grad = jnp.einsum(
        "ste,sde->td", stacked_grads, qkv_rows, preferred_element_type=jnp.float32
    )
    grad_tokens = slab_total(partial_grad).astype(jnp.bfloat16)
    patch_grad = jnp.einsum(
        "td,bfd->tbf", grad_tokens, embed_rows, preferred_element_type=jnp.float32
    ).astype(jnp.bfloat16)
    grid_grad = patch_grad.reshape(y_blocks, z_blocks, x_local, PY, PZ, channels).transpose(
        2, 1, 4, 0, 3, 5
    )
    grid_grad = grid_grad.reshape(x_local, z_total, y_cells, channels)
    grid_grad = lax.all_to_all(grid_grad, "zslab", split_axis=1, concat_axis=0, tiled=True)
    for layer_num in reversed(range(LAYERS)):
        conv_out = conv_outs[layer_num]
        sigma = jax.nn.sigmoid(conv_out)
        slope_grad = (
            gate_mask * sigma * (1.0 + conv_out * (1.0 - sigma)) * grid_grad.astype(jnp.float32)
        ).astype(jnp.bfloat16)
        flipped = (
            conv_weight[layer_num]
            .reshape(27, channels, channels)
            .transpose(0, 2, 1)
            .reshape(27 * channels, channels)
        )
        backward = apply_offsets(
            with_rim(slope_grad), flipped, dilation[layer_num], -1, field.shape
        )
        grid_grad = (grid_grad.astype(jnp.float32) + backward).astype(jnp.bfloat16)
    return grid_grad.transpose(0, 2, 1, 3)


def solution(mesh):
    return jax.shard_map(
        local,
        mesh=mesh,
        in_specs=(
            P("blk", None, "zslab", None),
            P("blk", None, "zslab"),
            P(),
            P(),
            P("zslab", "blk", None),
            P(None, "blk", "zslab"),
            P("blk", "zslab"),
        ),
        out_specs=P("blk", None, "zslab", None),
        check_vma=False,
    )
```

```python
import jax
import jax.numpy as jnp
from jax import lax
from jax.sharding import PartitionSpec as P

HD = 128
PY = 8
PZ = 2
LAYERS = 2
DMAX = 2


def padded_2(cells, sides, width):
    for axis, dim in sides:
        count = lax.axis_size(axis)
        ends = count - 1
        head = lax.slice_in_dim(cells, 0, width, axis=dim)
        tail = lax.slice_in_dim(cells, cells.shape[dim] - width, cells.shape[dim], axis=dim)
        cells = jnp.concatenate(
            [
                lax.ppermute(tail, axis, [(i, (i + 1) % count) for i in range(ends)]),
                cells,
                lax.ppermute(head, axis, [((i + 1) % count, i) for i in range(ends)]),
            ],
            axis=dim,
        )
    return cells


def copy_for_each(shard, axis):
    peers = lax.axis_size(axis)
    return lax.all_to_all(
        jnp.broadcast_to(shard[None], (peers, *shard.shape)), axis, 0, 0, tiled=True
    )


def taken_together(shard, axis):
    return copy_for_each(shard, axis).astype(jnp.float32).sum(axis=0)


def joined_along(pieces, dim):
    shape = list(pieces.shape[1:])
    shape[dim] *= pieces.shape[0]
    return jnp.moveaxis(pieces, 0, dim).reshape(shape)


def gather_together(arrays, axis, dims):
    line = jnp.concatenate([a.reshape(-1) for a in arrays])
    lines, at, finished = (lax.all_gather(line, axis), 0, [])
    for a, dim in zip(arrays, dims):
        pieces = lines[:, at : at + a.size].reshape(-1, *a.shape)
        finished.append(joined_along(pieces, dim))
        at += a.size
    return tuple(finished)


def side_by_side(arrays, axis, dim, along):
    ends, at = ([], 0)
    for a in arrays[:-1]:
        at += a.shape[along]
        ends.append(at)
    both = jnp.concatenate(arrays, axis=along)
    return tuple(jnp.split(lax.all_gather(both, axis, axis=dim, tiled=True), ends, axis=along))


def cut_along(shard, dim, peers):
    before, after = (shard.shape[:dim], shard.shape[dim + 1 :])
    return jnp.moveaxis(shard.reshape(*before, peers, -1, *after), dim, 0)


def sum_at_owner(shard, axis, dim):
    peers = lax.axis_size(axis)
    pieces = lax.all_to_all(cut_along(shard, dim, peers), axis, 0, 0, tiled=True)
    return jnp.sum(pieces.astype(jnp.float32), axis=0)


def gather_weights(embed_weight, qkv_weight):
    _, feat, width = embed_weight.shape
    qkv_flat = qkv_weight.reshape(-1, width)
    extra = -qkv_flat.shape[0] % 16
    rows = jnp.concatenate(
        [embed_weight[0], qkv_flat, jnp.zeros((extra, width), qkv_flat.dtype)], axis=0
    )
    peers = lax.axis_size("blk")
    near = [list(range(start, start + 4)) for start in range(0, peers, 4)]
    far = [list(range(start, peers, 4)) for start in range(4)]
    gathered = lax.all_gather(rows, "blk", axis=0, tiled=True, axis_index_groups=near)
    gathered = lax.all_gather(gathered, "blk", axis=0, tiled=True, axis_index_groups=far)
    gathered = gathered.reshape(peers, rows.shape[0], width)
    embed_rows = gathered[:, :feat, :]
    qkv_rows = gathered[:, feat : feat + qkv_flat.shape[0], :].reshape(peers, *qkv_weight.shape)
    qkv_rows = jnp.moveaxis(qkv_rows, 0, 1).reshape(
        qkv_weight.shape[0], peers * qkv_weight.shape[1], qkv_weight.shape[2]
    )
    return embed_rows, qkv_rows


def with_rim(volume):
    return padded_2(volume, (("zslab", 1), ("blk", 0)), DMAX)


def picked(cells, dim, step, rate, size):
    near = lax.slice_in_dim(cells, DMAX + step, DMAX + step + size, axis=dim)
    if step == 0:
        return near
    far = lax.slice_in_dim(cells, DMAX + 2 * step, DMAX + 2 * step + size, axis=dim)
    return jnp.where(rate == 1, near, far)


def shifted_y(values, step, rate):
    def by(amount):
        cells = values.shape[2]
        zeros = jnp.zeros_like(values[:, :, : abs(amount)])
        if amount > 0:
            return jnp.concatenate([values[:, :, amount:], zeros], axis=2)
        return jnp.concatenate([zeros, values[:, :, : cells + amount]], axis=2)

    if step == 0:
        return values
    return jnp.where(rate == 1, by(step), by(2 * step))


def apply_offsets(padded, weight, dilate, direction, dims_out):
    x_cells, z_cells, y_cells, channels = dims_out
    windows = []
    for offset_x in (-1, 0, 1):
        along_x = picked(padded, 0, direction * offset_x, dilate[0], x_cells)
        for offset_z in (-1, 0, 1):
            windows.append(picked(along_x, 1, direction * offset_z, dilate[2], z_cells))
    stacked = jnp.concatenate(windows, axis=3).reshape(x_cells * z_cells * y_cells, 9 * channels)
    taps = weight.reshape(3, 3, 3, channels, -1)
    summed = None
    for offset_y in (-1, 0, 1):
        rows = taps[:, offset_y + 1].reshape(9 * channels, -1)
        part = jnp.dot(stacked, rows, preferred_element_type=jnp.float32)
        part = shifted_y(part.reshape(x_cells, z_cells, y_cells, -1), direction * offset_y, dilate[1])
        summed = part if summed is None else summed + part
    return summed


def slab_total(term):
    return taken_together(term.astype(jnp.bfloat16), "zslab").astype(jnp.float32)


def local(field, fracture_mask, dilation, conv_weight, embed_weight, qkv_weight, out_grad):
    field = field.transpose(0, 2, 1, 3)
    fracture_mask = fracture_mask.transpose(0, 2, 1)
    x_cells, z_cells, y_cells, channels = field.shape
    gate_mask = fracture_mask.astype(jnp.float32)[..., None]
    hidden = field
    conv_outs = []
    for layer_num in range(LAYERS):
        conv_out = apply_offsets(
            with_rim(hidden), conv_weight[layer_num], dilation[layer_num], 1, field.shape
        )
        conv_outs.append(conv_out)
        hidden = (
            hidden.astype(jnp.float32) + gate_mask * (conv_out * jax.nn.sigmoid(conv_out))
        ).astype(jnp.bfloat16)
    sigma = jax.nn.sigmoid(conv_outs[-1])
    slope = gate_mask * sigma * (1.0 + conv_outs[-1] * (1.0 - sigma))
    rim = padded_2(slope.astype(jnp.bfloat16), (("zslab", 1),), DMAX).astype(jnp.float32)
    slope = jnp.concatenate([rim[:, :DMAX], slope, rim[:, -DMAX:]], axis=1)
    hidden, slope = lax.optimization_barrier((hidden, slope))
    slab_view = lax.all_to_all(hidden, "zslab", split_axis=0, concat_axis=1, tiled=True)
    x_local, z_total = (slab_view.shape[0], slab_view.shape[1])
    y_blocks, z_blocks = (y_cells // PY, z_total // PZ)
    patches = slab_view.reshape(x_local, z_blocks, PZ, y_blocks, PY, channels).transpose(
        3, 1, 0, 4, 2, 5
    )
    patches = patches.reshape(y_blocks * z_blocks, x_local, PY * PZ * channels)
    embed_rows, qkv_rows = gather_weights(embed_weight, qkv_weight)
    patches = patches.reshape(patches.shape[0], embed_rows.shape[0], embed_rows.shape[1])
    partial_value = jnp.einsum(
        "tbf,bfd->td", patches, embed_rows, preferred_element_type=jnp.float32
    )
    tokens = slab_total(partial_value).astype(jnp.bfloat16)
    projected = jnp.einsum(
        "td,sde->ste", tokens, qkv_rows, preferred_element_type=jnp.float32
    ).astype(jnp.bfloat16)
    key_rows, value_rows = jnp.split(
        joined_along(copy_for_each(jnp.concatenate([projected[1], projected[2]], axis=1), "blk"), 0),
        2,
        axis=1,
    )
    tok_rows = tokens.shape[0]
    head_cols = projected.shape[2]
    heads_here = head_cols // HD
    inv_root = HD ** (-0.5)
    queries = projected[0].reshape(tok_rows, heads_here, HD)
    key_all = key_rows.reshape(-1, heads_here, HD)
    value_all = value_rows.reshape(-1, heads_here, HD)
    grad_out = out_grad.reshape(tok_rows, heads_here, HD)
    scores = (
        jnp.einsum("qhd,khd->hqk", queries, key_all, preferred_element_type=jnp.float32) * inv_root
    )
    top_score = jnp.max(scores, axis=2, keepdims=True)
    expo = jnp.exp(scores - top_score)
    total = jnp.sum(expo, axis=2, keepdims=True)
    probs = expo / total
    probs_b = probs.astype(jnp.bfloat16)
    attended = jnp.einsum("hqk,khd->qhd", probs_b, value_all, preferred_element_type=jnp.float32)
    row_delta = jnp.sum(grad_out.astype(jnp.float32) * attended, axis=2).T[:, :, None]
    score_grad = jnp.einsum("qhd,khd->hqk", grad_out, value_all, preferred_element_type=jnp.float32)
    dscore = (probs * (score_grad - row_delta) * inv_root).astype(jnp.bfloat16)
    grad_query = jnp.einsum("hqk,khd->qhd", dscore, key_all, preferred_element_type=jnp.float32)
    grad_query = grad_query.astype(jnp.bfloat16).reshape(tok_rows, head_cols)
    key_term = jnp.einsum("hqk,qhd->khd", dscore, queries, preferred_element_type=jnp.float32)
    value_term = jnp.einsum("hqk,qhd->khd", probs_b, grad_out, preferred_element_type=jnp.float32)
    key_value_grad = sum_at_owner(
        jnp.concatenate(
            [
                key_term.reshape(tok_rows * lax.axis_size("blk"), head_cols),
                value_term.reshape(tok_rows * lax.axis_size("blk"), head_cols),
            ],
            axis=1,
        ).astype(jnp.bfloat16),
        "blk",
        0,
    ).astype(jnp.bfloat16)
    grad_key = key_value_grad[:, :head_cols]
    grad_value = key_value_grad[:, head_cols:]
    stacked_grads = jnp.stack([grad_query, grad_key, grad_value])
    partial_grad = jnp.einsum(
        "ste,sde->td", stacked_grads, qkv_rows, preferred_element_type=jnp.float32
    )
    grad_tokens = slab_total(partial_grad).astype(jnp.bfloat16)
    patch_grad = jnp.einsum(
        "td,bfd->tbf", grad_tokens, embed_rows, preferred_element_type=jnp.float32
    ).astype(jnp.bfloat16)
    grid_grad = patch_grad.reshape(y_blocks, z_blocks, x_local, PY, PZ, channels).transpose(
        2, 1, 4, 0, 3, 5
    )
    grid_grad = grid_grad.reshape(x_local, z_total, y_cells, channels)
    slabs = lax.axis_size("zslab")
    grid_grad = jnp.pad(grid_grad, ((0, 0), (DMAX, DMAX), (0, 0), (0, 0)))
    grid_grad = jnp.stack(
        [grid_grad[:, k * z_cells : (k + 1) * z_cells + 2 * DMAX] for k in range(slabs)]
    )
    wide_grad = lax.all_to_all(grid_grad, "zslab", split_axis=0, concat_axis=1, tiled=True)
    wide_grad = wide_grad.reshape(x_cells, z_cells + 2 * DMAX, y_cells, channels)
    grid_grad = wide_grad[:, DMAX : DMAX + z_cells]
    for layer_num in reversed(range(LAYERS)):
        conv_out = conv_outs[layer_num]
        sigma = jax.nn.sigmoid(conv_out)
        if layer_num == LAYERS - 1:
            slope_grad = (slope * wide_grad.astype(jnp.float32)).astype(jnp.bfloat16)
            padded = padded_2(slope_grad, (("blk", 0),), DMAX)
        else:
            slope_grad = (
                gate_mask * sigma * (1.0 + conv_out * (1.0 - sigma)) * grid_grad.astype(jnp.float32)
            ).astype(jnp.bfloat16)
            padded = with_rim(slope_grad)
        flipped = (
            conv_weight[layer_num]
            .reshape(27, channels, channels)
            .transpose(0, 2, 1)
            .reshape(27 * channels, channels)
        )
        backward = apply_offsets(padded, flipped, dilation[layer_num], -1, field.shape)
        grid_grad = (grid_grad.astype(jnp.float32) + backward).astype(jnp.bfloat16)
    return grid_grad.transpose(0, 2, 1, 3)


def solution(mesh):
    return jax.shard_map(
        local,
        mesh=mesh,
        in_specs=(
            P("blk", None, "zslab", None),
            P("blk", None, "zslab"),
            P(),
            P(),
            P("zslab", "blk", None),
            P(None, "blk", "zslab"),
            P("blk", "zslab"),
        ),
        out_specs=P("blk", None, "zslab", None),
        check_vma=False,
    )
```

```python
import jax
import jax.numpy as jnp
from jax import lax
from jax.sharding import PartitionSpec as P

HD = 128
PY = 8
PZ = 2
LAYERS = 2
DMAX = 2


def padded_2(cells, sides, width):
    for axis, dim in sides:
        count = lax.axis_size(axis)
        ends = count - 1
        head = lax.slice_in_dim(cells, 0, width, axis=dim)
        tail = lax.slice_in_dim(cells, cells.shape[dim] - width, cells.shape[dim], axis=dim)
        cells = jnp.concatenate(
            [
                lax.ppermute(tail, axis, [(i, (i + 1) % count) for i in range(ends)]),
                cells,
                lax.ppermute(head, axis, [((i + 1) % count, i) for i in range(ends)]),
            ],
            axis=dim,
        )
    return cells


def copy_for_each(shard, axis):
    peers = lax.axis_size(axis)
    return lax.all_to_all(
        jnp.broadcast_to(shard[None], (peers, *shard.shape)), axis, 0, 0, tiled=True
    )


def taken_together(shard, axis):
    return copy_for_each(shard, axis).astype(jnp.float32).sum(axis=0)


def joined_along(pieces, dim):
    shape = list(pieces.shape[1:])
    shape[dim] *= pieces.shape[0]
    return jnp.moveaxis(pieces, 0, dim).reshape(shape)


def gather_together(arrays, axis, dims):
    line = jnp.concatenate([a.reshape(-1) for a in arrays])
    lines, at, finished = (lax.all_gather(line, axis), 0, [])
    for a, dim in zip(arrays, dims):
        pieces = lines[:, at : at + a.size].reshape(-1, *a.shape)
        finished.append(joined_along(pieces, dim))
        at += a.size
    return tuple(finished)


def side_by_side(arrays, axis, dim, along):
    ends, at = ([], 0)
    for a in arrays[:-1]:
        at += a.shape[along]
        ends.append(at)
    both = jnp.concatenate(arrays, axis=along)
    return tuple(jnp.split(lax.all_gather(both, axis, axis=dim, tiled=True), ends, axis=along))


def cut_along(shard, dim, peers):
    before, after = (shard.shape[:dim], shard.shape[dim + 1 :])
    return jnp.moveaxis(shard.reshape(*before, peers, -1, *after), dim, 0)


def sum_at_owner(shard, axis, dim):
    peers = lax.axis_size(axis)
    pieces = lax.all_to_all(cut_along(shard, dim, peers), axis, 0, 0, tiled=True)
    return jnp.sum(pieces.astype(jnp.float32), axis=0)


def gather_weights(embed_weight, qkv_weight):
    _, feat, width = embed_weight.shape
    qkv_flat = qkv_weight.reshape(-1, width)
    extra = -qkv_flat.shape[0] % 4
    rows = jnp.concatenate(
        [embed_weight[0], qkv_flat, jnp.zeros((extra, width), qkv_flat.dtype)], axis=0
    )
    peers = lax.axis_size("blk")
    near = [list(range(start, start + 4)) for start in range(0, peers, 4)]
    far = [list(range(start, peers, 4)) for start in range(4)]
    gathered = lax.all_gather(rows, "blk", axis=0, tiled=True, axis_index_groups=near)
    gathered = lax.all_gather(gathered, "blk", axis=0, tiled=True, axis_index_groups=far)
    gathered = gathered.reshape(peers, rows.shape[0], width)
    embed_rows = gathered[:, :feat, :]
    qkv_rows = gathered[:, feat : feat + qkv_flat.shape[0], :].reshape(peers, *qkv_weight.shape)
    qkv_rows = jnp.moveaxis(qkv_rows, 0, 1).reshape(
        qkv_weight.shape[0], peers * qkv_weight.shape[1], qkv_weight.shape[2]
    )
    return embed_rows, qkv_rows


def with_rim(volume):
    return padded_2(volume, (("zslab", 1), ("blk", 0)), DMAX)


def picked(cells, dim, step, rate, size):
    near = lax.slice_in_dim(cells, DMAX + step, DMAX + step + size, axis=dim)
    if step == 0:
        return near
    far = lax.slice_in_dim(cells, DMAX + 2 * step, DMAX + 2 * step + size, axis=dim)
    return jnp.where(rate == 1, near, far)


def shifted_y(values, step, rate):
    def by(amount):
        cells = values.shape[2]
        zeros = jnp.zeros_like(values[:, :, : abs(amount)])
        if amount > 0:
            return jnp.concatenate([values[:, :, amount:], zeros], axis=2)
        return jnp.concatenate([zeros, values[:, :, : cells + amount]], axis=2)

    if step == 0:
        return values
    return jnp.where(rate == 1, by(step), by(2 * step))


def apply_offsets(padded, weight, dilate, direction, dims_out):
    x_cells, z_cells, y_cells, channels = dims_out
    windows = []
    for offset_x in (-1, 0, 1):
        along_x = picked(padded, 0, direction * offset_x, dilate[0], x_cells)
        for offset_z in (-1, 0, 1):
            windows.append(picked(along_x, 1, direction * offset_z, dilate[2], z_cells))
    stacked = jnp.concatenate(windows, axis=3).reshape(x_cells * z_cells * y_cells, 9 * channels)
    taps = weight.reshape(3, 3, 3, channels, -1)
    summed = None
    for offset_y in (-1, 0, 1):
        rows = taps[:, offset_y + 1].reshape(9 * channels, -1)
        part = jnp.dot(stacked, rows, preferred_element_type=jnp.float32)
        part = shifted_y(part.reshape(x_cells, z_cells, y_cells, -1), direction * offset_y, dilate[1])
        summed = part if summed is None else summed + part
    return summed


def slab_total(term):
    return taken_together(term.astype(jnp.bfloat16), "zslab").astype(jnp.float32)


def local(field, fracture_mask, dilation, conv_weight, embed_weight, qkv_weight, out_grad):
    field = field.transpose(0, 2, 1, 3)
    fracture_mask = fracture_mask.transpose(0, 2, 1)
    x_cells, z_cells, y_cells, channels = field.shape
    gate_mask = fracture_mask.astype(jnp.float32)[..., None]
    hidden = field
    conv_outs = []
    for layer_num in range(LAYERS):
        conv_out = apply_offsets(
            with_rim(hidden), conv_weight[layer_num], dilation[layer_num], 1, field.shape
        )
        conv_outs.append(conv_out)
        hidden = (
            hidden.astype(jnp.float32) + gate_mask * (conv_out * jax.nn.sigmoid(conv_out))
        ).astype(jnp.bfloat16)
    slab_view = lax.all_to_all(hidden, "zslab", split_axis=0, concat_axis=1, tiled=True)
    x_local, z_total = (slab_view.shape[0], slab_view.shape[1])
    y_blocks, z_blocks = (y_cells // PY, z_total // PZ)
    patches = slab_view.reshape(x_local, z_blocks, PZ, y_blocks, PY, channels).transpose(
        3, 1, 0, 4, 2, 5
    )
    patches = patches.reshape(y_blocks * z_blocks, x_local, PY * PZ * channels)
    embed_rows, qkv_rows = gather_weights(embed_weight, qkv_weight)
    patches = patches.reshape(patches.shape[0], embed_rows.shape[0], embed_rows.shape[1])
    partial_value = jnp.einsum(
        "tbf,bfd->td", patches, embed_rows, preferred_element_type=jnp.float32
    )
    tokens = slab_total(partial_value).astype(jnp.bfloat16)
    projected = jnp.einsum(
        "td,sde->ste", tokens, qkv_rows, preferred_element_type=jnp.float32
    ).astype(jnp.bfloat16)
    key_rows, value_rows = jnp.split(
        joined_along(copy_for_each(jnp.concatenate([projected[1], projected[2]], axis=1), "blk"), 0),
        2,
        axis=1,
    )
    tok_rows = tokens.shape[0]
    head_cols = projected.shape[2]
    heads_here = head_cols // HD
    inv_root = HD ** (-0.5)
    queries = projected[0].reshape(tok_rows, heads_here, HD)
    key_all = key_rows.reshape(-1, heads_here, HD)
    value_all = value_rows.reshape(-1, heads_here, HD)
    grad_out = out_grad.reshape(tok_rows, heads_here, HD)
    scores = (
        jnp.einsum("qhd,khd->hqk", queries, key_all, preferred_element_type=jnp.float32) * inv_root
    )
    top_score = jnp.max(scores, axis=2, keepdims=True)
    expo = jnp.exp(scores - top_score)
    total = jnp.sum(expo, axis=2, keepdims=True)
    probs = expo / total
    probs_b = probs.astype(jnp.bfloat16)
    attended = jnp.einsum("hqk,khd->qhd", probs_b, value_all, preferred_element_type=jnp.float32)
    row_delta = jnp.sum(grad_out.astype(jnp.float32) * attended, axis=2).T[:, :, None]
    score_grad = jnp.einsum("qhd,khd->hqk", grad_out, value_all, preferred_element_type=jnp.float32)
    dscore = (probs * (score_grad - row_delta) * inv_root).astype(jnp.bfloat16)
    grad_query = jnp.einsum("hqk,khd->qhd", dscore, key_all, preferred_element_type=jnp.float32)
    grad_query = grad_query.astype(jnp.bfloat16).reshape(tok_rows, head_cols)
    key_term = jnp.einsum("hqk,qhd->khd", dscore, queries, preferred_element_type=jnp.float32)
    value_term = jnp.einsum("hqk,qhd->khd", probs_b, grad_out, preferred_element_type=jnp.float32)
    key_value_grad = sum_at_owner(
        jnp.concatenate(
            [
                key_term.reshape(tok_rows * lax.axis_size("blk"), head_cols),
                value_term.reshape(tok_rows * lax.axis_size("blk"), head_cols),
            ],
            axis=1,
        ).astype(jnp.bfloat16),
        "blk",
        0,
    ).astype(jnp.bfloat16)
    grad_key = key_value_grad[:, :head_cols]
    grad_value = key_value_grad[:, head_cols:]
    stacked_grads = jnp.stack([grad_query, grad_key, grad_value])
    partial_grad = jnp.einsum(
        "ste,sde->td", stacked_grads, qkv_rows, preferred_element_type=jnp.float32
    )
    grad_tokens = slab_total(partial_grad).astype(jnp.bfloat16)
    patch_grad = jnp.einsum(
        "td,bfd->tbf", grad_tokens, embed_rows, preferred_element_type=jnp.float32
    ).astype(jnp.bfloat16)
    grid_grad = patch_grad.reshape(y_blocks, z_blocks, x_local, PY, PZ, channels).transpose(
        2, 1, 4, 0, 3, 5
    )
    grid_grad = grid_grad.reshape(x_local, z_total, y_cells, channels)
    grid_grad = lax.all_to_all(grid_grad, "zslab", split_axis=1, concat_axis=0, tiled=True)
    for layer_num in reversed(range(LAYERS)):
        conv_out = conv_outs[layer_num]
        sigma = jax.nn.sigmoid(conv_out)
        slope_grad = (
            gate_mask * sigma * (1.0 + conv_out * (1.0 - sigma)) * grid_grad.astype(jnp.float32)
        ).astype(jnp.bfloat16)
        flipped = (
            conv_weight[layer_num]
            .reshape(27, channels, channels)
            .transpose(0, 2, 1)
            .reshape(27 * channels, channels)
        )
        backward = apply_offsets(
            with_rim(slope_grad), flipped, dilation[layer_num], -1, field.shape
        )
        grid_grad = (grid_grad.astype(jnp.float32) + backward).astype(jnp.bfloat16)
    return grid_grad.transpose(0, 2, 1, 3)


def solution(mesh):
    return jax.shard_map(
        local,
        mesh=mesh,
        in_specs=(
            P("blk", None, "zslab", None),
            P("blk", None, "zslab"),
            P(),
            P(),
            P("zslab", "blk", None),
            P(None, "blk", "zslab"),
            P("blk", "zslab"),
        ),
        out_specs=P("blk", None, "zslab", None),
        check_vma=False,
    )
```
